32 devices in a mesh: cuts: 2 (over x), mode: 16 (over z, y, core).
Axes of the slice: x: 2, y: 2, z: 4, core: 2. Of those that a mesh axis runs over, the one named last changes fastest.
Arguments:
- stem_blocks: bfloat16 [2, 4096, 2, 256], P('cuts', 'mode'), may hold values from -6 to 6
- w1_table: bfloat16 [8, 2, 256, 256], replicated, may hold values from -0.25 to 0.25
- w2_table: bfloat16 [8, 2, 256, 256], replicated, may hold values from -0.125 to 0.125
- slice_ids: int32 [2, 2, 2], P('cuts'), may hold values from 0 to 7, as said below
- mode_perm: int32 [256], replicated, may hold values from 0 to 255, each once
Outputs:
- amplitudes: float32 [256, 16, 2, 256], P('mode', 'cuts')
The draws below stay inside these ranges and needn't reach their ends.
Inputs may be any that keep to these rules, and one draw needn't show every extreme that they name: For each stem block b, the 2 values slice_ids[:,b,0] are distinct, and so are the 2 values slice_ids[:,b,1]. `mode_perm`: each column appears once.
All inputs are finite; a program needn't handle non-finite values.
Results may differ from the reference program's by a relative error of at most 0.0029.
Values may be sent and summed in bfloat16 or wider, within the bound.
No kernel may reach another device: no remote copies, remote signals or barrier semaphores. Data moves between devices by JAX's collectives and lax.ppermute only.
A program may use at most 64 MiB of HBM per device.

```python
import jax
import jax.numpy as jnp
from jax import lax

K = 256
J = 256
K2 = 256
L = 256
NSLICE = 8
NB = 2
ROWS = 4096
N_CUTS = 2
N_MODE = 16


def draw_slice_ids(key, part):
    keys = jax.random.split(key, 2 * NB)
    orders = jax.vmap(lambda one_key: jax.random.permutation(one_key, NSLICE))(keys)
    picked = orders[:, :N_CUTS].reshape(NB, 2, N_CUTS)
    return jnp.transpose(picked, (2, 0, 1)).astype(jnp.int32)


def block_scale(key, shape, pieces, smallest, largest):
    factor_of, own = 1.0, jax.random.fold_in(key, 6)
    for axis_at, parts in pieces:
        heights = jnp.exp(jax.random.uniform(jax.random.fold_in(own, axis_at), (parts,), jnp.float32, smallest / len(pieces), largest / len(pieces)))
        factor_of = factor_of * jnp.repeat(heights, shape[axis_at] // parts).reshape([-1 if axis == axis_at else 1 for axis in range(len(shape))])
    return factor_of


def normal_values(own_key, dims, deviation, bound, shards=(), kind=jnp.bfloat16):
    array = jax.random.normal(own_key, dims, jnp.float32) * deviation
    if len(shards) > 0:
        array = block_scale(own_key, dims, shards, -0.22, 0.18) * array
    return jnp.clip(array, min=-bound, max=bound).astype(kind)


def setup_inputs(seed: int = 0) -> dict:
    streams_of = jax.random.split(jax.random.key(seed), 6)
    return {
        "stem_blocks": normal_values(streams_of[0], (N_CUTS, ROWS, 2, K), 1.0, 6.0, ((0, 2), (1, 16))),
        "w1_table": normal_values(streams_of[1], (NSLICE, 2, K, J), (2 * K) ** -0.5, 0.25),
        "w2_table": normal_values(streams_of[2], (NSLICE, 2, K2, L), (2 * K2 * N_CUTS * N_CUTS) ** -0.5, 0.125),
        "slice_ids": draw_slice_ids(jax.random.fold_in(streams_of[5], 71), 0),
        "mode_perm": jax.random.permutation(streams_of[4], J).astype(jnp.int32),
    }


def widen_first(entry):
    real_part, imag_part = entry[0], entry[1]
    upper = jnp.concatenate([real_part, imag_part], axis=1)
    lower = jnp.concatenate([-imag_part, real_part], axis=1)
    return jnp.concatenate([upper, lower], axis=0)


def widen_second(entry):
    real_part, imag_part = entry[0], entry[1]
    first_row = jnp.concatenate([real_part, imag_part], axis=1)
    second_row = jnp.concatenate([-imag_part, real_part], axis=1)
    return jnp.stack([first_row, second_row], axis=0)


def reference(stem_blocks, w1_table, w2_table, slice_ids, mode_perm):
    row_count = stem_blocks.shape[1]
    stem_width = stem_blocks.shape[3]
    out_width = w2_table.shape[3]
    mode_count = N_MODE
    piece_rows = row_count // mode_count
    contract_cols = K2 // mode_count
    free_cols = J // contract_cols
    first_all = jax.vmap(widen_first)(jnp.take(w1_table, mode_perm, axis=3))
    second_all = jax.vmap(widen_second)(w2_table)
    owners_flat = jnp.tile(jnp.arange(NB, dtype=jnp.int32), N_CUTS).astype(jnp.int32)
    slices_flat = slice_ids.reshape(-1, 2).astype(jnp.int32)

    def one_block(running, item):
        owner_now, slice_pair = item
        stem_part = lax.dynamic_index_in_dim(stem_blocks, owner_now, 0, keepdims=False)
        weight_one = lax.dynamic_index_in_dim(first_all, slice_pair[0], 0, keepdims=False)
        product = jnp.dot(stem_part.reshape(row_count, 2 * stem_width), weight_one, preferred_element_type=jnp.float32).astype(jnp.bfloat16)
        split = product.astype(jnp.float32).reshape(mode_count, piece_rows, 2, contract_cols, free_cols)
        weight_two = lax.dynamic_index_in_dim(second_all, slice_pair[1], 0, keepdims=False).astype(jnp.float32)
        weight_two = weight_two.reshape(2, mode_count, contract_cols, 2 * out_width)
        return running + jnp.einsum("hqpcs,phco->qso", split, weight_two), None

    begin = jnp.zeros((piece_rows, free_cols, 2 * out_width), jnp.float32)
    amplitude, _ = lax.scan(one_block, begin, (owners_flat, slices_flat))
    return amplitude.reshape(piece_rows, free_cols, 2, out_width)
```

```python
import jax
import jax.numpy as jnp
from jax import lax
from jax.sharding import PartitionSpec as P


def gather_over_cuts(own, n_cuts):
    pieces = [own]
    current = own
    ring = [(j, (j + 1) % n_cuts) for j in range(n_cuts)]
    for _ in range(1, n_cuts):
        current = lax.ppermute(current, "cuts", ring)
        pieces.append(current)
    stacked = jnp.stack(pieces)
    me = lax.axis_index("cuts")
    order = (me - jnp.arange(n_cuts, dtype=jnp.int32)) % n_cuts
    return jnp.take(stacked, order, axis=0)


def blocks_part(stem_rows, first_all, w2_table, first_ids, second_ids, sizes):
    n_mode, t_local, n_cuts, a_count, q_local = sizes
    chunk = stem_rows.shape[0]
    wide_in = stem_rows.shape[2]
    col_width = first_all.shape[2]
    slice_count, _, inner, out_width = w2_table.shape
    first_w = jnp.take(first_all, first_ids, axis=0)
    first_w = jnp.transpose(first_w, (0, 2, 1, 3)).reshape(
        chunk, wide_in, n_cuts * col_width
    )
    product = jnp.einsum(
        "bri,bio->bro", stem_rows, first_w, preferred_element_type=jnp.float32
    ).astype(jnp.bfloat16)
    split = product.reshape(chunk, n_mode, t_local, n_cuts, 2, a_count, q_local)
    real_p, imag_p = split[:, :, :, :, 0], split[:, :, :, :, 1]
    lhs = jnp.stack(
        [
            jnp.stack([real_p, -imag_p]),
            jnp.stack([imag_p, real_p]),
        ]
    )
    lhs = jnp.transpose(lhs, (4, 7, 0, 2, 5, 1, 3, 6)).reshape(
        t_local * q_local * 2, chunk * n_cuts * 2 * inner
    )
    second_w = jnp.take(
        w2_table.reshape(slice_count, 2 * inner, out_width), second_ids, axis=0
    ).reshape(chunk * n_cuts * 2 * inner, out_width)
    return jnp.dot(lhs, second_w, preferred_element_type=jnp.float32)


def on_device(stem_blocks, w1_table, w2_table, slice_ids, mode_perm):
    n_mode = lax.axis_size("mode")
    n_cuts = lax.axis_size("cuts")
    rows = stem_blocks.shape[1]
    width = stem_blocks.shape[3]
    mid = w1_table.shape[3]
    inner = w2_table.shape[2]
    out_width = w2_table.shape[3]
    block_count = slice_ids.shape[1]
    t_local = rows // n_mode
    a_count = inner // n_mode
    q_count = mid // a_count
    q_local = q_count // n_cuts
    me = lax.axis_index("cuts")
    sizes = (n_mode, t_local, n_cuts, a_count, q_local)

    pieces = stem_blocks[0].reshape(1, n_mode, t_local, 2 * width)
    payload = jnp.broadcast_to(pieces, (n_cuts, n_mode, t_local, 2 * width))
    payload = payload.reshape(n_cuts * n_mode, t_local, 2 * width)
    stem_rows = lax.all_to_all(payload, ("cuts", "mode"), 0, 0, tiled=True)
    stem_rows = stem_rows.reshape(block_count, n_mode * t_local, 2 * width)

    all_ids = gather_over_cuts(slice_ids[0], n_cuts)
    first_ids = all_ids[:, :, 0].T
    second_ids = all_ids[:, :, 1].T

    perm_grid = mode_perm.reshape(a_count, q_count)
    wanted = lax.dynamic_slice_in_dim(perm_grid, me * q_local, q_local, axis=1).reshape(-1)
    picker = (jnp.arange(mid, dtype=jnp.int32)[:, None] == wanted[None, :]).astype(w1_table.dtype)
    first_cols = jnp.einsum(
        "spkj,jn->spkn", w1_table, picker, preferred_element_type=jnp.float32
    ).astype(w1_table.dtype)
    real_part, imag_part = first_cols[:, 0], first_cols[:, 1]
    upper = jnp.concatenate([real_part, imag_part], axis=2)
    lower = jnp.concatenate([-imag_part, real_part], axis=2)
    first_all = jnp.concatenate([upper, lower], axis=1)

    if block_count * n_cuts <= 8:
        amplitude = blocks_part(
            stem_rows, first_all, w2_table, first_ids, second_ids.reshape(-1), sizes
        )
    else:
        def one_block(index, running):
            stem_one = lax.dynamic_slice_in_dim(stem_rows, index, 1, axis=0)
            first_one = lax.dynamic_slice_in_dim(first_ids, index, 1, axis=0)
            second_one = lax.dynamic_slice_in_dim(second_ids, index, 1, axis=0)
            return running + blocks_part(
                stem_one, first_all, w2_table, first_one, second_one.reshape(-1), sizes
            )

        begin = jnp.zeros((t_local * q_local * 2, out_width), jnp.float32)
        amplitude = lax.fori_loop(0, block_count, one_block, begin)
    return amplitude.reshape(t_local, q_local, 2, out_width)


def solution(mesh):
    placed = (P("cuts", "mode", None, None), P(), P(), P("cuts", None, None), P())
    return jax.shard_map(
        on_device,
        mesh=mesh,
        in_specs=placed,
        out_specs=P("mode", "cuts", None, None),
        check_vma=False,
    )
```

```python
import jax
import jax.numpy as jnp
from jax import lax
from jax.sharding import PartitionSpec as P


def gather_over_cuts(own, n_cuts):
    pieces = [own]
    current = own
    ring = [(j, (j + 1) % n_cuts) for j in range(n_cuts)]
    for _ in range(1, n_cuts):
        current = lax.ppermute(current, "cuts", ring)
        pieces.append(current)
    stacked = jnp.stack(pieces)
    me = lax.axis_index("cuts")
    order = (me - jnp.arange(n_cuts, dtype=jnp.int32)) % n_cuts
    return jnp.take(stacked, order, axis=0)


def blocks_part(stem_rows, first_all, w2_table, first_ids, second_ids, sizes):
    n_mode, t_local, n_cuts, a_count, q_local = sizes
    chunk = stem_rows.shape[0]
    wide_in = stem_rows.shape[2]
    col_width = first_all.shape[2]
    slice_count, _, inner, out_width = w2_table.shape
    first_w = jnp.take(first_all, first_ids, axis=0)
    first_w = jnp.transpose(first_w, (0, 2, 1, 3)).reshape(
        chunk, wide_in, n_cuts * col_width
    )
    product = jnp.einsum(
        "bri,bio->bro", stem_rows, first_w, preferred_element_type=jnp.float32
    ).astype(jnp.bfloat16)
    split = product.reshape(chunk, n_mode, t_local, n_cuts, 2, a_count, q_local)
    real_p, imag_p = split[:, :, :, :, 0], split[:, :, :, :, 1]
    lhs = jnp.stack(
        [
            jnp.stack([real_p, -imag_p]),
            jnp.stack([imag_p, real_p]),
        ]
    )
    lhs = jnp.transpose(lhs, (4, 7, 0, 2, 5, 1, 3, 6)).reshape(
        t_local * q_local * 2, chunk * n_cuts * 2 * inner
    )
    second_w = jnp.take(
        w2_table.reshape(slice_count, 2 * inner, out_width), second_ids, axis=0
    ).reshape(chunk * n_cuts * 2 * inner, out_width)
    return jnp.dot(lhs, second_w, preferred_element_type=jnp.float32)


def stacked_part(stem_rows, first_cols, w2_table, first_ids, second_ids, sizes):
    n_mode, t_local, n_cuts, a_count, q_local = sizes
    block_count = stem_rows.shape[0]
    slice_count, _, width, _ = first_cols.shape
    _, _, inner, out_width = w2_table.shape
    group = n_cuts * 2 * a_count
    split_cols = first_cols.reshape(slice_count, 2, width, a_count, q_local)
    real_part, imag_part = split_cols[:, 0], split_cols[:, 1]
    first_w = jnp.stack(
        [jnp.stack([real_part, imag_part]), jnp.stack([-imag_part, real_part])]
    )
    first_w = jnp.take(first_w, first_ids.reshape(-1), axis=2)
    first_w = first_w.reshape(2, 2, block_count, n_cuts, width, a_count, q_local)
    first_w = jnp.transpose(first_w, (2, 0, 4, 6, 3, 1, 5)).reshape(
        block_count, 2 * width, q_local * group
    )
    product = jnp.einsum(
        "bri,bio->bro", stem_rows, first_w, preferred_element_type=jnp.float32
    ).astype(jnp.bfloat16)
    lhs = product.reshape(block_count * n_mode, t_local, q_local, group)
    lhs = jnp.transpose(lhs, (2, 1, 0, 3)).reshape(
        q_local * t_local, block_count * n_mode * group
    )
    second = jnp.take(w2_table, second_ids.reshape(-1), axis=0)
    second = second.reshape(block_count, n_cuts, 2, n_mode, a_count, out_width)
    real_two, imag_two = second[:, :, 0], second[:, :, 1]
    second_w = jnp.stack(
        [jnp.stack([real_two, imag_two]), jnp.stack([-imag_two, real_two])]
    )
    second_w = jnp.transpose(second_w, (2, 4, 3, 0, 5, 1, 6)).reshape(
        block_count * n_mode * group, 2 * out_width
    )
    amplitude = jnp.dot(lhs, second_w, preferred_element_type=jnp.float32)
    amplitude = amplitude.reshape(q_local, t_local, 2, out_width)
    return jnp.transpose(amplitude, (1, 0, 2, 3))

def on_device(stem_blocks, w1_table, w2_table, slice_ids, mode_perm):
    n_mode = lax.axis_size("mode")
    n_cuts = lax.axis_size("cuts")
    rows = stem_blocks.shape[1]
    width = stem_blocks.shape[3]
    mid = w1_table.shape[3]
    inner = w2_table.shape[2]
    out_width = w2_table.shape[3]
    block_count = slice_ids.shape[1]
    t_local = rows // n_mode
    a_count = inner // n_mode
    q_count = mid // a_count
    q_local = q_count // n_cuts
    me = lax.axis_index("cuts")
    sizes = (n_mode, t_local, n_cuts, a_count, q_local)

    pieces = stem_blocks[0].reshape(1, n_mode, t_local, 2 * width)
    payload = jnp.broadcast_to(pieces, (n_cuts, n_mode, t_local, 2 * width))
    payload = payload.reshape(n_cuts * n_mode, t_local, 2 * width)
    stem_rows = lax.all_to_all(payload, ("cuts", "mode"), 0, 0, tiled=True)
    stem_rows = stem_rows.reshape(block_count, n_mode * t_local, 2 * width)

    all_ids = gather_over_cuts(slice_ids[0], n_cuts)
    first_ids = all_ids[:, :, 0].T
    second_ids = all_ids[:, :, 1].T

    perm_grid = mode_perm.reshape(a_count, q_count)
    wanted = lax.dynamic_slice_in_dim(perm_grid, me * q_local, q_local, axis=1).reshape(-1)
    picker = (jnp.arange(mid, dtype=jnp.int32)[:, None] == wanted[None, :]).astype(w1_table.dtype)
    first_cols = jnp.einsum(
        "spkj,jn->spkn", w1_table, picker, preferred_element_type=jnp.float32
    ).astype(w1_table.dtype)
    real_part, imag_part = first_cols[:, 0], first_cols[:, 1]
    upper = jnp.concatenate([real_part, imag_part], axis=2)
    lower = jnp.concatenate([-imag_part, real_part], axis=2)
    first_all = jnp.concatenate([upper, lower], axis=1)

    if block_count * n_cuts <= 8:
        return stacked_part(stem_rows, first_cols, w2_table, first_ids, second_ids, sizes)
    else:
        def one_block(index, running):
            stem_one = lax.dynamic_slice_in_dim(stem_rows, index, 1, axis=0)
            first_one = lax.dynamic_slice_in_dim(first_ids, index, 1, axis=0)
            second_one = lax.dynamic_slice_in_dim(second_ids, index, 1, axis=0)
            return running + blocks_part(
                stem_one, first_all, w2_table, first_one, second_one.reshape(-1), sizes
            )

        begin = jnp.zeros((t_local * q_local * 2, out_width), jnp.float32)
        amplitude = lax.fori_loop(0, block_count, one_block, begin)
    return amplitude.reshape(t_local, q_local, 2, out_width)


def solution(mesh):
    placed = (P("cuts", "mode", None, None), P(), P(), P("cuts", None, None), P())
    return jax.shard_map(
        on_device,
        mesh=mesh,
        in_specs=placed,
        out_specs=P("mode", "cuts", None, None),
        check_vma=False,
    )
```

```python
import jax
import jax.numpy as jnp
from jax import lax
from jax.sharding import PartitionSpec as P


def gather_over_cuts(own, n_cuts):
    pieces = [own]
    current = own
    ring = [(j, (j + 1) % n_cuts) for j in range(n_cuts)]
    for _ in range(1, n_cuts):
        current = lax.ppermute(current, "cuts", ring)
        pieces.append(current)
    stacked = jnp.stack(pieces)
    me = lax.axis_index("cuts")
    order = (me - jnp.arange(n_cuts, dtype=jnp.int32)) % n_cuts
    return jnp.take(stacked, order, axis=0)


def blocks_part(stem_rows, first_all, w2_table, first_ids, second_ids, sizes):
    n_mode, t_local, n_cuts, a_count, q_local = sizes
    chunk = stem_rows.shape[0]
    wide_in = stem_rows.shape[2]
    col_width = first_all.shape[2]
    slice_count, _, inner, out_width = w2_table.shape
    first_w = jnp.take(first_all, first_ids, axis=0)
    first_w = jnp.transpose(first_w, (0, 2, 1, 3)).reshape(
        chunk, wide_in, n_cuts * col_width
    )
    product = jnp.einsum(
        "bri,bio->bro", stem_rows, first_w, preferred_element_type=jnp.float32
    ).astype(jnp.bfloat16)
    split = product.reshape(chunk, n_mode, t_local, n_cuts, 2, a_count, q_local)
    real_p, imag_p = split[:, :, :, :, 0], split[:, :, :, :, 1]
    lhs = jnp.stack(
        [
            jnp.stack([real_p, -imag_p]),
            jnp.stack([imag_p, real_p]),
        ]
    )
    lhs = jnp.transpose(lhs, (4, 7, 0, 2, 5, 1, 3, 6)).reshape(
        t_local * q_local * 2, chunk * n_cuts * 2 * inner
    )
    second_w = jnp.take(
        w2_table.reshape(slice_count, 2 * inner, out_width), second_ids, axis=0
    ).reshape(chunk * n_cuts * 2 * inner, out_width)
    return jnp.dot(lhs, second_w, preferred_element_type=jnp.float32)


def stacked_part(stem_rows, first_t, w2_table, first_ids, second_ids, sizes):
    n_mode, t_local, n_cuts, a_count, q_local = sizes
    block_count = stem_rows.shape[0]
    width = first_t.shape[3]
    _, _, inner, out_width = w2_table.shape
    group = n_cuts * 2 * a_count
    picked = jnp.take(first_t, first_ids.reshape(-1), axis=0)
    picked = picked.reshape(block_count, n_cuts, 2, q_local, a_count, width)
    real_part, imag_part = picked[:, :, 0], picked[:, :, 1]
    first_w = jnp.stack(
        [jnp.stack([real_part, imag_part]), jnp.stack([-imag_part, real_part])]
    )
    first_w = jnp.transpose(first_w, (2, 4, 3, 1, 5, 0, 6)).reshape(
        block_count, q_local * group, 2 * width
    )
    product = jnp.einsum(
        "brk,bnk->brn", stem_rows, first_w, preferred_element_type=jnp.float32
    ).astype(jnp.bfloat16)
    lhs = product.reshape(block_count, n_mode, t_local, q_local, group)
    lhs = jnp.transpose(lhs, (3, 2, 0, 1, 4)).reshape(
        q_local * t_local, block_count * n_mode * group
    )
    second = jnp.take(w2_table, second_ids.reshape(-1), axis=0)
    second = jnp.swapaxes(second, 2, 3)
    second = second.reshape(block_count, n_cuts, 2, out_width, n_mode, a_count)
    real_two, imag_two = second[:, :, 0], second[:, :, 1]
    second_w = jnp.stack(
        [jnp.stack([real_two, -imag_two]), jnp.stack([imag_two, real_two])]
    )
    second_w = jnp.transpose(second_w, (0, 4, 2, 5, 3, 1, 6)).reshape(
        2 * out_width, block_count * n_mode * group
    )
    amplitude = jnp.einsum(
        "mk,nk->mn", lhs, second_w, preferred_element_type=jnp.float32
    )
    amplitude = amplitude.reshape(q_local, t_local, 2, out_width)
    return jnp.transpose(amplitude, (1, 0, 2, 3))

def on_device(stem_blocks, w1_table, w2_table, slice_ids, mode_perm):
    n_mode = lax.axis_size("mode")
    n_cuts = lax.axis_size("cuts")
    rows = stem_blocks.shape[1]
    width = stem_blocks.shape[3]
    mid = w1_table.shape[3]
    inner = w2_table.shape[2]
    out_width = w2_table.shape[3]
    block_count = slice_ids.shape[1]
    t_local = rows // n_mode
    a_count = inner // n_mode
    q_count = mid // a_count
    q_local = q_count // n_cuts
    me = lax.axis_index("cuts")
    sizes = (n_mode, t_local, n_cuts, a_count, q_local)

    pieces = stem_blocks[0].reshape(1, n_mode, t_local, 2 * width)
    payload = jnp.broadcast_to(pieces, (n_cuts, n_mode, t_local, 2 * width))
    payload = payload.reshape(n_cuts * n_mode, t_local, 2 * width)
    stem_rows = lax.all_to_all(payload, ("cuts", "mode"), 0, 0, tiled=True)
    stem_rows = stem_rows.reshape(block_count, n_mode * t_local, 2 * width)

    all_ids = gather_over_cuts(slice_ids[0], n_cuts)
    first_ids = all_ids[:, :, 0].T
    second_ids = all_ids[:, :, 1].T

    perm_grid = mode_perm.reshape(a_count, q_count)
    wanted = lax.dynamic_slice_in_dim(perm_grid, me * q_local, q_local, axis=1).reshape(-1)
    picker = (jnp.arange(mid, dtype=jnp.int32)[:, None] == wanted[None, :]).astype(w1_table.dtype)
    first_cols = jnp.einsum(
        "spkj,jn->spkn", w1_table, picker, preferred_element_type=jnp.float32
    ).astype(w1_table.dtype)
    real_part, imag_part = first_cols[:, 0], first_cols[:, 1]
    upper = jnp.concatenate([real_part, imag_part], axis=2)
    lower = jnp.concatenate([-imag_part, real_part], axis=2)
    first_all = jnp.concatenate([upper, lower], axis=1)

    if block_count * n_cuts <= 8:
        wanted_t = lax.dynamic_slice_in_dim(perm_grid, me * q_local, q_local, axis=1).T.reshape(-1)
        picker_t = (wanted_t[:, None] == jnp.arange(mid, dtype=jnp.int32)[None, :]).astype(w1_table.dtype)
        first_t = jnp.einsum(
            "nj,spkj->spnk", picker_t, w1_table, preferred_element_type=jnp.float32
        ).astype(w1_table.dtype)
        return stacked_part(stem_rows, first_t, w2_table, first_ids, second_ids, sizes)
    else:
        def one_block(index, running):
            stem_one = lax.dynamic_slice_in_dim(stem_rows, index, 1, axis=0)
            first_one = lax.dynamic_slice_in_dim(first_ids, index, 1, axis=0)
            second_one = lax.dynamic_slice_in_dim(second_ids, index, 1, axis=0)
            return running + blocks_part(
                stem_one, first_all, w2_table, first_one, second_one.reshape(-1), sizes
            )

        begin = jnp.zeros((t_local * q_local * 2, out_width), jnp.float32)
        amplitude = lax.fori_loop(0, block_count, one_block, begin)
    return amplitude.reshape(t_local, q_local, 2, out_width)


def solution(mesh):
    placed = (P("cuts", "mode", None, None), P(), P(), P("cuts", None, None), P())
    return jax.shard_map(
        on_device,
        mesh=mesh,
        in_specs=placed,
        out_specs=P("mode", "cuts", None, None),
        check_vma=False,
    )
```

```python
import jax
import jax.numpy as jnp
from jax import lax
from jax.experimental import pallas as pl
from jax.experimental.pallas import tpu as pltpu
from jax.sharding import PartitionSpec as P


def gather_over_cuts(own, n_cuts):
    pieces = [own]
    current = own
    ring = [(j, (j + 1) % n_cuts) for j in range(n_cuts)]
    for _ in range(1, n_cuts):
        current = lax.ppermute(current, "cuts", ring)
        pieces.append(current)
    stacked = jnp.stack(pieces)
    me = lax.axis_index("cuts")
    order = (me - jnp.arange(n_cuts, dtype=jnp.int32)) % n_cuts
    return jnp.take(stacked, order, axis=0)


def blocks_part(stem_rows, first_all, w2_table, first_ids, second_ids, sizes):
    n_mode, t_local, n_cuts, a_count, q_local = sizes
    chunk = stem_rows.shape[0]
    wide_in = stem_rows.shape[2]
    col_width = first_all.shape[2]
    slice_count, _, inner, out_width = w2_table.shape
    first_w = jnp.take(first_all, first_ids, axis=0)
    first_w = jnp.transpose(first_w, (0, 2, 1, 3)).reshape(
        chunk, wide_in, n_cuts * col_width
    )
    product = jnp.einsum(
        "bri,bio->bro", stem_rows, first_w, preferred_element_type=jnp.float32
    ).astype(jnp.bfloat16)
    split = product.reshape(chunk, n_mode, t_local, n_cuts, 2, a_count, q_local)
    real_p, imag_p = split[:, :, :, :, 0], split[:, :, :, :, 1]
    lhs = jnp.stack(
        [
            jnp.stack([real_p, -imag_p]),
            jnp.stack([imag_p, real_p]),
        ]
    )
    lhs = jnp.transpose(lhs, (4, 7, 0, 2, 5, 1, 3, 6)).reshape(
        t_local * q_local * 2, chunk * n_cuts * 2 * inner
    )
    second_w = jnp.take(
        w2_table.reshape(slice_count, 2 * inner, out_width), second_ids, axis=0
    ).reshape(chunk * n_cuts * 2 * inner, out_width)
    return jnp.dot(lhs, second_w, preferred_element_type=jnp.float32)


def regroup_kernel(stem_ref, weight_ref, out_ref):
    block_count, rows, _ = stem_ref.shape
    q_local = weight_ref.shape[1] // 64
    t_local = 16
    n_mode = rows // t_local
    lane = lax.broadcasted_iota(jnp.int32, (t_local, 128), 1)
    low = lane < 64
    for b in range(block_count):
        product = lax.dot_general(
            stem_ref[b], weight_ref[b], (((1,), (1,)), ((), ())),
            preferred_element_type=jnp.float32,
        ).astype(jnp.bfloat16)
        for pair in range(n_mode // 2):
            upper = product[(2 * pair) * t_local:(2 * pair + 1) * t_local]
            lower = product[(2 * pair + 1) * t_local:(2 * pair + 2) * t_local]
            col = (b * n_mode // 2 + pair) * 128
            for qp in range(q_local // 2):
                first = upper[:, qp * 128:(qp + 1) * 128]
                second = lower[:, qp * 128:(qp + 1) * 128]
                even = jnp.where(low, first, pltpu.roll(second, 64, 1))
                odd = jnp.where(low, pltpu.roll(first, 64, 1), second)
                out_ref[(2 * qp) * t_local:(2 * qp + 1) * t_local, col:col + 128] = even
                out_ref[(2 * qp + 1) * t_local:(2 * qp + 2) * t_local, col:col + 128] = odd


def regroup(stem_rows, first_w, q_local, t_local):
    block_count, rows, _ = stem_rows.shape
    n_mode = rows // t_local
    out_shape = jax.ShapeDtypeStruct((q_local * t_local, block_count * n_mode * 64), jnp.bfloat16)
    return pl.pallas_call(
        regroup_kernel,
        out_shape=out_shape,
        in_specs=[pl.BlockSpec(memory_space=pltpu.VMEM)] * 2,
        out_specs=pl.BlockSpec(memory_space=pltpu.VMEM),
        cost_estimate=pl.CostEstimate(
            flops=2 * stem_rows.shape[0] * rows * first_w.shape[1] * first_w.shape[2],
            transcendentals=0,
            bytes_accessed=2 * (stem_rows.size + first_w.size) + 2 * rows * block_count * first_w.shape[1],
        ),
    )(stem_rows, first_w)


def stacked_part(stem_rows, first_t, w2_table, first_ids, second_ids, sizes):
    n_mode, t_local, n_cuts, a_count, q_local = sizes
    block_count = stem_rows.shape[0]
    width = first_t.shape[3]
    _, _, inner, out_width = w2_table.shape
    group = n_cuts * 2 * a_count
    picked = jnp.take(first_t, first_ids.reshape(-1), axis=0)
    picked = picked.reshape(block_count, n_cuts, 2, q_local, a_count, width)
    real_part, imag_part = picked[:, :, 0], picked[:, :, 1]
    first_w = jnp.stack(
        [jnp.stack([real_part, imag_part]), jnp.stack([-imag_part, real_part])]
    )
    first_w = jnp.transpose(first_w, (2, 4, 3, 1, 5, 0, 6)).reshape(
        block_count, q_local * group, 2 * width
    )
    if group == 64 and t_local == 16 and n_mode % 2 == 0 and q_local % 2 == 0:
        lhs = regroup(stem_rows, first_w, q_local, t_local)
    else:
        product = jnp.einsum(
            "brk,bnk->brn", stem_rows, first_w, preferred_element_type=jnp.float32
        ).astype(jnp.bfloat16)
        lhs = product.reshape(block_count, n_mode, t_local, q_local, group)
        lhs = jnp.transpose(lhs, (3, 2, 0, 1, 4)).reshape(
            q_local * t_local, block_count * n_mode * group
        )
    second = jnp.take(w2_table, second_ids.reshape(-1), axis=0)
    second = jnp.swapaxes(second, 2, 3)
    second = second.reshape(block_count, n_cuts, 2, out_width, n_mode, a_count)
    real_two, imag_two = second[:, :, 0], second[:, :, 1]
    second_w = jnp.stack(
        [jnp.stack([real_two, -imag_two]), jnp.stack([imag_two, real_two])]
    )
    second_w = jnp.transpose(second_w, (0, 4, 2, 5, 3, 1, 6)).reshape(
        2 * out_width, block_count * n_mode * group
    )
    amplitude = jnp.einsum(
        "mk,nk->mn", lhs, second_w, preferred_element_type=jnp.float32
    )
    amplitude = amplitude.reshape(q_local, t_local, 2, out_width)
    return jnp.transpose(amplitude, (1, 0, 2, 3))

def on_device(stem_blocks, w1_table, w2_table, slice_ids, mode_perm):
    n_mode = lax.axis_size("mode")
    n_cuts = lax.axis_size("cuts")
    rows = stem_blocks.shape[1]
    width = stem_blocks.shape[3]
    mid = w1_table.shape[3]
    inner = w2_table.shape[2]
    out_width = w2_table.shape[3]
    block_count = slice_ids.shape[1]
    t_local = rows // n_mode
    a_count = inner // n_mode
    q_count = mid // a_count
    q_local = q_count // n_cuts
    me = lax.axis_index("cuts")
    sizes = (n_mode, t_local, n_cuts, a_count, q_local)

    pieces = stem_blocks[0].reshape(1, n_mode, t_local, 2 * width)
    payload = jnp.broadcast_to(pieces, (n_cuts, n_mode, t_local, 2 * width))
    payload = payload.reshape(n_cuts * n_mode, t_local, 2 * width)
    stem_rows = lax.all_to_all(payload, ("cuts", "mode"), 0, 0, tiled=True)
    stem_rows = stem_rows.reshape(block_count, n_mode * t_local, 2 * width)

    all_ids = gather_over_cuts(slice_ids[0], n_cuts)
    first_ids = all_ids[:, :, 0].T
    second_ids = all_ids[:, :, 1].T

    perm_grid = mode_perm.reshape(a_count, q_count)
    wanted = lax.dynamic_slice_in_dim(perm_grid, me * q_local, q_local, axis=1).reshape(-1)
    picker = (jnp.arange(mid, dtype=jnp.int32)[:, None] == wanted[None, :]).astype(w1_table.dtype)
    first_cols = jnp.einsum(
        "spkj,jn->spkn", w1_table, picker, preferred_element_type=jnp.float32
    ).astype(w1_table.dtype)
    real_part, imag_part = first_cols[:, 0], first_cols[:, 1]
    upper = jnp.concatenate([real_part, imag_part], axis=2)
    lower = jnp.concatenate([-imag_part, real_part], axis=2)
    first_all = jnp.concatenate([upper, lower], axis=1)

    if block_count * n_cuts <= 8:
        wanted_t = lax.dynamic_slice_in_dim(perm_grid, me * q_local, q_local, axis=1).T.reshape(-1)
        picker_t = (wanted_t[:, None] == jnp.arange(mid, dtype=jnp.int32)[None, :]).astype(w1_table.dtype)
        first_t = jnp.einsum(
            "nj,spkj->spnk", picker_t, w1_table, preferred_element_type=jnp.float32
        ).astype(w1_table.dtype)
        return stacked_part(stem_rows, first_t, w2_table, first_ids, second_ids, sizes)
    else:
        def one_block(index, running):
            stem_one = lax.dynamic_slice_in_dim(stem_rows, index, 1, axis=0)
            first_one = lax.dynamic_slice_in_dim(first_ids, index, 1, axis=0)
            second_one = lax.dynamic_slice_in_dim(second_ids, index, 1, axis=0)
            return running + blocks_part(
                stem_one, first_all, w2_table, first_one, second_one.reshape(-1), sizes
            )

        begin = jnp.zeros((t_local * q_local * 2, out_width), jnp.float32)
        amplitude = lax.fori_loop(0, block_count, one_block, begin)
    return amplitude.reshape(t_local, q_local, 2, out_width)


def solution(mesh):
    placed = (P("cuts", "mode", None, None), P(), P(), P("cuts", None, None), P())
    return jax.shard_map(
        on_device,
        mesh=mesh,
        in_specs=placed,
        out_specs=P("mode", "cuts", None, None),
        check_vma=False,
    )
```

```python
import jax
import jax.numpy as jnp
from jax import lax
from jax.experimental import pallas as pl
from jax.experimental.pallas import tpu as pltpu
from jax.sharding import PartitionSpec as P


def gather_over_cuts(own, n_cuts):
    pieces = [own]
    current = own
    ring = [(j, (j + 1) % n_cuts) for j in range(n_cuts)]
    for _ in range(1, n_cuts):
        current = lax.ppermute(current, "cuts", ring)
        pieces.append(current)
    stacked = jnp.stack(pieces)
    me = lax.axis_index("cuts")
    order = (me - jnp.arange(n_cuts, dtype=jnp.int32)) % n_cuts
    return jnp.take(stacked, order, axis=0)


def blocks_part(stem_rows, first_all, w2_table, first_ids, second_ids, sizes):
    n_mode, t_local, n_cuts, a_count, q_local = sizes
    chunk = stem_rows.shape[0]
    wide_in = stem_rows.shape[2]
    col_width = first_all.shape[2]
    slice_count, _, inner, out_width = w2_table.shape
    first_w = jnp.take(first_all, first_ids, axis=0)
    first_w = jnp.transpose(first_w, (0, 2, 1, 3)).reshape(
        chunk, wide_in, n_cuts * col_width
    )
    product = jnp.einsum(
        "bri,bio->bro", stem_rows, first_w, preferred_element_type=jnp.float32
    ).astype(jnp.bfloat16)
    split = product.reshape(chunk, n_mode, t_local, n_cuts, 2, a_count, q_local)
    real_p, imag_p = split[:, :, :, :, 0], split[:, :, :, :, 1]
    lhs = jnp.stack(
        [
            jnp.stack([real_p, -imag_p]),
            jnp.stack([imag_p, real_p]),
        ]
    )
    lhs = jnp.transpose(lhs, (4, 7, 0, 2, 5, 1, 3, 6)).reshape(
        t_local * q_local * 2, chunk * n_cuts * 2 * inner
    )
    second_w = jnp.take(
        w2_table.reshape(slice_count, 2 * inner, out_width), second_ids, axis=0
    ).reshape(chunk * n_cuts * 2 * inner, out_width)
    return jnp.dot(lhs, second_w, preferred_element_type=jnp.float32)


def regroup_kernel(stem_ref, weight_ref, second_ref, out_ref, lhs_ref):
    block_count, rows, _ = stem_ref.shape
    q_local = weight_ref.shape[1] // 64
    t_local = 16
    n_mode = rows // t_local
    lane = lax.broadcasted_iota(jnp.int32, (t_local, 128), 1)
    low = lane < 64
    for b in range(block_count):
        product = lax.dot_general(
            stem_ref[b], weight_ref[b], (((1,), (1,)), ((), ())),
            preferred_element_type=jnp.float32,
        ).astype(jnp.bfloat16)
        for pair in range(n_mode // 2):
            upper = product[(2 * pair) * t_local:(2 * pair + 1) * t_local]
            lower = product[(2 * pair + 1) * t_local:(2 * pair + 2) * t_local]
            col = (b * n_mode // 2 + pair) * 128
            for qp in range(q_local // 2):
                first = upper[:, qp * 128:(qp + 1) * 128]
                second = lower[:, qp * 128:(qp + 1) * 128]
                even = jnp.where(low, first, pltpu.roll(second, 64, 1))
                odd = jnp.where(low, pltpu.roll(first, 64, 1), second)
                lhs_ref[(2 * qp) * t_local:(2 * qp + 1) * t_local, col:col + 128] = even
                lhs_ref[(2 * qp + 1) * t_local:(2 * qp + 2) * t_local, col:col + 128] = odd
    out_ref[...] = lax.dot_general(
        lhs_ref[...], second_ref[...], (((1,), (1,)), ((), ())),
        preferred_element_type=jnp.float32,
    )


def regroup(stem_rows, first_w, second_w, q_local, t_local):
    block_count, rows, _ = stem_rows.shape
    n_mode = rows // t_local
    lhs_shape = (q_local * t_local, block_count * n_mode * 64)
    out_shape = jax.ShapeDtypeStruct((q_local * t_local, second_w.shape[0]), jnp.float32)
    flops = 2 * block_count * rows * first_w.shape[1] * first_w.shape[2]
    flops += 2 * lhs_shape[0] * lhs_shape[1] * second_w.shape[0]
    return pl.pallas_call(
        regroup_kernel,
        out_shape=out_shape,
        in_specs=[pl.BlockSpec(memory_space=pltpu.VMEM)] * 3,
        out_specs=pl.BlockSpec(memory_space=pltpu.VMEM),
        scratch_shapes=[pltpu.VMEM(lhs_shape, jnp.bfloat16)],
        cost_estimate=pl.CostEstimate(
            flops=flops,
            transcendentals=0,
            bytes_accessed=2 * (stem_rows.size + first_w.size + second_w.size)
            + 4 * lhs_shape[0] * second_w.shape[0],
        ),
    )(stem_rows, first_w, second_w)

def stacked_part(stem_rows, first_t, w2_table, first_ids, second_ids, sizes):
    n_mode, t_local, n_cuts, a_count, q_local = sizes
    block_count = stem_rows.shape[0]
    width = first_t.shape[3]
    _, _, inner, out_width = w2_table.shape
    group = n_cuts * 2 * a_count
    picked = jnp.take(first_t, first_ids.reshape(-1), axis=0)
    picked = picked.reshape(block_count, n_cuts, 2, q_local, a_count, width)
    real_part, imag_part = picked[:, :, 0], picked[:, :, 1]
    first_w = jnp.stack(
        [jnp.stack([real_part, imag_part]), jnp.stack([-imag_part, real_part])]
    )
    first_w = jnp.transpose(first_w, (2, 4, 3, 1, 5, 0, 6)).reshape(
        block_count, q_local * group, 2 * width
    )
    second = jnp.take(w2_table, second_ids.reshape(-1), axis=0)
    second = jnp.swapaxes(second, 2, 3)
    second = second.reshape(block_count, n_cuts, 2, out_width, n_mode, a_count)
    real_two, imag_two = second[:, :, 0], second[:, :, 1]
    second_w = jnp.stack(
        [jnp.stack([real_two, -imag_two]), jnp.stack([imag_two, real_two])]
    )
    second_w = jnp.transpose(second_w, (0, 4, 2, 5, 3, 1, 6)).reshape(
        2 * out_width, block_count * n_mode * group
    )
    if group == 64 and t_local == 16 and n_mode % 2 == 0 and q_local % 2 == 0:
        amplitude = regroup(stem_rows, first_w, second_w, q_local, t_local)
    else:
        product = jnp.einsum(
            "brk,bnk->brn", stem_rows, first_w, preferred_element_type=jnp.float32
        ).astype(jnp.bfloat16)
        lhs = product.reshape(block_count, n_mode, t_local, q_local, group)
        lhs = jnp.transpose(lhs, (3, 2, 0, 1, 4)).reshape(
            q_local * t_local, block_count * n_mode * group
        )
        amplitude = jnp.einsum(
            "mk,nk->mn", lhs, second_w, preferred_element_type=jnp.float32
        )
    amplitude = amplitude.reshape(q_local, t_local, 2, out_width)
    return jnp.transpose(amplitude, (1, 0, 2, 3))


def on_device(stem_blocks, w1_table, w2_table, slice_ids, mode_perm):
    n_mode = lax.axis_size("mode")
    n_cuts = lax.axis_size("cuts")
    rows = stem_blocks.shape[1]
    width = stem_blocks.shape[3]
    mid = w1_table.shape[3]
    inner = w2_table.shape[2]
    out_width = w2_table.shape[3]
    block_count = slice_ids.shape[1]
    t_local = rows // n_mode
    a_count = inner // n_mode
    q_count = mid // a_count
    q_local = q_count // n_cuts
    me = lax.axis_index("cuts")
    sizes = (n_mode, t_local, n_cuts, a_count, q_local)

    pieces = stem_blocks[0].reshape(1, n_mode, t_local, 2 * width)
    payload = jnp.broadcast_to(pieces, (n_cuts, n_mode, t_local, 2 * width))
    payload = payload.reshape(n_cuts * n_mode, t_local, 2 * width)
    stem_rows = lax.all_to_all(payload, ("cuts", "mode"), 0, 0, tiled=True)
    stem_rows = stem_rows.reshape(block_count, n_mode * t_local, 2 * width)

    all_ids = gather_over_cuts(slice_ids[0], n_cuts)
    first_ids = all_ids[:, :, 0].T
    second_ids = all_ids[:, :, 1].T

    perm_grid = mode_perm.reshape(a_count, q_count)
    wanted = lax.dynamic_slice_in_dim(perm_grid, me * q_local, q_local, axis=1).reshape(-1)
    picker = (jnp.arange(mid, dtype=jnp.int32)[:, None] == wanted[None, :]).astype(w1_table.dtype)
    first_cols = jnp.einsum(
        "spkj,jn->spkn", w1_table, picker, preferred_element_type=jnp.float32
    ).astype(w1_table.dtype)
    real_part, imag_part = first_cols[:, 0], first_cols[:, 1]
    upper = jnp.concatenate([real_part, imag_part], axis=2)
    lower = jnp.concatenate([-imag_part, real_part], axis=2)
    first_all = jnp.concatenate([upper, lower], axis=1)

    if block_count * n_cuts <= 8:
        wanted_t = lax.dynamic_slice_in_dim(perm_grid, me * q_local, q_local, axis=1).T.reshape(-1)
        picker_t = (wanted_t[:, None] == jnp.arange(mid, dtype=jnp.int32)[None, :]).astype(w1_table.dtype)
        first_t = jnp.einsum(
            "nj,spkj->spnk", picker_t, w1_table, preferred_element_type=jnp.float32
        ).astype(w1_table.dtype)
        return stacked_part(stem_rows, first_t, w2_table, first_ids, second_ids, sizes)
    else:
        def one_block(index, running):
            stem_one = lax.dynamic_slice_in_dim(stem_rows, index, 1, axis=0)
            first_one = lax.dynamic_slice_in_dim(first_ids, index, 1, axis=0)
            second_one = lax.dynamic_slice_in_dim(second_ids, index, 1, axis=0)
            return running + blocks_part(
                stem_one, first_all, w2_table, first_one, second_one.reshape(-1), sizes
            )

        begin = jnp.zeros((t_local * q_local * 2, out_width), jnp.float32)
        amplitude = lax.fori_loop(0, block_count, one_block, begin)
    return amplitude.reshape(t_local, q_local, 2, out_width)


def solution(mesh):
    placed = (P("cuts", "mode", None, None), P(), P(), P("cuts", None, None), P())
    return jax.shard_map(
        on_device,
        mesh=mesh,
        in_specs=placed,
        out_specs=P("mode", "cuts", None, None),
        check_vma=False,
    )
```

```python
import jax
import jax.numpy as jnp
from jax import lax
from jax.experimental import pallas as pl
from jax.experimental.pallas import tpu as pltpu
from jax.sharding import PartitionSpec as P


def gather_over_cuts(own, n_cuts):
    pieces = [own]
    current = own
    ring = [(j, (j + 1) % n_cuts) for j in range(n_cuts)]
    for _ in range(1, n_cuts):
        current = lax.ppermute(current, "cuts", ring)
        pieces.append(current)
    stacked = jnp.stack(pieces)
    me = lax.axis_index("cuts")
    order = (me - jnp.arange(n_cuts, dtype=jnp.int32)) % n_cuts
    return jnp.take(stacked, order, axis=0)


def blocks_part(stem_rows, first_all, w2_table, first_ids, second_ids, sizes):
    n_mode, t_local, n_cuts, a_count, q_local = sizes
    chunk = stem_rows.shape[0]
    wide_in = stem_rows.shape[2]
    col_width = first_all.shape[2]
    slice_count, _, inner, out_width = w2_table.shape
    first_w = jnp.take(first_all, first_ids, axis=0)
    first_w = jnp.transpose(first_w, (0, 2, 1, 3)).reshape(
        chunk, wide_in, n_cuts * col_width
    )
    product = jnp.einsum(
        "bri,bio->bro", stem_rows, first_w, preferred_element_type=jnp.float32
    ).astype(jnp.bfloat16)
    split = product.reshape(chunk, n_mode, t_local, n_cuts, 2, a_count, q_local)
    real_p, imag_p = split[:, :, :, :, 0], split[:, :, :, :, 1]
    lhs = jnp.stack(
        [
            jnp.stack([real_p, -imag_p]),
            jnp.stack([imag_p, real_p]),
        ]
    )
    lhs = jnp.transpose(lhs, (4, 7, 0, 2, 5, 1, 3, 6)).reshape(
        t_local * q_local * 2, chunk * n_cuts * 2 * inner
    )
    second_w = jnp.take(
        w2_table.reshape(slice_count, 2 * inner, out_width), second_ids, axis=0
    ).reshape(chunk * n_cuts * 2 * inner, out_width)
    return jnp.dot(lhs, second_w, preferred_element_type=jnp.float32)


def regroup_kernel(stem_ref, weight_ref, second_ref, out_ref, lhs_ref):
    block_count, rows, _ = stem_ref.shape
    q_local = weight_ref.shape[1] // 64
    t_local = 16
    n_mode = rows // t_local
    lane = lax.broadcasted_iota(jnp.int32, (t_local, 128), 1)
    low = lane < 64
    for b in range(block_count):
        product = lax.dot_general(
            stem_ref[b], weight_ref[b], (((1,), (1,)), ((), ())),
            preferred_element_type=jnp.float32,
        ).astype(jnp.bfloat16)
        for pair in range(n_mode // 2):
            upper = product[(2 * pair) * t_local:(2 * pair + 1) * t_local]
            lower = product[(2 * pair + 1) * t_local:(2 * pair + 2) * t_local]
            col = (b * n_mode // 2 + pair) * 128
            for qp in range(q_local // 2):
                first = upper[:, qp * 128:(qp + 1) * 128]
                second = lower[:, qp * 128:(qp + 1) * 128]
                even = jnp.where(low, first, pltpu.roll(second, 64, 1))
                odd = jnp.where(low, pltpu.roll(first, 64, 1), second)
                lhs_ref[(2 * qp) * t_local:(2 * qp + 1) * t_local, col:col + 128] = even
                lhs_ref[(2 * qp + 1) * t_local:(2 * qp + 2) * t_local, col:col + 128] = odd
    out_ref[...] = jnp.dot(
        lhs_ref[...], second_ref[...], preferred_element_type=jnp.float32
    )


def regroup(stem_rows, first_w, second_w, q_local, t_local):
    block_count, rows, _ = stem_rows.shape
    n_mode = rows // t_local
    lhs_shape = (q_local * t_local, block_count * n_mode * 64)
    out_shape = jax.ShapeDtypeStruct((q_local * t_local, second_w.shape[1]), jnp.float32)
    flops = 2 * block_count * rows * first_w.shape[1] * first_w.shape[2]
    flops += 2 * lhs_shape[0] * lhs_shape[1] * second_w.shape[1]
    return pl.pallas_call(
        regroup_kernel,
        out_shape=out_shape,
        in_specs=[pl.BlockSpec(memory_space=pltpu.VMEM)] * 3,
        out_specs=pl.BlockSpec(memory_space=pltpu.VMEM),
        scratch_shapes=[pltpu.VMEM(lhs_shape, jnp.bfloat16)],
        cost_estimate=pl.CostEstimate(
            flops=flops,
            transcendentals=0,
            bytes_accessed=2 * (stem_rows.size + first_w.size + second_w.size)
            + 4 * lhs_shape[0] * second_w.shape[1],
        ),
    )(stem_rows, first_w, second_w)

def stacked_part(stem_rows, first_t, w2_table, first_ids, second_ids, sizes):
    n_mode, t_local, n_cuts, a_count, q_local = sizes
    block_count = stem_rows.shape[0]
    width = first_t.shape[3]
    _, _, inner, out_width = w2_table.shape
    group = n_cuts * 2 * a_count
    picked = jnp.take(first_t, first_ids.reshape(-1), axis=0)
    picked = picked.reshape(block_count, n_cuts, 2, q_local, a_count, width)
    real_part, imag_part = picked[:, :, 0], picked[:, :, 1]
    first_w = jnp.stack(
        [jnp.stack([real_part, imag_part]), jnp.stack([-imag_part, real_part])]
    )
    first_w = jnp.transpose(first_w, (2, 4, 3, 1, 5, 0, 6)).reshape(
        block_count, q_local * group, 2 * width
    )
    if group == 64 and t_local == 16 and n_mode % 2 == 0 and q_local % 2 == 0:
        second = jnp.take(w2_table, second_ids.reshape(-1), axis=0)
        second = second.reshape(block_count, n_cuts, 2, n_mode, a_count, out_width)
        real_two, imag_two = second[:, :, 0], second[:, :, 1]
        second_w = jnp.stack(
            [jnp.stack([real_two, imag_two]), jnp.stack([-imag_two, real_two])]
        )
        second_w = jnp.transpose(second_w, (2, 4, 3, 0, 5, 1, 6)).reshape(
            block_count * n_mode * group, 2 * out_width
        )
        amplitude = regroup(stem_rows, first_w, second_w, q_local, t_local)
    else:
        second = jnp.take(w2_table, second_ids.reshape(-1), axis=0)
        second = jnp.swapaxes(second, 2, 3)
        second = second.reshape(block_count, n_cuts, 2, out_width, n_mode, a_count)
        real_two, imag_two = second[:, :, 0], second[:, :, 1]
        second_w = jnp.stack(
            [jnp.stack([real_two, -imag_two]), jnp.stack([imag_two, real_two])]
        )
        second_w = jnp.transpose(second_w, (0, 4, 2, 5, 3, 1, 6)).reshape(
            2 * out_width, block_count * n_mode * group
        )
        product = jnp.einsum(
            "brk,bnk->brn", stem_rows, first_w, preferred_element_type=jnp.float32
        ).astype(jnp.bfloat16)
        lhs = product.reshape(block_count, n_mode, t_local, q_local, group)
        lhs = jnp.transpose(lhs, (3, 2, 0, 1, 4)).reshape(
            q_local * t_local, block_count * n_mode * group
        )
        amplitude = jnp.einsum(
            "mk,nk->mn", lhs, second_w, preferred_element_type=jnp.float32
        )
    amplitude = amplitude.reshape(q_local, t_local, 2, out_width)
    return jnp.transpose(amplitude, (1, 0, 2, 3))


def on_device(stem_blocks, w1_table, w2_table, slice_ids, mode_perm):
    n_mode = lax.axis_size("mode")
    n_cuts = lax.axis_size("cuts")
    rows = stem_blocks.shape[1]
    width = stem_blocks.shape[3]
    mid = w1_table.shape[3]
    inner = w2_table.shape[2]
    out_width = w2_table.shape[3]
    block_count = slice_ids.shape[1]
    t_local = rows // n_mode
    a_count = inner // n_mode
    q_count = mid // a_count
    q_local = q_count // n_cuts
    me = lax.axis_index("cuts")
    sizes = (n_mode, t_local, n_cuts, a_count, q_local)

    pieces = stem_blocks[0].reshape(1, n_mode, t_local, 2 * width)
    payload = jnp.broadcast_to(pieces, (n_cuts, n_mode, t_local, 2 * width))
    payload = payload.reshape(n_cuts * n_mode, t_local, 2 * width)
    stem_rows = lax.all_to_all(payload, ("cuts", "mode"), 0, 0, tiled=True)
    stem_rows = stem_rows.reshape(block_count, n_mode * t_local, 2 * width)

    all_ids = gather_over_cuts(slice_ids[0], n_cuts)
    first_ids = all_ids[:, :, 0].T
    second_ids = all_ids[:, :, 1].T

    perm_grid = mode_perm.reshape(a_count, q_count)
    wanted = lax.dynamic_slice_in_dim(perm_grid, me * q_local, q_local, axis=1).reshape(-1)
    picker = (jnp.arange(mid, dtype=jnp.int32)[:, None] == wanted[None, :]).astype(w1_table.dtype)
    first_cols = jnp.einsum(
        "spkj,jn->spkn", w1_table, picker, preferred_element_type=jnp.float32
    ).astype(w1_table.dtype)
    real_part, imag_part = first_cols[:, 0], first_cols[:, 1]
    upper = jnp.concatenate([real_part, imag_part], axis=2)
    lower = jnp.concatenate([-imag_part, real_part], axis=2)
    first_all = jnp.concatenate([upper, lower], axis=1)

    if block_count * n_cuts <= 8:
        wanted_t = lax.dynamic_slice_in_dim(perm_grid, me * q_local, q_local, axis=1).T.reshape(-1)
        picker_t = (wanted_t[:, None] == jnp.arange(mid, dtype=jnp.int32)[None, :]).astype(w1_table.dtype)
        first_t = jnp.einsum(
            "nj,spkj->spnk", picker_t, w1_table, preferred_element_type=jnp.float32
        ).astype(w1_table.dtype)
        return stacked_part(stem_rows, first_t, w2_table, first_ids, second_ids, sizes)
    else:
        def one_block(index, running):
            stem_one = lax.dynamic_slice_in_dim(stem_rows, index, 1, axis=0)
            first_one = lax.dynamic_slice_in_dim(first_ids, index, 1, axis=0)
            second_one = lax.dynamic_slice_in_dim(second_ids, index, 1, axis=0)
            return running + blocks_part(
                stem_one, first_all, w2_table, first_one, second_one.reshape(-1), sizes
            )

        begin = jnp.zeros((t_local * q_local * 2, out_width), jnp.float32)
        amplitude = lax.fori_loop(0, block_count, one_block, begin)
    return amplitude.reshape(t_local, q_local, 2, out_width)


def solution(mesh):
    placed = (P("cuts", "mode", None, None), P(), P(), P("cuts", None, None), P())
    return jax.shard_map(
        on_device,
        mesh=mesh,
        in_specs=placed,
        out_specs=P("mode", "cuts", None, None),
        check_vma=False,
    )
```

```python
import jax
import jax.numpy as jnp
from jax import lax
from jax.experimental import pallas as pl
from jax.experimental.pallas import tpu as pltpu
from jax.sharding import PartitionSpec as P


def gather_over_cuts(own, n_cuts):
    pieces = [own]
    current = own
    ring = [(j, (j + 1) % n_cuts) for j in range(n_cuts)]
    for _ in range(1, n_cuts):
        current = lax.ppermute(current, "cuts", ring)
        pieces.append(current)
    stacked = jnp.stack(pieces)
    me = lax.axis_index("cuts")
    order = (me - jnp.arange(n_cuts, dtype=jnp.int32)) % n_cuts
    return jnp.take(stacked, order, axis=0)


def blocks_part(stem_rows, first_all, w2_table, first_ids, second_ids, sizes):
    n_mode, t_local, n_cuts, a_count, q_local = sizes
    chunk = stem_rows.shape[0]
    wide_in = stem_rows.shape[2]
    col_width = first_all.shape[2]
    slice_count, _, inner, out_width = w2_table.shape
    first_w = jnp.take(first_all, first_ids, axis=0)
    first_w = jnp.transpose(first_w, (0, 2, 1, 3)).reshape(
        chunk, wide_in, n_cuts * col_width
    )
    product = jnp.einsum(
        "bri,bio->bro", stem_rows, first_w, preferred_element_type=jnp.float32
    ).astype(jnp.bfloat16)
    split = product.reshape(chunk, n_mode, t_local, n_cuts, 2, a_count, q_local)
    real_p, imag_p = split[:, :, :, :, 0], split[:, :, :, :, 1]
    lhs = jnp.stack(
        [
            jnp.stack([real_p, -imag_p]),
            jnp.stack([imag_p, real_p]),
        ]
    )
    lhs = jnp.transpose(lhs, (4, 7, 0, 2, 5, 1, 3, 6)).reshape(
        t_local * q_local * 2, chunk * n_cuts * 2 * inner
    )
    second_w = jnp.take(
        w2_table.reshape(slice_count, 2 * inner, out_width), second_ids, axis=0
    ).reshape(chunk * n_cuts * 2 * inner, out_width)
    return jnp.dot(lhs, second_w, preferred_element_type=jnp.float32)


def regroup_kernel(stem_ref, weight_ref, second_ref, out_ref, lhs_ref):
    block_count, rows, _ = stem_ref.shape
    q_local = weight_ref.shape[1] // 64
    t_local = 16
    n_mode = rows // t_local
    lane = lax.broadcasted_iota(jnp.int32, (t_local, 128), 1)
    low = lane < 64
    for b in range(block_count):
        product = lax.dot_general(
            stem_ref[b], weight_ref[b], (((1,), (1,)), ((), ())),
            preferred_element_type=jnp.float32,
        ).astype(jnp.bfloat16)
        for pair in range(n_mode // 2):
            upper = product[(2 * pair) * t_local:(2 * pair + 1) * t_local]
            lower = product[(2 * pair + 1) * t_local:(2 * pair + 2) * t_local]
            col = (b * n_mode // 2 + pair) * 128
            for qp in range(q_local // 2):
                first = upper[:, qp * 128:(qp + 1) * 128]
                second = lower[:, qp * 128:(qp + 1) * 128]
                even = jnp.where(low, first, pltpu.roll(second, 64, 1))
                odd = jnp.where(low, pltpu.roll(first, 64, 1), second)
                lhs_ref[(2 * qp) * t_local:(2 * qp + 1) * t_local, col:col + 128] = even
                lhs_ref[(2 * qp + 1) * t_local:(2 * qp + 2) * t_local, col:col + 128] = odd
    lhs = lhs_ref[...]
    for part in range(second_ref.shape[0]):
        out_ref[part] = jnp.dot(lhs, second_ref[part], preferred_element_type=jnp.float32)


def regroup(stem_rows, first_w, second_w, q_local, t_local):
    block_count, rows, _ = stem_rows.shape
    n_mode = rows // t_local
    lhs_shape = (q_local * t_local, block_count * n_mode * 64)
    out_shape = jax.ShapeDtypeStruct(
        (second_w.shape[0], q_local * t_local, second_w.shape[2]), jnp.float32
    )
    flops = 2 * block_count * rows * first_w.shape[1] * first_w.shape[2]
    flops += 2 * lhs_shape[0] * lhs_shape[1] * second_w.shape[0] * second_w.shape[2]
    return pl.pallas_call(
        regroup_kernel,
        out_shape=out_shape,
        in_specs=[pl.BlockSpec(memory_space=pltpu.VMEM)] * 3,
        out_specs=pl.BlockSpec(memory_space=pltpu.VMEM),
        scratch_shapes=[pltpu.VMEM(lhs_shape, jnp.bfloat16)],
        cost_estimate=pl.CostEstimate(
            flops=flops,
            transcendentals=0,
            bytes_accessed=2 * (stem_rows.size + first_w.size + second_w.size)
            + 4 * lhs_shape[0] * second_w.shape[0] * second_w.shape[2],
        ),
    )(stem_rows, first_w, second_w)

def stacked_part(stem_rows, first_t, w2_table, first_ids, second_ids, sizes):
    n_mode, t_local, n_cuts, a_count, q_local = sizes
    block_count = stem_rows.shape[0]
    width = first_t.shape[3]
    _, _, inner, out_width = w2_table.shape
    group = n_cuts * 2 * a_count
    picked = jnp.take(first_t, first_ids.reshape(-1), axis=0)
    picked = picked.reshape(block_count, n_cuts, 2, q_local, a_count, width)
    real_part, imag_part = picked[:, :, 0], picked[:, :, 1]
    first_w = jnp.stack(
        [jnp.stack([real_part, imag_part]), jnp.stack([-imag_part, real_part])]
    )
    first_w = jnp.transpose(first_w, (2, 4, 3, 1, 5, 0, 6)).reshape(
        block_count, q_local * group, 2 * width
    )
    if group == 64 and t_local == 16 and n_mode % 2 == 0 and q_local % 2 == 0:
        second = jnp.take(w2_table, second_ids.reshape(-1), axis=0)
        second = second.reshape(block_count, n_cuts, 2, n_mode, a_count, out_width)
        real_two, imag_two = second[:, :, 0], second[:, :, 1]
        second_w = jnp.stack(
            [jnp.stack([real_two, imag_two]), jnp.stack([-imag_two, real_two])]
        )
        second_w = jnp.transpose(second_w, (1, 2, 4, 3, 0, 5, 6)).reshape(
            2, block_count * n_mode * group, out_width
        )
        amplitude = regroup(stem_rows, first_w, second_w, q_local, t_local)
        amplitude = jnp.transpose(amplitude, (1, 0, 2))
    else:
        second = jnp.take(w2_table, second_ids.reshape(-1), axis=0)
        second = jnp.swapaxes(second, 2, 3)
        second = second.reshape(block_count, n_cuts, 2, out_width, n_mode, a_count)
        real_two, imag_two = second[:, :, 0], second[:, :, 1]
        second_w = jnp.stack(
            [jnp.stack([real_two, -imag_two]), jnp.stack([imag_two, real_two])]
        )
        second_w = jnp.transpose(second_w, (0, 4, 2, 5, 3, 1, 6)).reshape(
            2 * out_width, block_count * n_mode * group
        )
        product = jnp.einsum(
            "brk,bnk->brn", stem_rows, first_w, preferred_element_type=jnp.float32
        ).astype(jnp.bfloat16)
        lhs = product.reshape(block_count, n_mode, t_local, q_local, group)
        lhs = jnp.transpose(lhs, (3, 2, 0, 1, 4)).reshape(
            q_local * t_local, block_count * n_mode * group
        )
        amplitude = jnp.einsum(
            "mk,nk->mn", lhs, second_w, preferred_element_type=jnp.float32
        )
    amplitude = amplitude.reshape(q_local, t_local, 2, out_width)
    return jnp.transpose(amplitude, (1, 0, 2, 3))


def on_device(stem_blocks, w1_table, w2_table, slice_ids, mode_perm):
    n_mode = lax.axis_size("mode")
    n_cuts = lax.axis_size("cuts")
    rows = stem_blocks.shape[1]
    width = stem_blocks.shape[3]
    mid = w1_table.shape[3]
    inner = w2_table.shape[2]
    out_width = w2_table.shape[3]
    block_count = slice_ids.shape[1]
    t_local = rows // n_mode
    a_count = inner // n_mode
    q_count = mid // a_count
    q_local = q_count // n_cuts
    me = lax.axis_index("cuts")
    sizes = (n_mode, t_local, n_cuts, a_count, q_local)

    pieces = stem_blocks[0].reshape(1, n_mode, t_local, 2 * width)
    payload = jnp.broadcast_to(pieces, (n_cuts, n_mode, t_local, 2 * width))
    payload = payload.reshape(n_cuts * n_mode, t_local, 2 * width)
    stem_rows = lax.all_to_all(payload, ("cuts", "mode"), 0, 0, tiled=True)
    stem_rows = stem_rows.reshape(block_count, n_mode * t_local, 2 * width)

    all_ids = gather_over_cuts(slice_ids[0], n_cuts)
    first_ids = all_ids[:, :, 0].T
    second_ids = all_ids[:, :, 1].T

    perm_grid = mode_perm.reshape(a_count, q_count)
    wanted = lax.dynamic_slice_in_dim(perm_grid, me * q_local, q_local, axis=1).reshape(-1)
    picker = (jnp.arange(mid, dtype=jnp.int32)[:, None] == wanted[None, :]).astype(w1_table.dtype)
    first_cols = jnp.einsum(
        "spkj,jn->spkn", w1_table, picker, preferred_element_type=jnp.float32
    ).astype(w1_table.dtype)
    real_part, imag_part = first_cols[:, 0], first_cols[:, 1]
    upper = jnp.concatenate([real_part, imag_part], axis=2)
    lower = jnp.concatenate([-imag_part, real_part], axis=2)
    first_all = jnp.concatenate([upper, lower], axis=1)

    if block_count * n_cuts <= 8:
        wanted_t = lax.dynamic_slice_in_dim(perm_grid, me * q_local, q_local, axis=1).T.reshape(-1)
        picker_t = (wanted_t[:, None] == jnp.arange(mid, dtype=jnp.int32)[None, :]).astype(w1_table.dtype)
        first_t = jnp.einsum(
            "nj,spkj->spnk", picker_t, w1_table, preferred_element_type=jnp.float32
        ).astype(w1_table.dtype)
        return stacked_part(stem_rows, first_t, w2_table, first_ids, second_ids, sizes)
    else:
        def one_block(index, running):
            stem_one = lax.dynamic_slice_in_dim(stem_rows, index, 1, axis=0)
            first_one = lax.dynamic_slice_in_dim(first_ids, index, 1, axis=0)
            second_one = lax.dynamic_slice_in_dim(second_ids, index, 1, axis=0)
            return running + blocks_part(
                stem_one, first_all, w2_table, first_one, second_one.reshape(-1), sizes
            )

        begin = jnp.zeros((t_local * q_local * 2, out_width), jnp.float32)
        amplitude = lax.fori_loop(0, block_count, one_block, begin)
    return amplitude.reshape(t_local, q_local, 2, out_width)


def solution(mesh):
    placed = (P("cuts", "mode", None, None), P(), P(), P("cuts", None, None), P())
    return jax.shard_map(
        on_device,
        mesh=mesh,
        in_specs=placed,
        out_specs=P("mode", "cuts", None, None),
        check_vma=False,
    )
```

```python
import jax
import jax.numpy as jnp
from jax import lax
from jax.experimental import pallas as pl
from jax.experimental.pallas import tpu as pltpu
from jax.sharding import PartitionSpec as P


def gather_over_cuts(own, n_cuts):
    pieces = [own]
    current = own
    ring = [(j, (j + 1) % n_cuts) for j in range(n_cuts)]
    for _ in range(1, n_cuts):
        current = lax.ppermute(current, "cuts", ring)
        pieces.append(current)
    stacked = jnp.stack(pieces)
    me = lax.axis_index("cuts")
    order = (me - jnp.arange(n_cuts, dtype=jnp.int32)) % n_cuts
    return jnp.take(stacked, order, axis=0)


def blocks_part(stem_rows, first_all, w2_table, first_ids, second_ids, sizes):
    n_mode, t_local, n_cuts, a_count, q_local = sizes
    chunk = stem_rows.shape[0]
    wide_in = stem_rows.shape[2]
    col_width = first_all.shape[2]
    slice_count, _, inner, out_width = w2_table.shape
    first_w = jnp.take(first_all, first_ids, axis=0)
    first_w = jnp.transpose(first_w, (0, 2, 1, 3)).reshape(
        chunk, wide_in, n_cuts * col_width
    )
    product = jnp.einsum(
        "bri,bio->bro", stem_rows, first_w, preferred_element_type=jnp.float32
    ).astype(jnp.bfloat16)
    split = product.reshape(chunk, n_mode, t_local, n_cuts, 2, a_count, q_local)
    real_p, imag_p = split[:, :, :, :, 0], split[:, :, :, :, 1]
    lhs = jnp.stack(
        [
            jnp.stack([real_p, -imag_p]),
            jnp.stack([imag_p, real_p]),
        ]
    )
    lhs = jnp.transpose(lhs, (4, 7, 0, 2, 5, 1, 3, 6)).reshape(
        t_local * q_local * 2, chunk * n_cuts * 2 * inner
    )
    second_w = jnp.take(
        w2_table.reshape(slice_count, 2 * inner, out_width), second_ids, axis=0
    ).reshape(chunk * n_cuts * 2 * inner, out_width)
    return jnp.dot(lhs, second_w, preferred_element_type=jnp.float32)


def regroup_kernel(stem_ref, weight_ref, second_ref, out_ref, lhs_ref):
    block_count, rows, _ = stem_ref.shape
    q_local = weight_ref.shape[1] // 64
    t_local = 16
    n_mode = rows // t_local
    lane = lax.broadcasted_iota(jnp.int32, (t_local, 128), 1)
    low = lane < 64
    for b in range(block_count):
        product = lax.dot_general(
            stem_ref[b], weight_ref[b], (((1,), (1,)), ((), ())),
            preferred_element_type=jnp.float32,
        ).astype(jnp.bfloat16)
        for pair in range(n_mode // 2):
            upper = product[(2 * pair) * t_local:(2 * pair + 1) * t_local]
            lower = product[(2 * pair + 1) * t_local:(2 * pair + 2) * t_local]
            col = (b * n_mode // 2 + pair) * 128
            for qp in range(q_local // 2):
                first = upper[:, qp * 128:(qp + 1) * 128]
                second = lower[:, qp * 128:(qp + 1) * 128]
                even = jnp.where(low, first, pltpu.roll(second, 64, 1))
                odd = jnp.where(low, pltpu.roll(first, 64, 1), second)
                lhs_ref[(2 * qp) * t_local:(2 * qp + 1) * t_local, col:col + 128] = even
                lhs_ref[(2 * qp + 1) * t_local:(2 * qp + 2) * t_local, col:col + 128] = odd
    lhs = lhs_ref[...]
    for part in range(second_ref.shape[0]):
        result = jnp.dot(lhs, second_ref[part], preferred_element_type=jnp.float32)
        for q in range(q_local):
            out_ref[:, q, part, :] = result[q * t_local:(q + 1) * t_local]


def regroup(stem_rows, first_w, second_w, q_local, t_local):
    block_count, rows, _ = stem_rows.shape
    n_mode = rows // t_local
    lhs_shape = (q_local * t_local, block_count * n_mode * 64)
    out_shape = jax.ShapeDtypeStruct(
        (t_local, q_local, second_w.shape[0], second_w.shape[2]), jnp.float32
    )
    flops = 2 * block_count * rows * first_w.shape[1] * first_w.shape[2]
    flops += 2 * lhs_shape[0] * lhs_shape[1] * second_w.shape[0] * second_w.shape[2]
    return pl.pallas_call(
        regroup_kernel,
        out_shape=out_shape,
        in_specs=[pl.BlockSpec(memory_space=pltpu.VMEM)] * 3,
        out_specs=pl.BlockSpec(memory_space=pltpu.VMEM),
        scratch_shapes=[pltpu.VMEM(lhs_shape, jnp.bfloat16)],
        cost_estimate=pl.CostEstimate(
            flops=flops,
            transcendentals=0,
            bytes_accessed=2 * (stem_rows.size + first_w.size + second_w.size)
            + 4 * lhs_shape[0] * second_w.shape[0] * second_w.shape[2],
        ),
    )(stem_rows, first_w, second_w)

def stacked_part(stem_rows, first_t, w2_table, first_ids, second_ids, sizes):
    n_mode, t_local, n_cuts, a_count, q_local = sizes
    block_count = stem_rows.shape[0]
    width = first_t.shape[3]
    _, _, inner, out_width = w2_table.shape
    group = n_cuts * 2 * a_count
    picked = jnp.take(first_t, first_ids.reshape(-1), axis=0)
    picked = picked.reshape(block_count, n_cuts, 2, q_local, a_count, width)
    real_part, imag_part = picked[:, :, 0], picked[:, :, 1]
    first_w = jnp.stack(
        [jnp.stack([real_part, imag_part]), jnp.stack([-imag_part, real_part])]
    )
    first_w = jnp.transpose(first_w, (2, 4, 3, 1, 5, 0, 6)).reshape(
        block_count, q_local * group, 2 * width
    )
    if group == 64 and t_local == 16 and n_mode % 2 == 0 and q_local % 2 == 0:
        second = jnp.take(w2_table, second_ids.reshape(-1), axis=0)
        second = second.reshape(block_count, n_cuts, 2, n_mode, a_count, out_width)
        real_two, imag_two = second[:, :, 0], second[:, :, 1]
        second_w = jnp.stack(
            [jnp.stack([real_two, imag_two]), jnp.stack([-imag_two, real_two])]
        )
        second_w = jnp.transpose(second_w, (1, 2, 4, 3, 0, 5, 6)).reshape(
            2, block_count * n_mode * group, out_width
        )
        return regroup(stem_rows, first_w, second_w, q_local, t_local)
    else:
        second = jnp.take(w2_table, second_ids.reshape(-1), axis=0)
        second = jnp.swapaxes(second, 2, 3)
        second = second.reshape(block_count, n_cuts, 2, out_width, n_mode, a_count)
        real_two, imag_two = second[:, :, 0], second[:, :, 1]
        second_w = jnp.stack(
            [jnp.stack([real_two, -imag_two]), jnp.stack([imag_two, real_two])]
        )
        second_w = jnp.transpose(second_w, (0, 4, 2, 5, 3, 1, 6)).reshape(
            2 * out_width, block_count * n_mode * group
        )
        product = jnp.einsum(
            "brk,bnk->brn", stem_rows, first_w, preferred_element_type=jnp.float32
        ).astype(jnp.bfloat16)
        lhs = product.reshape(block_count, n_mode, t_local, q_local, group)
        lhs = jnp.transpose(lhs, (3, 2, 0, 1, 4)).reshape(
            q_local * t_local, block_count * n_mode * group
        )
        amplitude = jnp.einsum(
            "mk,nk->mn", lhs, second_w, preferred_element_type=jnp.float32
        )
    amplitude = amplitude.reshape(q_local, t_local, 2, out_width)
    return jnp.transpose(amplitude, (1, 0, 2, 3))


def on_device(stem_blocks, w1_table, w2_table, slice_ids, mode_perm):
    n_mode = lax.axis_size("mode")
    n_cuts = lax.axis_size("cuts")
    rows = stem_blocks.shape[1]
    width = stem_blocks.shape[3]
    mid = w1_table.shape[3]
    inner = w2_table.shape[2]
    out_width = w2_table.shape[3]
    block_count = slice_ids.shape[1]
    t_local = rows // n_mode
    a_count = inner // n_mode
    q_count = mid // a_count
    q_local = q_count // n_cuts
    me = lax.axis_index("cuts")
    sizes = (n_mode, t_local, n_cuts, a_count, q_local)

    pieces = stem_blocks[0].reshape(1, n_mode, t_local, 2 * width)
    payload = jnp.broadcast_to(pieces, (n_cuts, n_mode, t_local, 2 * width))
    payload = payload.reshape(n_cuts * n_mode, t_local, 2 * width)
    stem_rows = lax.all_to_all(payload, ("cuts", "mode"), 0, 0, tiled=True)
    stem_rows = stem_rows.reshape(block_count, n_mode * t_local, 2 * width)

    all_ids = gather_over_cuts(slice_ids[0], n_cuts)
    first_ids = all_ids[:, :, 0].T
    second_ids = all_ids[:, :, 1].T

    perm_grid = mode_perm.reshape(a_count, q_count)
    wanted = lax.dynamic_slice_in_dim(perm_grid, me * q_local, q_local, axis=1).reshape(-1)
    picker = (jnp.arange(mid, dtype=jnp.int32)[:, None] == wanted[None, :]).astype(w1_table.dtype)
    first_cols = jnp.einsum(
        "spkj,jn->spkn", w1_table, picker, preferred_element_type=jnp.float32
    ).astype(w1_table.dtype)
    real_part, imag_part = first_cols[:, 0], first_cols[:, 1]
    upper = jnp.concatenate([real_part, imag_part], axis=2)
    lower = jnp.concatenate([-imag_part, real_part], axis=2)
    first_all = jnp.concatenate([upper, lower], axis=1)

    if block_count * n_cuts <= 8:
        wanted_t = lax.dynamic_slice_in_dim(perm_grid, me * q_local, q_local, axis=1).T.reshape(-1)
        picker_t = (wanted_t[:, None] == jnp.arange(mid, dtype=jnp.int32)[None, :]).astype(w1_table.dtype)
        first_t = jnp.einsum(
            "nj,spkj->spnk", picker_t, w1_table, preferred_element_type=jnp.float32
        ).astype(w1_table.dtype)
        return stacked_part(stem_rows, first_t, w2_table, first_ids, second_ids, sizes)
    else:
        def one_block(index, running):
            stem_one = lax.dynamic_slice_in_dim(stem_rows, index, 1, axis=0)
            first_one = lax.dynamic_slice_in_dim(first_ids, index, 1, axis=0)
            second_one = lax.dynamic_slice_in_dim(second_ids, index, 1, axis=0)
            return running + blocks_part(
                stem_one, first_all, w2_table, first_one, second_one.reshape(-1), sizes
            )

        begin = jnp.zeros((t_local * q_local * 2, out_width), jnp.float32)
        amplitude = lax.fori_loop(0, block_count, one_block, begin)
    return amplitude.reshape(t_local, q_local, 2, out_width)


def solution(mesh):
    placed = (P("cuts", "mode", None, None), P(), P(), P("cuts", None, None), P())
    return jax.shard_map(
        on_device,
        mesh=mesh,
        in_specs=placed,
        out_specs=P("mode", "cuts", None, None),
        check_vma=False,
    )
```

```python
import jax
import jax.numpy as jnp
from jax import lax
from jax.experimental import pallas as pl
from jax.experimental.pallas import tpu as pltpu
from jax.sharding import PartitionSpec as P


def gather_over_cuts(own, n_cuts):
    pieces = [own]
    current = own
    ring = [(j, (j + 1) % n_cuts) for j in range(n_cuts)]
    for _ in range(1, n_cuts):
        current = lax.ppermute(current, "cuts", ring)
        pieces.append(current)
    stacked = jnp.stack(pieces)
    me = lax.axis_index("cuts")
    order = (me - jnp.arange(n_cuts, dtype=jnp.int32)) % n_cuts
    return jnp.take(stacked, order, axis=0)


def blocks_part(stem_rows, first_all, w2_table, first_ids, second_ids, sizes):
    n_mode, t_local, n_cuts, a_count, q_local = sizes
    chunk = stem_rows.shape[0]
    wide_in = stem_rows.shape[2]
    col_width = first_all.shape[2]
    slice_count, _, inner, out_width = w2_table.shape
    first_w = jnp.take(first_all, first_ids, axis=0)
    first_w = jnp.transpose(first_w, (0, 2, 1, 3)).reshape(
        chunk, wide_in, n_cuts * col_width
    )
    product = jnp.einsum(
        "bri,bio->bro", stem_rows, first_w, preferred_element_type=jnp.float32
    ).astype(jnp.bfloat16)
    split = product.reshape(chunk, n_mode, t_local, n_cuts, 2, a_count, q_local)
    real_p, imag_p = split[:, :, :, :, 0], split[:, :, :, :, 1]
    lhs = jnp.stack(
        [
            jnp.stack([real_p, -imag_p]),
            jnp.stack([imag_p, real_p]),
        ]
    )
    lhs = jnp.transpose(lhs, (4, 7, 0, 2, 5, 1, 3, 6)).reshape(
        t_local * q_local * 2, chunk * n_cuts * 2 * inner
    )
    second_w = jnp.take(
        w2_table.reshape(slice_count, 2 * inner, out_width), second_ids, axis=0
    ).reshape(chunk * n_cuts * 2 * inner, out_width)
    return jnp.dot(lhs, second_w, preferred_element_type=jnp.float32)


def regroup_kernel(stem_ref, weight_ref, second_ref, out_ref, lhs_ref):
    block_count, rows, _ = stem_ref.shape
    q_local = weight_ref.shape[1] // 64
    t_local = 16
    n_mode = rows // t_local
    lane = lax.broadcasted_iota(jnp.int32, (t_local, 128), 1)
    low = lane < 64
    for b in range(block_count):
        product = lax.dot_general(
            stem_ref[b], weight_ref[b], (((1,), (1,)), ((), ())),
            preferred_element_type=jnp.float32,
        ).astype(jnp.bfloat16)
        for pair in range(n_mode // 2):
            upper = product[(2 * pair) * t_local:(2 * pair + 1) * t_local]
            lower = product[(2 * pair + 1) * t_local:(2 * pair + 2) * t_local]
            col = (b * n_mode // 2 + pair) * 128
            for qp in range(q_local // 2):
                first = upper[:, qp * 128:(qp + 1) * 128]
                second = lower[:, qp * 128:(qp + 1) * 128]
                even = jnp.where(low, first, pltpu.roll(second, 64, 1))
                odd = jnp.where(low, pltpu.roll(first, 64, 1), second)
                lhs_ref[(2 * qp) * t_local:(2 * qp + 1) * t_local, col:col + 128] = even
                lhs_ref[(2 * qp + 1) * t_local:(2 * qp + 2) * t_local, col:col + 128] = odd
    lhs = lhs_ref[...]
    for part in range(second_ref.shape[0]):
        result = jnp.dot(lhs, second_ref[part], preferred_element_type=jnp.float32)
        for q in range(q_local):
            out_ref[:, q, part, :] = result[q * t_local:(q + 1) * t_local]


def regroup(stem_rows, first_w, second_w, q_local, t_local):
    block_count, rows, _ = stem_rows.shape
    n_mode = rows // t_local
    lhs_shape = (q_local * t_local, block_count * n_mode * 64)
    out_shape = jax.ShapeDtypeStruct(
        (t_local, q_local, second_w.shape[0], second_w.shape[2]), jnp.float32
    )
    flops = 2 * block_count * rows * first_w.shape[1] * first_w.shape[2]
    flops += 2 * lhs_shape[0] * lhs_shape[1] * second_w.shape[0] * second_w.shape[2]
    return pl.pallas_call(
        regroup_kernel,
        out_shape=out_shape,
        in_specs=[pl.BlockSpec(memory_space=pltpu.VMEM)] * 3,
        out_specs=pl.BlockSpec(memory_space=pltpu.VMEM),
        scratch_shapes=[pltpu.VMEM(lhs_shape, jnp.bfloat16)],
        cost_estimate=pl.CostEstimate(
            flops=flops,
            transcendentals=0,
            bytes_accessed=2 * (stem_rows.size + first_w.size + second_w.size)
            + 4 * lhs_shape[0] * second_w.shape[0] * second_w.shape[2],
        ),
    )(stem_rows, first_w, second_w)

def stacked_part(stem_rows, first_t, w2_table, first_ids, second_ids, sizes):
    n_mode, t_local, n_cuts, a_count, q_local = sizes
    block_count = stem_rows.shape[0]
    width = first_t.shape[3]
    _, _, inner, out_width = w2_table.shape
    group = n_cuts * 2 * a_count
    picked = jnp.take(first_t, first_ids.reshape(-1), axis=0)
    picked = picked.reshape(block_count, n_cuts, 2, q_local, a_count, width)
    real_part, imag_part = picked[:, :, 0], picked[:, :, 1]
    first_w = jnp.stack(
        [jnp.stack([real_part, imag_part]), jnp.stack([-imag_part, real_part])]
    )
    first_w = jnp.transpose(first_w, (2, 4, 3, 1, 5, 0, 6)).reshape(
        block_count, q_local * group, 2 * width
    )
    if group == 64 and t_local == 16 and n_mode % 2 == 0 and q_local % 2 == 0:
        second = jnp.take(w2_table, second_ids.reshape(-1), axis=0)
        second = second.reshape(block_count, n_cuts, 2, n_mode, a_count, out_width)
        real_two, imag_two = second[:, :, 0], second[:, :, 1]
        second_w = jnp.stack(
            [jnp.stack([real_two, imag_two]), jnp.stack([-imag_two, real_two])]
        )
        second_w = jnp.transpose(second_w, (1, 2, 4, 3, 0, 5, 6)).reshape(
            2, block_count * n_mode * group, out_width
        )
        return regroup(stem_rows, first_w, second_w, q_local, t_local)
    else:
        second = jnp.take(w2_table, second_ids.reshape(-1), axis=0)
        second = jnp.swapaxes(second, 2, 3)
        second = second.reshape(block_count, n_cuts, 2, out_width, n_mode, a_count)
        real_two, imag_two = second[:, :, 0], second[:, :, 1]
        second_w = jnp.stack(
            [jnp.stack([real_two, -imag_two]), jnp.stack([imag_two, real_two])]
        )
        second_w = jnp.transpose(second_w, (0, 4, 2, 5, 3, 1, 6)).reshape(
            2 * out_width, block_count * n_mode * group
        )
        product = jnp.einsum(
            "brk,bnk->brn", stem_rows, first_w, preferred_element_type=jnp.float32
        ).astype(jnp.bfloat16)
        lhs = product.reshape(block_count, n_mode, t_local, q_local, group)
        lhs = jnp.transpose(lhs, (3, 2, 0, 1, 4)).reshape(
            q_local * t_local, block_count * n_mode * group
        )
        amplitude = jnp.einsum(
            "mk,nk->mn", lhs, second_w, preferred_element_type=jnp.float32
        )
    amplitude = amplitude.reshape(q_local, t_local, 2, out_width)
    return jnp.transpose(amplitude, (1, 0, 2, 3))


def on_device(stem_blocks, w1_table, w2_table, slice_ids, mode_perm):
    n_mode = lax.axis_size("mode")
    n_cuts = lax.axis_size("cuts")
    rows = stem_blocks.shape[1]
    width = stem_blocks.shape[3]
    mid = w1_table.shape[3]
    inner = w2_table.shape[2]
    out_width = w2_table.shape[3]
    block_count = slice_ids.shape[1]
    t_local = rows // n_mode
    a_count = inner // n_mode
    q_count = mid // a_count
    q_local = q_count // n_cuts
    me = lax.axis_index("cuts")
    sizes = (n_mode, t_local, n_cuts, a_count, q_local)

    pieces = stem_blocks[0].reshape(1, n_mode, t_local, 2 * width)
    payload = jnp.broadcast_to(pieces, (n_cuts, n_mode, t_local, 2 * width))
    payload = payload.reshape(n_cuts * n_mode, t_local, 2 * width)
    stem_rows = lax.all_to_all(payload, ("cuts", "mode"), 0, 0, tiled=True)
    stem_rows = stem_rows.reshape(block_count, n_mode * t_local, 2 * width)

    tie = (payload[0, 0, 0] * 0).astype(slice_ids.dtype)
    all_ids = gather_over_cuts(slice_ids[0] + tie, n_cuts)
    first_ids = all_ids[:, :, 0].T
    second_ids = all_ids[:, :, 1].T

    perm_grid = mode_perm.reshape(a_count, q_count)
    wanted = lax.dynamic_slice_in_dim(perm_grid, me * q_local, q_local, axis=1).reshape(-1)
    picker = (jnp.arange(mid, dtype=jnp.int32)[:, None] == wanted[None, :]).astype(w1_table.dtype)
    first_cols = jnp.einsum(
        "spkj,jn->spkn", w1_table, picker, preferred_element_type=jnp.float32
    ).astype(w1_table.dtype)
    real_part, imag_part = first_cols[:, 0], first_cols[:, 1]
    upper = jnp.concatenate([real_part, imag_part], axis=2)
    lower = jnp.concatenate([-imag_part, real_part], axis=2)
    first_all = jnp.concatenate([upper, lower], axis=1)

    if block_count * n_cuts <= 8:
        wanted_t = lax.dynamic_slice_in_dim(perm_grid, me * q_local, q_local, axis=1).T.reshape(-1)
        picker_t = (wanted_t[:, None] == jnp.arange(mid, dtype=jnp.int32)[None, :]).astype(w1_table.dtype)
        first_t = jnp.einsum(
            "nj,spkj->spnk", picker_t, w1_table, preferred_element_type=jnp.float32
        ).astype(w1_table.dtype)
        return stacked_part(stem_rows, first_t, w2_table, first_ids, second_ids, sizes)
    else:
        def one_block(index, running):
            stem_one = lax.dynamic_slice_in_dim(stem_rows, index, 1, axis=0)
            first_one = lax.dynamic_slice_in_dim(first_ids, index, 1, axis=0)
            second_one = lax.dynamic_slice_in_dim(second_ids, index, 1, axis=0)
            return running + blocks_part(
                stem_one, first_all, w2_table, first_one, second_one.reshape(-1), sizes
            )

        begin = jnp.zeros((t_local * q_local * 2, out_width), jnp.float32)
        amplitude = lax.fori_loop(0, block_count, one_block, begin)
    return amplitude.reshape(t_local, q_local, 2, out_width)


def solution(mesh):
    placed = (P("cuts", "mode", None, None), P(), P(), P("cuts", None, None), P())
    return jax.shard_map(
        on_device,
        mesh=mesh,
        in_specs=placed,
        out_specs=P("mode", "cuts", None, None),
        check_vma=False,
    )
```

```python
import jax
import jax.numpy as jnp
from jax import lax
from jax.experimental import pallas as pl
from jax.experimental.pallas import tpu as pltpu
from jax.sharding import PartitionSpec as P


def gather_over_cuts(own, n_cuts):
    pieces = [own]
    current = own
    ring = [(j, (j + 1) % n_cuts) for j in range(n_cuts)]
    for _ in range(1, n_cuts):
        current = lax.ppermute(current, "cuts", ring)
        pieces.append(current)
    stacked = jnp.stack(pieces)
    me = lax.axis_index("cuts")
    order = (me - jnp.arange(n_cuts, dtype=jnp.int32)) % n_cuts
    return jnp.take(stacked, order, axis=0)


def blocks_part(stem_rows, first_all, w2_table, first_ids, second_ids, sizes):
    n_mode, t_local, n_cuts, a_count, q_local = sizes
    chunk = stem_rows.shape[0]
    wide_in = stem_rows.shape[2]
    col_width = first_all.shape[2]
    slice_count, _, inner, out_width = w2_table.shape
    first_w = jnp.take(first_all, first_ids, axis=0)
    first_w = jnp.transpose(first_w, (0, 2, 1, 3)).reshape(
        chunk, wide_in, n_cuts * col_width
    )
    product = jnp.einsum(
        "bri,bio->bro", stem_rows, first_w, preferred_element_type=jnp.float32
    ).astype(jnp.bfloat16)
    split = product.reshape(chunk, n_mode, t_local, n_cuts, 2, a_count, q_local)
    real_p, imag_p = split[:, :, :, :, 0], split[:, :, :, :, 1]
    lhs = jnp.stack(
        [
            jnp.stack([real_p, -imag_p]),
            jnp.stack([imag_p, real_p]),
        ]
    )
    lhs = jnp.transpose(lhs, (4, 7, 0, 2, 5, 1, 3, 6)).reshape(
        t_local * q_local * 2, chunk * n_cuts * 2 * inner
    )
    second_w = jnp.take(
        w2_table.reshape(slice_count, 2 * inner, out_width), second_ids, axis=0
    ).reshape(chunk * n_cuts * 2 * inner, out_width)
    return jnp.dot(lhs, second_w, preferred_element_type=jnp.float32)


def regroup_kernel(stem_ref, weight_ref, second_hbm, out_ref, lhs_ref, second_ref, second_sem):
    block_count, rows, _ = stem_ref.shape
    q_local = weight_ref.shape[1] // 64
    t_local = 16
    n_mode = rows // t_local
    second_copy = pltpu.make_async_copy(second_hbm, second_ref, second_sem)
    second_copy.start()
    lane = lax.broadcasted_iota(jnp.int32, (t_local, 128), 1)
    low = lane < 64
    for b in range(block_count):
        product = lax.dot_general(
            stem_ref[b], weight_ref[b], (((1,), (1,)), ((), ())),
            preferred_element_type=jnp.float32,
        ).astype(jnp.bfloat16)
        for pair in range(n_mode // 2):
            upper = product[(2 * pair) * t_local:(2 * pair + 1) * t_local]
            lower = product[(2 * pair + 1) * t_local:(2 * pair + 2) * t_local]
            col = (b * n_mode // 2 + pair) * 128
            for qp in range(q_local // 2):
                first = upper[:, qp * 128:(qp + 1) * 128]
                second = lower[:, qp * 128:(qp + 1) * 128]
                even = jnp.where(low, first, pltpu.roll(second, 64, 1))
                odd = jnp.where(low, pltpu.roll(first, 64, 1), second)
                lhs_ref[(2 * qp) * t_local:(2 * qp + 1) * t_local, col:col + 128] = even
                lhs_ref[(2 * qp + 1) * t_local:(2 * qp + 2) * t_local, col:col + 128] = odd
    second_copy.wait()
    lhs = lhs_ref[...]
    for part in range(second_ref.shape[0]):
        result = jnp.dot(lhs, second_ref[part], preferred_element_type=jnp.float32)
        for q in range(q_local):
            out_ref[:, q, part, :] = result[q * t_local:(q + 1) * t_local]


def regroup(stem_rows, first_w, second_w, q_local, t_local):
    block_count, rows, _ = stem_rows.shape
    n_mode = rows // t_local
    lhs_shape = (q_local * t_local, block_count * n_mode * 64)
    out_shape = jax.ShapeDtypeStruct(
        (t_local, q_local, second_w.shape[0], second_w.shape[2]), jnp.float32
    )
    flops = 2 * block_count * rows * first_w.shape[1] * first_w.shape[2]
    flops += 2 * lhs_shape[0] * lhs_shape[1] * second_w.shape[0] * second_w.shape[2]
    return pl.pallas_call(
        regroup_kernel,
        out_shape=out_shape,
        in_specs=[pl.BlockSpec(memory_space=pltpu.VMEM)] * 2 + [pl.BlockSpec(memory_space=pl.ANY)],
        out_specs=pl.BlockSpec(memory_space=pltpu.VMEM),
        scratch_shapes=[
            pltpu.VMEM(lhs_shape, jnp.bfloat16),
            pltpu.VMEM(second_w.shape, second_w.dtype),
            pltpu.SemaphoreType.DMA(()),
        ],
        cost_estimate=pl.CostEstimate(
            flops=flops,
            transcendentals=0,
            bytes_accessed=2 * (stem_rows.size + first_w.size + second_w.size)
            + 4 * lhs_shape[0] * second_w.shape[0] * second_w.shape[2],
        ),
    )(stem_rows, first_w, second_w)

def stacked_part(stem_rows, first_t, w2_table, first_ids, second_ids, sizes):
    n_mode, t_local, n_cuts, a_count, q_local = sizes
    block_count = stem_rows.shape[0]
    width = first_t.shape[3]
    _, _, inner, out_width = w2_table.shape
    group = n_cuts * 2 * a_count
    picked = jnp.take(first_t, first_ids.reshape(-1), axis=0)
    picked = picked.reshape(block_count, n_cuts, 2, q_local, a_count, width)
    real_part, imag_part = picked[:, :, 0], picked[:, :, 1]
    first_w = jnp.stack(
        [jnp.stack([real_part, imag_part]), jnp.stack([-imag_part, real_part])]
    )
    first_w = jnp.transpose(first_w, (2, 4, 3, 1, 5, 0, 6)).reshape(
        block_count, q_local * group, 2 * width
    )
    if group == 64 and t_local == 16 and n_mode % 2 == 0 and q_local % 2 == 0:
        second = jnp.take(w2_table, second_ids.reshape(-1), axis=0)
        second = second.reshape(block_count, n_cuts, 2, n_mode, a_count, out_width)
        real_two, imag_two = second[:, :, 0], second[:, :, 1]
        second_w = jnp.stack(
            [jnp.stack([real_two, imag_two]), jnp.stack([-imag_two, real_two])]
        )
        second_w = jnp.transpose(second_w, (1, 2, 4, 3, 0, 5, 6)).reshape(
            2, block_count * n_mode * group, out_width
        )
        return regroup(stem_rows, first_w, second_w, q_local, t_local)
    else:
        second = jnp.take(w2_table, second_ids.reshape(-1), axis=0)
        second = jnp.swapaxes(second, 2, 3)
        second = second.reshape(block_count, n_cuts, 2, out_width, n_mode, a_count)
        real_two, imag_two = second[:, :, 0], second[:, :, 1]
        second_w = jnp.stack(
            [jnp.stack([real_two, -imag_two]), jnp.stack([imag_two, real_two])]
        )
        second_w = jnp.transpose(second_w, (0, 4, 2, 5, 3, 1, 6)).reshape(
            2 * out_width, block_count * n_mode * group
        )
        product = jnp.einsum(
            "brk,bnk->brn", stem_rows, first_w, preferred_element_type=jnp.float32
        ).astype(jnp.bfloat16)
        lhs = product.reshape(block_count, n_mode, t_local, q_local, group)
        lhs = jnp.transpose(lhs, (3, 2, 0, 1, 4)).reshape(
            q_local * t_local, block_count * n_mode * group
        )
        amplitude = jnp.einsum(
            "mk,nk->mn", lhs, second_w, preferred_element_type=jnp.float32
        )
    amplitude = amplitude.reshape(q_local, t_local, 2, out_width)
    return jnp.transpose(amplitude, (1, 0, 2, 3))


def on_device(stem_blocks, w1_table, w2_table, slice_ids, mode_perm):
    n_mode = lax.axis_size("mode")
    n_cuts = lax.axis_size("cuts")
    rows = stem_blocks.shape[1]
    width = stem_blocks.shape[3]
    mid = w1_table.shape[3]
    inner = w2_table.shape[2]
    out_width = w2_table.shape[3]
    block_count = slice_ids.shape[1]
    t_local = rows // n_mode
    a_count = inner // n_mode
    q_count = mid // a_count
    q_local = q_count // n_cuts
    me = lax.axis_index("cuts")
    sizes = (n_mode, t_local, n_cuts, a_count, q_local)

    pieces = stem_blocks[0].reshape(1, n_mode, t_local, 2 * width)
    payload = jnp.broadcast_to(pieces, (n_cuts, n_mode, t_local, 2 * width))
    payload = payload.reshape(n_cuts * n_mode, t_local, 2 * width)
    stem_rows = lax.all_to_all(payload, ("cuts", "mode"), 0, 0, tiled=True)
    stem_rows = stem_rows.reshape(block_count, n_mode * t_local, 2 * width)

    all_ids = gather_over_cuts(slice_ids[0], n_cuts)
    first_ids = all_ids[:, :, 0].T
    second_ids = all_ids[:, :, 1].T

    perm_grid = mode_perm.reshape(a_count, q_count)
    wanted = lax.dynamic_slice_in_dim(perm_grid, me * q_local, q_local, axis=1).reshape(-1)
    picker = (jnp.arange(mid, dtype=jnp.int32)[:, None] == wanted[None, :]).astype(w1_table.dtype)
    first_cols = jnp.einsum(
        "spkj,jn->spkn", w1_table, picker, preferred_element_type=jnp.float32
    ).astype(w1_table.dtype)
    real_part, imag_part = first_cols[:, 0], first_cols[:, 1]
    upper = jnp.concatenate([real_part, imag_part], axis=2)
    lower = jnp.concatenate([-imag_part, real_part], axis=2)
    first_all = jnp.concatenate([upper, lower], axis=1)

    if block_count * n_cuts <= 8:
        wanted_t = lax.dynamic_slice_in_dim(perm_grid, me * q_local, q_local, axis=1).T.reshape(-1)
        picker_t = (wanted_t[:, None] == jnp.arange(mid, dtype=jnp.int32)[None, :]).astype(w1_table.dtype)
        first_t = jnp.einsum(
            "nj,spkj->spnk", picker_t, w1_table, preferred_element_type=jnp.float32
        ).astype(w1_table.dtype)
        return stacked_part(stem_rows, first_t, w2_table, first_ids, second_ids, sizes)
    else:
        def one_block(index, running):
            stem_one = lax.dynamic_slice_in_dim(stem_rows, index, 1, axis=0)
            first_one = lax.dynamic_slice_in_dim(first_ids, index, 1, axis=0)
            second_one = lax.dynamic_slice_in_dim(second_ids, index, 1, axis=0)
            return running + blocks_part(
                stem_one, first_all, w2_table, first_one, second_one.reshape(-1), sizes
            )

        begin = jnp.zeros((t_local * q_local * 2, out_width), jnp.float32)
        amplitude = lax.fori_loop(0, block_count, one_block, begin)
    return amplitude.reshape(t_local, q_local, 2, out_width)


def solution(mesh):
    placed = (P("cuts", "mode", None, None), P(), P(), P("cuts", None, None), P())
    return jax.shard_map(
        on_device,
        mesh=mesh,
        in_specs=placed,
        out_specs=P("mode", "cuts", None, None),
        check_vma=False,
    )
```

```python
import jax
import jax.numpy as jnp
from jax import lax
from jax.experimental import pallas as pl
from jax.experimental.pallas import tpu as pltpu
from jax.sharding import PartitionSpec as P


def gather_over_cuts(own, n_cuts):
    pieces = [own]
    current = own
    ring = [(j, (j + 1) % n_cuts) for j in range(n_cuts)]
    for _ in range(1, n_cuts):
        current = lax.ppermute(current, "cuts", ring)
        pieces.append(current)
    stacked = jnp.stack(pieces)
    me = lax.axis_index("cuts")
    order = (me - jnp.arange(n_cuts, dtype=jnp.int32)) % n_cuts
    return jnp.take(stacked, order, axis=0)


def blocks_part(stem_rows, first_all, w2_table, first_ids, second_ids, sizes):
    n_mode, t_local, n_cuts, a_count, q_local = sizes
    chunk = stem_rows.shape[0]
    wide_in = stem_rows.shape[2]
    col_width = first_all.shape[2]
    slice_count, _, inner, out_width = w2_table.shape
    first_w = jnp.take(first_all, first_ids, axis=0)
    first_w = jnp.transpose(first_w, (0, 2, 1, 3)).reshape(
        chunk, wide_in, n_cuts * col_width
    )
    product = jnp.einsum(
        "bri,bio->bro", stem_rows, first_w, preferred_element_type=jnp.float32
    ).astype(jnp.bfloat16)
    split = product.reshape(chunk, n_mode, t_local, n_cuts, 2, a_count, q_local)
    real_p, imag_p = split[:, :, :, :, 0], split[:, :, :, :, 1]
    lhs = jnp.stack(
        [
            jnp.stack([real_p, -imag_p]),
            jnp.stack([imag_p, real_p]),
        ]
    )
    lhs = jnp.transpose(lhs, (4, 7, 0, 2, 5, 1, 3, 6)).reshape(
        t_local * q_local * 2, chunk * n_cuts * 2 * inner
    )
    second_w = jnp.take(
        w2_table.reshape(slice_count, 2 * inner, out_width), second_ids, axis=0
    ).reshape(chunk * n_cuts * 2 * inner, out_width)
    return jnp.dot(lhs, second_w, preferred_element_type=jnp.float32)


def regroup_kernel(stem_ref, weight_ref, second_ref, out_ref, lhs_ref):
    block_count, rows, _ = stem_ref.shape
    q_local = weight_ref.shape[2] // 64
    t_local = 16
    n_mode = rows // t_local
    lane = lax.broadcasted_iota(jnp.int32, (t_local, 128), 1)
    low = lane < 64
    for b in range(block_count):
        product = jnp.dot(
            stem_ref[b], weight_ref[b], preferred_element_type=jnp.float32
        ).astype(jnp.bfloat16)
        for pair in range(n_mode // 2):
            upper = product[(2 * pair) * t_local:(2 * pair + 1) * t_local]
            lower = product[(2 * pair + 1) * t_local:(2 * pair + 2) * t_local]
            col = (b * n_mode // 2 + pair) * 128
            for qp in range(q_local // 2):
                first = upper[:, qp * 128:(qp + 1) * 128]
                second = lower[:, qp * 128:(qp + 1) * 128]
                even = jnp.where(low, first, pltpu.roll(second, 64, 1))
                odd = jnp.where(low, pltpu.roll(first, 64, 1), second)
                lhs_ref[(2 * qp) * t_local:(2 * qp + 1) * t_local, col:col + 128] = even
                lhs_ref[(2 * qp + 1) * t_local:(2 * qp + 2) * t_local, col:col + 128] = odd
    lhs = lhs_ref[...]
    for part in range(second_ref.shape[0]):
        result = jnp.dot(lhs, second_ref[part], preferred_element_type=jnp.float32)
        for q in range(q_local):
            out_ref[:, q, part, :] = result[q * t_local:(q + 1) * t_local]


def regroup(stem_rows, first_w, second_w, q_local, t_local):
    block_count, rows, _ = stem_rows.shape
    n_mode = rows // t_local
    lhs_shape = (q_local * t_local, block_count * n_mode * 64)
    out_shape = jax.ShapeDtypeStruct(
        (t_local, q_local, second_w.shape[0], second_w.shape[2]), jnp.float32
    )
    flops = 2 * block_count * rows * first_w.shape[1] * first_w.shape[2]
    flops += 2 * lhs_shape[0] * lhs_shape[1] * second_w.shape[0] * second_w.shape[2]
    return pl.pallas_call(
        regroup_kernel,
        out_shape=out_shape,
        in_specs=[pl.BlockSpec(memory_space=pltpu.VMEM)] * 3,
        out_specs=pl.BlockSpec(memory_space=pltpu.VMEM),
        scratch_shapes=[pltpu.VMEM(lhs_shape, jnp.bfloat16)],
        cost_estimate=pl.CostEstimate(
            flops=flops,
            transcendentals=0,
            bytes_accessed=2 * (stem_rows.size + first_w.size + second_w.size)
            + 4 * lhs_shape[0] * second_w.shape[0] * second_w.shape[2],
        ),
    )(stem_rows, first_w, second_w)

def stacked_part(stem_rows, first_t, w2_table, first_ids, second_ids, sizes):
    n_mode, t_local, n_cuts, a_count, q_local = sizes
    block_count = stem_rows.shape[0]
    width = first_t.shape[3]
    _, _, inner, out_width = w2_table.shape
    group = n_cuts * 2 * a_count
    picked = jnp.take(first_t, first_ids.reshape(-1), axis=0)
    picked = picked.reshape(block_count, n_cuts, 2, q_local, a_count, width)
    real_part, imag_part = picked[:, :, 0], picked[:, :, 1]
    first_w = jnp.stack(
        [jnp.stack([real_part, imag_part]), jnp.stack([-imag_part, real_part])]
    )
    first_w = jnp.transpose(first_w, (2, 4, 3, 1, 5, 0, 6)).reshape(
        block_count, q_local * group, 2 * width
    )
    if group == 64 and t_local == 16 and n_mode % 2 == 0 and q_local % 2 == 0:
        second = jnp.take(w2_table, second_ids.reshape(-1), axis=0)
        second = second.reshape(block_count, n_cuts, 2, n_mode, a_count, out_width)
        real_two, imag_two = second[:, :, 0], second[:, :, 1]
        second_w = jnp.stack(
            [jnp.stack([real_two, imag_two]), jnp.stack([-imag_two, real_two])]
        )
        second_w = jnp.transpose(second_w, (1, 2, 4, 3, 0, 5, 6)).reshape(
            2, block_count * n_mode * group, out_width
        )
        return regroup(stem_rows, jnp.swapaxes(first_w, 1, 2), second_w, q_local, t_local)
    else:
        second = jnp.take(w2_table, second_ids.reshape(-1), axis=0)
        second = jnp.swapaxes(second, 2, 3)
        second = second.reshape(block_count, n_cuts, 2, out_width, n_mode, a_count)
        real_two, imag_two = second[:, :, 0], second[:, :, 1]
        second_w = jnp.stack(
            [jnp.stack([real_two, -imag_two]), jnp.stack([imag_two, real_two])]
        )
        second_w = jnp.transpose(second_w, (0, 4, 2, 5, 3, 1, 6)).reshape(
            2 * out_width, block_count * n_mode * group
        )
        product = jnp.einsum(
            "brk,bnk->brn", stem_rows, first_w, preferred_element_type=jnp.float32
        ).astype(jnp.bfloat16)
        lhs = product.reshape(block_count, n_mode, t_local, q_local, group)
        lhs = jnp.transpose(lhs, (3, 2, 0, 1, 4)).reshape(
            q_local * t_local, block_count * n_mode * group
        )
        amplitude = jnp.einsum(
            "mk,nk->mn", lhs, second_w, preferred_element_type=jnp.float32
        )
    amplitude = amplitude.reshape(q_local, t_local, 2, out_width)
    return jnp.transpose(amplitude, (1, 0, 2, 3))


def on_device(stem_blocks, w1_table, w2_table, slice_ids, mode_perm):
    n_mode = lax.axis_size("mode")
    n_cuts = lax.axis_size("cuts")
    rows = stem_blocks.shape[1]
    width = stem_blocks.shape[3]
    mid = w1_table.shape[3]
    inner = w2_table.shape[2]
    out_width = w2_table.shape[3]
    block_count = slice_ids.shape[1]
    t_local = rows // n_mode
    a_count = inner // n_mode
    q_count = mid // a_count
    q_local = q_count // n_cuts
    me = lax.axis_index("cuts")
    sizes = (n_mode, t_local, n_cuts, a_count, q_local)

    pieces = stem_blocks[0].reshape(1, n_mode, t_local, 2 * width)
    payload = jnp.broadcast_to(pieces, (n_cuts, n_mode, t_local, 2 * width))
    payload = payload.reshape(n_cuts * n_mode, t_local, 2 * width)
    stem_rows = lax.all_to_all(payload, ("cuts", "mode"), 0, 0, tiled=True)
    stem_rows = stem_rows.reshape(block_count, n_mode * t_local, 2 * width)

    all_ids = gather_over_cuts(slice_ids[0], n_cuts)
    first_ids = all_ids[:, :, 0].T
    second_ids = all_ids[:, :, 1].T

    perm_grid = mode_perm.reshape(a_count, q_count)
    wanted = lax.dynamic_slice_in_dim(perm_grid, me * q_local, q_local, axis=1).reshape(-1)
    picker = (jnp.arange(mid, dtype=jnp.int32)[:, None] == wanted[None, :]).astype(w1_table.dtype)
    first_cols = jnp.einsum(
        "spkj,jn->spkn", w1_table, picker, preferred_element_type=jnp.float32
    ).astype(w1_table.dtype)
    real_part, imag_part = first_cols[:, 0], first_cols[:, 1]
    upper = jnp.concatenate([real_part, imag_part], axis=2)
    lower = jnp.concatenate([-imag_part, real_part], axis=2)
    first_all = jnp.concatenate([upper, lower], axis=1)

    if block_count * n_cuts <= 8:
        wanted_t = lax.dynamic_slice_in_dim(perm_grid, me * q_local, q_local, axis=1).T.reshape(-1)
        picker_t = (wanted_t[:, None] == jnp.arange(mid, dtype=jnp.int32)[None, :]).astype(w1_table.dtype)
        first_t = jnp.einsum(
            "nj,spkj->spnk", picker_t, w1_table, preferred_element_type=jnp.float32
        ).astype(w1_table.dtype)
        return stacked_part(stem_rows, first_t, w2_table, first_ids, second_ids, sizes)
    else:
        def one_block(index, running):
            stem_one = lax.dynamic_slice_in_dim(stem_rows, index, 1, axis=0)
            first_one = lax.dynamic_slice_in_dim(first_ids, index, 1, axis=0)
            second_one = lax.dynamic_slice_in_dim(second_ids, index, 1, axis=0)
            return running + blocks_part(
                stem_one, first_all, w2_table, first_one, second_one.reshape(-1), sizes
            )

        begin = jnp.zeros((t_local * q_local * 2, out_width), jnp.float32)
        amplitude = lax.fori_loop(0, block_count, one_block, begin)
    return amplitude.reshape(t_local, q_local, 2, out_width)


def solution(mesh):
    placed = (P("cuts", "mode", None, None), P(), P(), P("cuts", None, None), P())
    return jax.shard_map(
        on_device,
        mesh=mesh,
        in_specs=placed,
        out_specs=P("mode", "cuts", None, None),
        check_vma=False,
    )
```

```python
import jax
import jax.numpy as jnp
from jax import lax
from jax.experimental import pallas as pl
from jax.experimental.pallas import tpu as pltpu
from jax.sharding import PartitionSpec as P


def gather_over_cuts(own, n_cuts):
    pieces = [own]
    current = own
    ring = [(j, (j + 1) % n_cuts) for j in range(n_cuts)]
    for _ in range(1, n_cuts):
        current = lax.ppermute(current, "cuts", ring)
        pieces.append(current)
    stacked = jnp.stack(pieces)
    me = lax.axis_index("cuts")
    order = (me - jnp.arange(n_cuts, dtype=jnp.int32)) % n_cuts
    return jnp.take(stacked, order, axis=0)


def blocks_part(stem_rows, first_all, w2_table, first_ids, second_ids, sizes):
    n_mode, t_local, n_cuts, a_count, q_local = sizes
    chunk = stem_rows.shape[0]
    wide_in = stem_rows.shape[2]
    col_width = first_all.shape[2]
    slice_count, _, inner, out_width = w2_table.shape
    first_w = jnp.take(first_all, first_ids, axis=0)
    first_w = jnp.transpose(first_w, (0, 2, 1, 3)).reshape(
        chunk, wide_in, n_cuts * col_width
    )
    product = jnp.einsum(
        "bri,bio->bro", stem_rows, first_w, preferred_element_type=jnp.float32
    ).astype(jnp.bfloat16)
    split = product.reshape(chunk, n_mode, t_local, n_cuts, 2, a_count, q_local)
    real_p, imag_p = split[:, :, :, :, 0], split[:, :, :, :, 1]
    lhs = jnp.stack(
        [
            jnp.stack([real_p, -imag_p]),
            jnp.stack([imag_p, real_p]),
        ]
    )
    lhs = jnp.transpose(lhs, (4, 7, 0, 2, 5, 1, 3, 6)).reshape(
        t_local * q_local * 2, chunk * n_cuts * 2 * inner
    )
    second_w = jnp.take(
        w2_table.reshape(slice_count, 2 * inner, out_width), second_ids, axis=0
    ).reshape(chunk * n_cuts * 2 * inner, out_width)
    return jnp.dot(lhs, second_w, preferred_element_type=jnp.float32)


def regroup_kernel(stem_ref, weight_ref, second_ref, out_ref, lhs_ref):
    block_count, rows, _ = stem_ref.shape
    q_local = weight_ref.shape[2] // 64
    t_local = 16
    n_mode = rows // t_local
    lane = lax.broadcasted_iota(jnp.int32, (t_local, 128), 1)
    low = lane < 64
    for b in range(block_count):
        product = jnp.dot(
            stem_ref[b], weight_ref[b], preferred_element_type=jnp.float32
        ).astype(jnp.bfloat16)
        for pair in range(n_mode // 2):
            upper = product[(2 * pair) * t_local:(2 * pair + 1) * t_local]
            lower = product[(2 * pair + 1) * t_local:(2 * pair + 2) * t_local]
            col = (b * n_mode // 2 + pair) * 128
            for qp in range(q_local // 2):
                first = upper[:, qp * 128:(qp + 1) * 128]
                second = lower[:, qp * 128:(qp + 1) * 128]
                even = jnp.where(low, first, pltpu.roll(second, 64, 1))
                odd = jnp.where(low, pltpu.roll(first, 64, 1), second)
                lhs_ref[(2 * qp) * t_local:(2 * qp + 1) * t_local, col:col + 128] = even
                lhs_ref[(2 * qp + 1) * t_local:(2 * qp + 2) * t_local, col:col + 128] = odd
    lhs = lhs_ref[...]
    for part in range(second_ref.shape[0]):
        result = jnp.dot(lhs, second_ref[part], preferred_element_type=jnp.float32)
        for q in range(q_local):
            out_ref[:, q, part, :] = result[q * t_local:(q + 1) * t_local]


def regroup(stem_rows, first_w, second_w, q_local, t_local):
    block_count, rows, _ = stem_rows.shape
    n_mode = rows // t_local
    lhs_shape = (q_local * t_local, block_count * n_mode * 64)
    out_shape = jax.ShapeDtypeStruct(
        (t_local, q_local, second_w.shape[0], second_w.shape[2]), jnp.float32
    )
    flops = 2 * block_count * rows * first_w.shape[1] * first_w.shape[2]
    flops += 2 * lhs_shape[0] * lhs_shape[1] * second_w.shape[0] * second_w.shape[2]
    return pl.pallas_call(
        regroup_kernel,
        out_shape=out_shape,
        in_specs=[pl.BlockSpec(memory_space=pltpu.VMEM)] * 3,
        out_specs=pl.BlockSpec(memory_space=pltpu.VMEM),
        scratch_shapes=[pltpu.VMEM(lhs_shape, jnp.bfloat16)],
        compiler_params=pltpu.CompilerParams(vmem_limit_bytes=16 * 1024 * 1024),
        cost_estimate=pl.CostEstimate(
            flops=flops,
            transcendentals=0,
            bytes_accessed=2 * (stem_rows.size + first_w.size + second_w.size)
            + 4 * lhs_shape[0] * second_w.shape[0] * second_w.shape[2],
        ),
    )(stem_rows, first_w, second_w)

def stacked_part(stem_rows, first_t, w2_table, first_ids, second_ids, sizes):
    n_mode, t_local, n_cuts, a_count, q_local = sizes
    block_count = stem_rows.shape[0]
    width = first_t.shape[3]
    _, _, inner, out_width = w2_table.shape
    group = n_cuts * 2 * a_count
    picked = jnp.take(first_t, first_ids.reshape(-1), axis=0)
    picked = picked.reshape(block_count, n_cuts, 2, q_local, a_count, width)
    real_part, imag_part = picked[:, :, 0], picked[:, :, 1]
    first_w = jnp.stack(
        [jnp.stack([real_part, imag_part]), jnp.stack([-imag_part, real_part])]
    )
    first_w = jnp.transpose(first_w, (2, 4, 3, 1, 5, 0, 6)).reshape(
        block_count, q_local * group, 2 * width
    )
    if group == 64 and t_local == 16 and n_mode % 2 == 0 and q_local % 2 == 0:
        second = jnp.take(w2_table, second_ids.reshape(-1), axis=0)
        second = second.reshape(block_count, n_cuts, 2, n_mode, a_count, out_width)
        real_two, imag_two = second[:, :, 0], second[:, :, 1]
        second_w = jnp.stack(
            [jnp.stack([real_two, imag_two]), jnp.stack([-imag_two, real_two])]
        )
        second_w = jnp.transpose(second_w, (1, 2, 4, 3, 0, 5, 6)).reshape(
            2, block_count * n_mode * group, out_width
        )
        return regroup(stem_rows, jnp.swapaxes(first_w, 1, 2), second_w, q_local, t_local)
    else:
        second = jnp.take(w2_table, second_ids.reshape(-1), axis=0)
        second = jnp.swapaxes(second, 2, 3)
        second = second.reshape(block_count, n_cuts, 2, out_width, n_mode, a_count)
        real_two, imag_two = second[:, :, 0], second[:, :, 1]
        second_w = jnp.stack(
            [jnp.stack([real_two, -imag_two]), jnp.stack([imag_two, real_two])]
        )
        second_w = jnp.transpose(second_w, (0, 4, 2, 5, 3, 1, 6)).reshape(
            2 * out_width, block_count * n_mode * group
        )
        product = jnp.einsum(
            "brk,bnk->brn", stem_rows, first_w, preferred_element_type=jnp.float32
        ).astype(jnp.bfloat16)
        lhs = product.reshape(block_count, n_mode, t_local, q_local, group)
        lhs = jnp.transpose(lhs, (3, 2, 0, 1, 4)).reshape(
            q_local * t_local, block_count * n_mode * group
        )
        amplitude = jnp.einsum(
            "mk,nk->mn", lhs, second_w, preferred_element_type=jnp.float32
        )
    amplitude = amplitude.reshape(q_local, t_local, 2, out_width)
    return jnp.transpose(amplitude, (1, 0, 2, 3))


def on_device(stem_blocks, w1_table, w2_table, slice_ids, mode_perm):
    n_mode = lax.axis_size("mode")
    n_cuts = lax.axis_size("cuts")
    rows = stem_blocks.shape[1]
    width = stem_blocks.shape[3]
    mid = w1_table.shape[3]
    inner = w2_table.shape[2]
    out_width = w2_table.shape[3]
    block_count = slice_ids.shape[1]
    t_local = rows // n_mode
    a_count = inner // n_mode
    q_count = mid // a_count
    q_local = q_count // n_cuts
    me = lax.axis_index("cuts")
    sizes = (n_mode, t_local, n_cuts, a_count, q_local)

    pieces = stem_blocks[0].reshape(1, n_mode, t_local, 2 * width)
    payload = jnp.broadcast_to(pieces, (n_cuts, n_mode, t_local, 2 * width))
    payload = payload.reshape(n_cuts * n_mode, t_local, 2 * width)
    stem_rows = lax.all_to_all(payload, ("cuts", "mode"), 0, 0, tiled=True)
    stem_rows = stem_rows.reshape(block_count, n_mode * t_local, 2 * width)

    all_ids = gather_over_cuts(slice_ids[0], n_cuts)
    first_ids = all_ids[:, :, 0].T
    second_ids = all_ids[:, :, 1].T

    perm_grid = mode_perm.reshape(a_count, q_count)
    wanted = lax.dynamic_slice_in_dim(perm_grid, me * q_local, q_local, axis=1).reshape(-1)
    picker = (jnp.arange(mid, dtype=jnp.int32)[:, None] == wanted[None, :]).astype(w1_table.dtype)
    first_cols = jnp.einsum(
        "spkj,jn->spkn", w1_table, picker, preferred_element_type=jnp.float32
    ).astype(w1_table.dtype)
    real_part, imag_part = first_cols[:, 0], first_cols[:, 1]
    upper = jnp.concatenate([real_part, imag_part], axis=2)
    lower = jnp.concatenate([-imag_part, real_part], axis=2)
    first_all = jnp.concatenate([upper, lower], axis=1)

    if block_count * n_cuts <= 8:
        wanted_t = lax.dynamic_slice_in_dim(perm_grid, me * q_local, q_local, axis=1).T.reshape(-1)
        picker_t = (wanted_t[:, None] == jnp.arange(mid, dtype=jnp.int32)[None, :]).astype(w1_table.dtype)
        first_t = jnp.einsum(
            "nj,spkj->spnk", picker_t, w1_table, preferred_element_type=jnp.float32
        ).astype(w1_table.dtype)
        return stacked_part(stem_rows, first_t, w2_table, first_ids, second_ids, sizes)
    else:
        def one_block(index, running):
            stem_one = lax.dynamic_slice_in_dim(stem_rows, index, 1, axis=0)
            first_one = lax.dynamic_slice_in_dim(first_ids, index, 1, axis=0)
            second_one = lax.dynamic_slice_in_dim(second_ids, index, 1, axis=0)
            return running + blocks_part(
                stem_one, first_all, w2_table, first_one, second_one.reshape(-1), sizes
            )

        begin = jnp.zeros((t_local * q_local * 2, out_width), jnp.float32)
        amplitude = lax.fori_loop(0, block_count, one_block, begin)
    return amplitude.reshape(t_local, q_local, 2, out_width)


def solution(mesh):
    placed = (P("cuts", "mode", None, None), P(), P(), P("cuts", None, None), P())
    return jax.shard_map(
        on_device,
        mesh=mesh,
        in_specs=placed,
        out_specs=P("mode", "cuts", None, None),
        check_vma=False,
    )
```

```python
import jax
import jax.numpy as jnp
from jax import lax
from jax.experimental import pallas as pl
from jax.experimental.pallas import tpu as pltpu
from jax.sharding import PartitionSpec as P


def gather_over_cuts(own, n_cuts):
    pieces = [own]
    current = own
    ring = [(j, (j + 1) % n_cuts) for j in range(n_cuts)]
    for _ in range(1, n_cuts):
        current = lax.ppermute(current, "cuts", ring)
        pieces.append(current)
    stacked = jnp.stack(pieces)
    me = lax.axis_index("cuts")
    order = (me - jnp.arange(n_cuts, dtype=jnp.int32)) % n_cuts
    return jnp.take(stacked, order, axis=0)


def blocks_part(stem_rows, first_all, w2_table, first_ids, second_ids, sizes):
    n_mode, t_local, n_cuts, a_count, q_local = sizes
    chunk = stem_rows.shape[0]
    wide_in = stem_rows.shape[2]
    col_width = first_all.shape[2]
    slice_count, _, inner, out_width = w2_table.shape
    first_w = jnp.take(first_all, first_ids, axis=0)
    first_w = jnp.transpose(first_w, (0, 2, 1, 3)).reshape(
        chunk, wide_in, n_cuts * col_width
    )
    product = jnp.einsum(
        "bri,bio->bro", stem_rows, first_w, preferred_element_type=jnp.float32
    ).astype(jnp.bfloat16)
    split = product.reshape(chunk, n_mode, t_local, n_cuts, 2, a_count, q_local)
    real_p, imag_p = split[:, :, :, :, 0], split[:, :, :, :, 1]
    lhs = jnp.stack(
        [
            jnp.stack([real_p, -imag_p]),
            jnp.stack([imag_p, real_p]),
        ]
    )
    lhs = jnp.transpose(lhs, (4, 7, 0, 2, 5, 1, 3, 6)).reshape(
        t_local * q_local * 2, chunk * n_cuts * 2 * inner
    )
    second_w = jnp.take(
        w2_table.reshape(slice_count, 2 * inner, out_width), second_ids, axis=0
    ).reshape(chunk * n_cuts * 2 * inner, out_width)
    return jnp.dot(lhs, second_w, preferred_element_type=jnp.float32)


def regroup_kernel(stem_ref, weight_ref, second_ref, out_ref, lhs_ref):
    pieces, t_local, _, width = stem_ref.shape
    block_count = weight_ref.shape[0]
    q_local = weight_ref.shape[2] // 64
    n_mode = pieces // block_count
    rows = n_mode * t_local
    lane = lax.broadcasted_iota(jnp.int32, (t_local, 128), 1)
    low = lane < 64
    for b in range(block_count):
        own = stem_ref[b * n_mode:(b + 1) * n_mode]
        product = jnp.dot(
            own[:, :, 0, :].reshape(rows, width), weight_ref[b, :width],
            preferred_element_type=jnp.float32,
        )
        product = product + jnp.dot(
            own[:, :, 1, :].reshape(rows, width), weight_ref[b, width:],
            preferred_element_type=jnp.float32,
        )
        product = product.astype(jnp.bfloat16)
        for pair in range(n_mode // 2):
            upper = product[(2 * pair) * t_local:(2 * pair + 1) * t_local]
            lower = product[(2 * pair + 1) * t_local:(2 * pair + 2) * t_local]
            col = (b * n_mode // 2 + pair) * 128
            for qp in range(q_local // 2):
                first = upper[:, qp * 128:(qp + 1) * 128]
                second = lower[:, qp * 128:(qp + 1) * 128]
                even = jnp.where(low, first, pltpu.roll(second, 64, 1))
                odd = jnp.where(low, pltpu.roll(first, 64, 1), second)
                lhs_ref[(2 * qp) * t_local:(2 * qp + 1) * t_local, col:col + 128] = even
                lhs_ref[(2 * qp + 1) * t_local:(2 * qp + 2) * t_local, col:col + 128] = odd
    lhs = lhs_ref[...]
    for part in range(second_ref.shape[0]):
        result = jnp.dot(lhs, second_ref[part], preferred_element_type=jnp.float32)
        for q in range(q_local):
            out_ref[:, q, part, :] = result[q * t_local:(q + 1) * t_local]


def regroup(stem_rows, first_w, second_w, q_local, t_local):
    block_count = first_w.shape[0]
    n_mode = stem_rows.shape[0] // block_count
    rows = n_mode * t_local
    lhs_shape = (q_local * t_local, block_count * n_mode * 64)
    out_shape = jax.ShapeDtypeStruct(
        (t_local, q_local, second_w.shape[0], second_w.shape[2]), jnp.float32
    )
    flops = 2 * block_count * rows * first_w.shape[1] * first_w.shape[2]
    flops += 2 * lhs_shape[0] * lhs_shape[1] * second_w.shape[0] * second_w.shape[2]
    return pl.pallas_call(
        regroup_kernel,
        out_shape=out_shape,
        in_specs=[pl.BlockSpec(memory_space=pltpu.VMEM)] * 3,
        out_specs=pl.BlockSpec(memory_space=pltpu.VMEM),
        scratch_shapes=[pltpu.VMEM(lhs_shape, jnp.bfloat16)],
        cost_estimate=pl.CostEstimate(
            flops=flops,
            transcendentals=0,
            bytes_accessed=2 * (stem_rows.size + first_w.size + second_w.size)
            + 4 * lhs_shape[0] * second_w.shape[0] * second_w.shape[2],
        ),
    )(stem_rows, first_w, second_w)

def stacked_part(stem_rows, first_t, w2_table, first_ids, second_ids, sizes, stem_parts):
    n_mode, t_local, n_cuts, a_count, q_local = sizes
    block_count = stem_rows.shape[0]
    width = first_t.shape[3]
    _, _, inner, out_width = w2_table.shape
    group = n_cuts * 2 * a_count
    picked = jnp.take(first_t, first_ids.reshape(-1), axis=0)
    picked = picked.reshape(block_count, n_cuts, 2, q_local, a_count, width)
    real_part, imag_part = picked[:, :, 0], picked[:, :, 1]
    first_w = jnp.stack(
        [jnp.stack([real_part, imag_part]), jnp.stack([-imag_part, real_part])]
    )
    first_w = jnp.transpose(first_w, (2, 4, 3, 1, 5, 0, 6)).reshape(
        block_count, q_local * group, 2 * width
    )
    if group == 64 and t_local == 16 and n_mode % 2 == 0 and q_local % 2 == 0:
        second = jnp.take(w2_table, second_ids.reshape(-1), axis=0)
        second = second.reshape(block_count, n_cuts, 2, n_mode, a_count, out_width)
        real_two, imag_two = second[:, :, 0], second[:, :, 1]
        second_w = jnp.stack(
            [jnp.stack([real_two, imag_two]), jnp.stack([-imag_two, real_two])]
        )
        second_w = jnp.transpose(second_w, (1, 2, 4, 3, 0, 5, 6)).reshape(
            2, block_count * n_mode * group, out_width
        )
        return regroup(stem_parts, jnp.swapaxes(first_w, 1, 2), second_w, q_local, t_local)
    else:
        second = jnp.take(w2_table, second_ids.reshape(-1), axis=0)
        second = jnp.swapaxes(second, 2, 3)
        second = second.reshape(block_count, n_cuts, 2, out_width, n_mode, a_count)
        real_two, imag_two = second[:, :, 0], second[:, :, 1]
        second_w = jnp.stack(
            [jnp.stack([real_two, -imag_two]), jnp.stack([imag_two, real_two])]
        )
        second_w = jnp.transpose(second_w, (0, 4, 2, 5, 3, 1, 6)).reshape(
            2 * out_width, block_count * n_mode * group
        )
        product = jnp.einsum(
            "brk,bnk->brn", stem_rows, first_w, preferred_element_type=jnp.float32
        ).astype(jnp.bfloat16)
        lhs = product.reshape(block_count, n_mode, t_local, q_local, group)
        lhs = jnp.transpose(lhs, (3, 2, 0, 1, 4)).reshape(
            q_local * t_local, block_count * n_mode * group
        )
        amplitude = jnp.einsum(
            "mk,nk->mn", lhs, second_w, preferred_element_type=jnp.float32
        )
    amplitude = amplitude.reshape(q_local, t_local, 2, out_width)
    return jnp.transpose(amplitude, (1, 0, 2, 3))


def on_device(stem_blocks, w1_table, w2_table, slice_ids, mode_perm):
    n_mode = lax.axis_size("mode")
    n_cuts = lax.axis_size("cuts")
    rows = stem_blocks.shape[1]
    width = stem_blocks.shape[3]
    mid = w1_table.shape[3]
    inner = w2_table.shape[2]
    out_width = w2_table.shape[3]
    block_count = slice_ids.shape[1]
    t_local = rows // n_mode
    a_count = inner // n_mode
    q_count = mid // a_count
    q_local = q_count // n_cuts
    me = lax.axis_index("cuts")
    sizes = (n_mode, t_local, n_cuts, a_count, q_local)

    pieces = stem_blocks[0].reshape(1, n_mode, t_local, 2, width)
    payload = jnp.broadcast_to(pieces, (n_cuts, n_mode, t_local, 2, width))
    payload = payload.reshape(n_cuts * n_mode, t_local, 2, width)
    stem_parts = lax.all_to_all(payload, ("cuts", "mode"), 0, 0, tiled=True)
    stem_rows = stem_parts.reshape(block_count, n_mode * t_local, 2 * width)

    all_ids = gather_over_cuts(slice_ids[0], n_cuts)
    first_ids = all_ids[:, :, 0].T
    second_ids = all_ids[:, :, 1].T

    perm_grid = mode_perm.reshape(a_count, q_count)
    wanted = lax.dynamic_slice_in_dim(perm_grid, me * q_local, q_local, axis=1).reshape(-1)
    picker = (jnp.arange(mid, dtype=jnp.int32)[:, None] == wanted[None, :]).astype(w1_table.dtype)
    first_cols = jnp.einsum(
        "spkj,jn->spkn", w1_table, picker, preferred_element_type=jnp.float32
    ).astype(w1_table.dtype)
    real_part, imag_part = first_cols[:, 0], first_cols[:, 1]
    upper = jnp.concatenate([real_part, imag_part], axis=2)
    lower = jnp.concatenate([-imag_part, real_part], axis=2)
    first_all = jnp.concatenate([upper, lower], axis=1)

    if block_count * n_cuts <= 8:
        wanted_t = lax.dynamic_slice_in_dim(perm_grid, me * q_local, q_local, axis=1).T.reshape(-1)
        picker_t = (wanted_t[:, None] == jnp.arange(mid, dtype=jnp.int32)[None, :]).astype(w1_table.dtype)
        first_t = jnp.einsum(
            "nj,spkj->spnk", picker_t, w1_table, preferred_element_type=jnp.float32
        ).astype(w1_table.dtype)
        return stacked_part(stem_rows, first_t, w2_table, first_ids, second_ids, sizes, stem_parts)
    else:
        def one_block(index, running):
            stem_one = lax.dynamic_slice_in_dim(stem_rows, index, 1, axis=0)
            first_one = lax.dynamic_slice_in_dim(first_ids, index, 1, axis=0)
            second_one = lax.dynamic_slice_in_dim(second_ids, index, 1, axis=0)
            return running + blocks_part(
                stem_one, first_all, w2_table, first_one, second_one.reshape(-1), sizes
            )

        begin = jnp.zeros((t_local * q_local * 2, out_width), jnp.float32)
        amplitude = lax.fori_loop(0, block_count, one_block, begin)
    return amplitude.reshape(t_local, q_local, 2, out_width)


def solution(mesh):
    placed = (P("cuts", "mode", None, None), P(), P(), P("cuts", None, None), P())
    return jax.shard_map(
        on_device,
        mesh=mesh,
        in_specs=placed,
        out_specs=P("mode", "cuts", None, None),
        check_vma=False,
    )
```

```python
import jax
import jax.numpy as jnp
from jax import lax
from jax.experimental import pallas as pl
from jax.experimental.pallas import tpu as pltpu
from jax.sharding import PartitionSpec as P


def gather_over_cuts(own, n_cuts):
    pieces = [own]
    current = own
    ring = [(j, (j + 1) % n_cuts) for j in range(n_cuts)]
    for _ in range(1, n_cuts):
        current = lax.ppermute(current, "cuts", ring)
        pieces.append(current)
    stacked = jnp.stack(pieces)
    me = lax.axis_index("cuts")
    order = (me - jnp.arange(n_cuts, dtype=jnp.int32)) % n_cuts
    return jnp.take(stacked, order, axis=0)


def blocks_part(stem_rows, first_all, w2_table, first_ids, second_ids, sizes):
    n_mode, t_local, n_cuts, a_count, q_local = sizes
    chunk = stem_rows.shape[0]
    wide_in = stem_rows.shape[2]
    col_width = first_all.shape[2]
    slice_count, _, inner, out_width = w2_table.shape
    first_w = jnp.take(first_all, first_ids, axis=0)
    first_w = jnp.transpose(first_w, (0, 2, 1, 3)).reshape(
        chunk, wide_in, n_cuts * col_width
    )
    product = jnp.einsum(
        "bri,bio->bro", stem_rows, first_w, preferred_element_type=jnp.float32
    ).astype(jnp.bfloat16)
    split = product.reshape(chunk, n_mode, t_local, n_cuts, 2, a_count, q_local)
    real_p, imag_p = split[:, :, :, :, 0], split[:, :, :, :, 1]
    lhs = jnp.stack(
        [
            jnp.stack([real_p, -imag_p]),
            jnp.stack([imag_p, real_p]),
        ]
    )
    lhs = jnp.transpose(lhs, (4, 7, 0, 2, 5, 1, 3, 6)).reshape(
        t_local * q_local * 2, chunk * n_cuts * 2 * inner
    )
    second_w = jnp.take(
        w2_table.reshape(slice_count, 2 * inner, out_width), second_ids, axis=0
    ).reshape(chunk * n_cuts * 2 * inner, out_width)
    return jnp.dot(lhs, second_w, preferred_element_type=jnp.float32)


def regroup_kernel(stem_ref, weight_ref, second_ref, out_ref, real_ref, imag_ref):
    block_count, rows, _ = stem_ref.shape
    q_local = weight_ref.shape[2] // 64
    t_local = 16
    n_mode = rows // t_local
    lane = lax.broadcasted_iota(jnp.int32, (t_local, 128), 1)
    low = lane < 64
    imag_lane = (lane // 16) % 2 == 1

    def store(row, col, tile):
        real_ref[row:row + t_local, col:col + 128] = jnp.where(imag_lane, -tile, tile)
        imag_ref[row:row + t_local, col:col + 128] = jnp.where(
            imag_lane, pltpu.roll(tile, 16, 1), pltpu.roll(tile, 112, 1)
        )

    for b in range(block_count):
        product = jnp.dot(
            stem_ref[b], weight_ref[b], preferred_element_type=jnp.float32
        ).astype(jnp.bfloat16)
        for pair in range(n_mode // 2):
            upper = product[(2 * pair) * t_local:(2 * pair + 1) * t_local]
            lower = product[(2 * pair + 1) * t_local:(2 * pair + 2) * t_local]
            col = (b * n_mode // 2 + pair) * 128
            for qp in range(q_local // 2):
                first = upper[:, qp * 128:(qp + 1) * 128]
                second = lower[:, qp * 128:(qp + 1) * 128]
                store((2 * qp) * t_local, col, jnp.where(low, first, pltpu.roll(second, 64, 1)))
                store((2 * qp + 1) * t_local, col, jnp.where(low, pltpu.roll(first, 64, 1), second))
    weights = second_ref[...]
    for part, lhs_ref in enumerate((real_ref, imag_ref)):
        result = jnp.dot(lhs_ref[...], weights, preferred_element_type=jnp.float32)
        for q in range(q_local):
            out_ref[:, q, part, :] = result[q * t_local:(q + 1) * t_local]


def regroup(stem_rows, first_w, second_w, q_local, t_local):
    block_count, rows, _ = stem_rows.shape
    n_mode = rows // t_local
    lhs_shape = (q_local * t_local, block_count * n_mode * 64)
    out_shape = jax.ShapeDtypeStruct(
        (t_local, q_local, 2, second_w.shape[1]), jnp.float32
    )
    flops = 2 * block_count * rows * first_w.shape[1] * first_w.shape[2]
    flops += 2 * 2 * lhs_shape[0] * lhs_shape[1] * second_w.shape[1]
    return pl.pallas_call(
        regroup_kernel,
        out_shape=out_shape,
        in_specs=[pl.BlockSpec(memory_space=pltpu.VMEM)] * 3,
        out_specs=pl.BlockSpec(memory_space=pltpu.VMEM),
        scratch_shapes=[pltpu.VMEM(lhs_shape, jnp.bfloat16)] * 2,
        compiler_params=pltpu.CompilerParams(vmem_limit_bytes=16 * 1024 * 1024),
        cost_estimate=pl.CostEstimate(
            flops=flops,
            transcendentals=0,
            bytes_accessed=2 * (stem_rows.size + first_w.size + second_w.size)
            + 4 * lhs_shape[0] * 2 * second_w.shape[1],
        ),
    )(stem_rows, first_w, second_w)

def stacked_part(stem_rows, first_t, w2_table, first_ids, second_ids, sizes):
    n_mode, t_local, n_cuts, a_count, q_local = sizes
    block_count = stem_rows.shape[0]
    width = first_t.shape[3]
    _, _, inner, out_width = w2_table.shape
    group = n_cuts * 2 * a_count
    picked = jnp.take(first_t, first_ids.reshape(-1), axis=0)
    picked = picked.reshape(block_count, n_cuts, 2, q_local, a_count, width)
    real_part, imag_part = picked[:, :, 0], picked[:, :, 1]
    first_w = jnp.stack(
        [jnp.stack([real_part, imag_part]), jnp.stack([-imag_part, real_part])]
    )
    first_w = jnp.transpose(first_w, (2, 4, 3, 1, 5, 0, 6)).reshape(
        block_count, q_local * group, 2 * width
    )
    if group == 64 and t_local == 16 and n_mode % 2 == 0 and q_local % 2 == 0:
        second = jnp.take(w2_table, second_ids.reshape(-1), axis=0)
        second = second.reshape(block_count, n_cuts, 2, n_mode, a_count, out_width)
        second_w = jnp.transpose(second, (0, 3, 1, 2, 4, 5)).reshape(
            block_count * n_mode * group, out_width
        )
        return regroup(stem_rows, jnp.swapaxes(first_w, 1, 2), second_w, q_local, t_local)
    else:
        second = jnp.take(w2_table, second_ids.reshape(-1), axis=0)
        second = jnp.swapaxes(second, 2, 3)
        second = second.reshape(block_count, n_cuts, 2, out_width, n_mode, a_count)
        real_two, imag_two = second[:, :, 0], second[:, :, 1]
        second_w = jnp.stack(
            [jnp.stack([real_two, -imag_two]), jnp.stack([imag_two, real_two])]
        )
        second_w = jnp.transpose(second_w, (0, 4, 2, 5, 3, 1, 6)).reshape(
            2 * out_width, block_count * n_mode * group
        )
        product = jnp.einsum(
            "brk,bnk->brn", stem_rows, first_w, preferred_element_type=jnp.float32
        ).astype(jnp.bfloat16)
        lhs = product.reshape(block_count, n_mode, t_local, q_local, group)
        lhs = jnp.transpose(lhs, (3, 2, 0, 1, 4)).reshape(
            q_local * t_local, block_count * n_mode * group
        )
        amplitude = jnp.einsum(
            "mk,nk->mn", lhs, second_w, preferred_element_type=jnp.float32
        )
    amplitude = amplitude.reshape(q_local, t_local, 2, out_width)
    return jnp.transpose(amplitude, (1, 0, 2, 3))


def on_device(stem_blocks, w1_table, w2_table, slice_ids, mode_perm):
    n_mode = lax.axis_size("mode")
    n_cuts = lax.axis_size("cuts")
    rows = stem_blocks.shape[1]
    width = stem_blocks.shape[3]
    mid = w1_table.shape[3]
    inner = w2_table.shape[2]
    out_width = w2_table.shape[3]
    block_count = slice_ids.shape[1]
    t_local = rows // n_mode
    a_count = inner // n_mode
    q_count = mid // a_count
    q_local = q_count // n_cuts
    me = lax.axis_index("cuts")
    sizes = (n_mode, t_local, n_cuts, a_count, q_local)

    pieces = stem_blocks[0].reshape(1, n_mode, t_local, 2 * width)
    payload = jnp.broadcast_to(pieces, (n_cuts, n_mode, t_local, 2 * width))
    payload = payload.reshape(n_cuts * n_mode, t_local, 2 * width)
    stem_rows = lax.all_to_all(payload, ("cuts", "mode"), 0, 0, tiled=True)
    stem_rows = stem_rows.reshape(block_count, n_mode * t_local, 2 * width)

    all_ids = gather_over_cuts(slice_ids[0], n_cuts)
    first_ids = all_ids[:, :, 0].T
    second_ids = all_ids[:, :, 1].T

    perm_grid = mode_perm.reshape(a_count, q_count)
    wanted = lax.dynamic_slice_in_dim(perm_grid, me * q_local, q_local, axis=1).reshape(-1)
    picker = (jnp.arange(mid, dtype=jnp.int32)[:, None] == wanted[None, :]).astype(w1_table.dtype)
    first_cols = jnp.einsum(
        "spkj,jn->spkn", w1_table, picker, preferred_element_type=jnp.float32
    ).astype(w1_table.dtype)
    real_part, imag_part = first_cols[:, 0], first_cols[:, 1]
    upper = jnp.concatenate([real_part, imag_part], axis=2)
    lower = jnp.concatenate([-imag_part, real_part], axis=2)
    first_all = jnp.concatenate([upper, lower], axis=1)

    if block_count * n_cuts <= 8:
        wanted_t = lax.dynamic_slice_in_dim(perm_grid, me * q_local, q_local, axis=1).T.reshape(-1)
        picker_t = (wanted_t[:, None] == jnp.arange(mid, dtype=jnp.int32)[None, :]).astype(w1_table.dtype)
        first_t = jnp.einsum(
            "nj,spkj->spnk", picker_t, w1_table, preferred_element_type=jnp.float32
        ).astype(w1_table.dtype)
        return stacked_part(stem_rows, first_t, w2_table, first_ids, second_ids, sizes)
    else:
        def one_block(index, running):
            stem_one = lax.dynamic_slice_in_dim(stem_rows, index, 1, axis=0)
            first_one = lax.dynamic_slice_in_dim(first_ids, index, 1, axis=0)
            second_one = lax.dynamic_slice_in_dim(second_ids, index, 1, axis=0)
            return running + blocks_part(
                stem_one, first_all, w2_table, first_one, second_one.reshape(-1), sizes
            )

        begin = jnp.zeros((t_local * q_local * 2, out_width), jnp.float32)
        amplitude = lax.fori_loop(0, block_count, one_block, begin)
    return amplitude.reshape(t_local, q_local, 2, out_width)


def solution(mesh):
    placed = (P("cuts", "mode", None, None), P(), P(), P("cuts", None, None), P())
    return jax.shard_map(
        on_device,
        mesh=mesh,
        in_specs=placed,
        out_specs=P("mode", "cuts", None, None),
        check_vma=False,
    )
```

```python
import jax
import jax.numpy as jnp
from jax import lax
from jax.experimental import pallas as pl
from jax.experimental.pallas import tpu as pltpu
from jax.sharding import PartitionSpec as P


def gather_over_cuts(own, n_cuts):
    pieces = [own]
    current = own
    ring = [(j, (j + 1) % n_cuts) for j in range(n_cuts)]
    for _ in range(1, n_cuts):
        current = lax.ppermute(current, "cuts", ring)
        pieces.append(current)
    stacked = jnp.stack(pieces)
    me = lax.axis_index("cuts")
    order = (me - jnp.arange(n_cuts, dtype=jnp.int32)) % n_cuts
    return jnp.take(stacked, order, axis=0)


def blocks_part(stem_rows, first_all, w2_table, first_ids, second_ids, sizes):
    n_mode, t_local, n_cuts, a_count, q_local = sizes
    chunk = stem_rows.shape[0]
    wide_in = stem_rows.shape[2]
    col_width = first_all.shape[2]
    slice_count, _, inner, out_width = w2_table.shape
    first_w = jnp.take(first_all, first_ids, axis=0)
    first_w = jnp.transpose(first_w, (0, 2, 1, 3)).reshape(
        chunk, wide_in, n_cuts * col_width
    )
    product = jnp.einsum(
        "bri,bio->bro", stem_rows, first_w, preferred_element_type=jnp.float32
    ).astype(jnp.bfloat16)
    split = product.reshape(chunk, n_mode, t_local, n_cuts, 2, a_count, q_local)
    real_p, imag_p = split[:, :, :, :, 0], split[:, :, :, :, 1]
    lhs = jnp.stack(
        [
            jnp.stack([real_p, -imag_p]),
            jnp.stack([imag_p, real_p]),
        ]
    )
    lhs = jnp.transpose(lhs, (4, 7, 0, 2, 5, 1, 3, 6)).reshape(
        t_local * q_local * 2, chunk * n_cuts * 2 * inner
    )
    second_w = jnp.take(
        w2_table.reshape(slice_count, 2 * inner, out_width), second_ids, axis=0
    ).reshape(chunk * n_cuts * 2 * inner, out_width)
    return jnp.dot(lhs, second_w, preferred_element_type=jnp.float32)


def regroup_kernel(stem_ref, weight_ref, second_ref, out_ref, real_ref, imag_ref):
    block_count, rows, _ = stem_ref.shape
    q_local = weight_ref.shape[2] // 64
    t_local = 16
    n_mode = rows // t_local
    lane = lax.broadcasted_iota(jnp.int32, (t_local, 128), 1)
    low = lane < 64
    imag_lane = (lane // 16) % 2 == 1

    def store(row, col, tile):
        real_ref[row:row + t_local, col:col + 128] = jnp.where(imag_lane, -tile, tile)
        imag_ref[row:row + t_local, col:col + 128] = jnp.where(
            imag_lane, pltpu.roll(tile, 16, 1), pltpu.roll(tile, 112, 1)
        )

    for b in range(block_count):
        product = jnp.dot(
            stem_ref[b], weight_ref[b], preferred_element_type=jnp.float32
        ).astype(jnp.bfloat16)
        for pair in range(n_mode // 2):
            upper = product[(2 * pair) * t_local:(2 * pair + 1) * t_local]
            lower = product[(2 * pair + 1) * t_local:(2 * pair + 2) * t_local]
            col = (b * n_mode // 2 + pair) * 128
            for qp in range(q_local // 2):
                first = upper[:, qp * 128:(qp + 1) * 128]
                second = lower[:, qp * 128:(qp + 1) * 128]
                store((2 * qp) * t_local, col, jnp.where(low, first, pltpu.roll(second, 64, 1)))
                store((2 * qp + 1) * t_local, col, jnp.where(low, pltpu.roll(first, 64, 1), second))
    weights = second_ref[...]
    for part, lhs_ref in enumerate((real_ref, imag_ref)):
        result = jnp.dot(lhs_ref[...], weights, preferred_element_type=jnp.float32)
        for q in range(q_local):
            out_ref[:, q, part, :] = result[q * t_local:(q + 1) * t_local]


def regroup(stem_rows, first_w, second_w, q_local, t_local):
    block_count, rows, _ = stem_rows.shape
    n_mode = rows // t_local
    lhs_shape = (q_local * t_local, block_count * n_mode * 64)
    out_shape = jax.ShapeDtypeStruct(
        (t_local, q_local, 2, second_w.shape[1]), jnp.float32
    )
    flops = 2 * block_count * rows * first_w.shape[1] * first_w.shape[2]
    flops += 2 * 2 * lhs_shape[0] * lhs_shape[1] * second_w.shape[1]
    return pl.pallas_call(
        regroup_kernel,
        out_shape=out_shape,
        in_specs=[pl.BlockSpec(memory_space=pltpu.VMEM)] * 3,
        out_specs=pl.BlockSpec(memory_space=pltpu.VMEM),
        scratch_shapes=[pltpu.VMEM(lhs_shape, jnp.bfloat16)] * 2,
        cost_estimate=pl.CostEstimate(
            flops=flops,
            transcendentals=0,
            bytes_accessed=2 * (stem_rows.size + first_w.size + second_w.size)
            + 4 * lhs_shape[0] * 2 * second_w.shape[1],
        ),
    )(stem_rows, first_w, second_w)

def stacked_part(stem_rows, first_t, w2_table, first_ids, second_ids, sizes):
    n_mode, t_local, n_cuts, a_count, q_local = sizes
    block_count = stem_rows.shape[0]
    width = first_t.shape[3]
    _, _, inner, out_width = w2_table.shape
    group = n_cuts * 2 * a_count
    picked = jnp.take(first_t, first_ids.reshape(-1), axis=0)
    picked = picked.reshape(block_count, n_cuts, 2, q_local, a_count, width)
    real_part, imag_part = picked[:, :, 0], picked[:, :, 1]
    first_w = jnp.stack(
        [jnp.stack([real_part, imag_part]), jnp.stack([-imag_part, real_part])]
    )
    first_w = jnp.transpose(first_w, (2, 4, 3, 1, 5, 0, 6)).reshape(
        block_count, q_local * group, 2 * width
    )
    if group == 64 and t_local == 16 and n_mode % 2 == 0 and q_local % 2 == 0:
        second = jnp.take(w2_table, second_ids.reshape(-1), axis=0)
        second = second.reshape(block_count, n_cuts, 2, n_mode, a_count, out_width)
        second_w = jnp.transpose(second, (0, 3, 1, 2, 4, 5)).reshape(
            block_count * n_mode * group, out_width
        )
        return regroup(stem_rows, jnp.swapaxes(first_w, 1, 2), second_w, q_local, t_local)
    else:
        second = jnp.take(w2_table, second_ids.reshape(-1), axis=0)
        second = jnp.swapaxes(second, 2, 3)
        second = second.reshape(block_count, n_cuts, 2, out_width, n_mode, a_count)
        real_two, imag_two = second[:, :, 0], second[:, :, 1]
        second_w = jnp.stack(
            [jnp.stack([real_two, -imag_two]), jnp.stack([imag_two, real_two])]
        )
        second_w = jnp.transpose(second_w, (0, 4, 2, 5, 3, 1, 6)).reshape(
            2 * out_width, block_count * n_mode * group
        )
        product = jnp.einsum(
            "brk,bnk->brn", stem_rows, first_w, preferred_element_type=jnp.float32
        ).astype(jnp.bfloat16)
        lhs = product.reshape(block_count, n_mode, t_local, q_local, group)
        lhs = jnp.transpose(lhs, (3, 2, 0, 1, 4)).reshape(
            q_local * t_local, block_count * n_mode * group
        )
        amplitude = jnp.einsum(
            "mk,nk->mn", lhs, second_w, preferred_element_type=jnp.float32
        )
    amplitude = amplitude.reshape(q_local, t_local, 2, out_width)
    return jnp.transpose(amplitude, (1, 0, 2, 3))


def on_device(stem_blocks, w1_table, w2_table, slice_ids, mode_perm):
    n_mode = lax.axis_size("mode")
    n_cuts = lax.axis_size("cuts")
    rows = stem_blocks.shape[1]
    width = stem_blocks.shape[3]
    mid = w1_table.shape[3]
    inner = w2_table.shape[2]
    out_width = w2_table.shape[3]
    block_count = slice_ids.shape[1]
    t_local = rows // n_mode
    a_count = inner // n_mode
    q_count = mid // a_count
    q_local = q_count // n_cuts
    me = lax.axis_index("cuts")
    sizes = (n_mode, t_local, n_cuts, a_count, q_local)

    pieces = stem_blocks[0].reshape(1, n_mode, t_local, 2 * width)
    payload = jnp.broadcast_to(pieces, (n_cuts, n_mode, t_local, 2 * width))
    payload = payload.reshape(n_cuts * n_mode, t_local, 2 * width)
    stem_rows = lax.all_to_all(payload, ("cuts", "mode"), 0, 0, tiled=True)
    stem_rows = stem_rows.reshape(block_count, n_mode * t_local, 2 * width)

    all_ids = gather_over_cuts(slice_ids[0], n_cuts)
    first_ids = all_ids[:, :, 0].T
    second_ids = all_ids[:, :, 1].T

    perm_grid = mode_perm.reshape(a_count, q_count)
    wanted = lax.dynamic_slice_in_dim(perm_grid, me * q_local, q_local, axis=1).reshape(-1)
    picker = (jnp.arange(mid, dtype=jnp.int32)[:, None] == wanted[None, :]).astype(w1_table.dtype)
    first_cols = jnp.einsum(
        "spkj,jn->spkn", w1_table, picker, preferred_element_type=jnp.float32
    ).astype(w1_table.dtype)
    real_part, imag_part = first_cols[:, 0], first_cols[:, 1]
    upper = jnp.concatenate([real_part, imag_part], axis=2)
    lower = jnp.concatenate([-imag_part, real_part], axis=2)
    first_all = jnp.concatenate([upper, lower], axis=1)

    if block_count * n_cuts <= 8:
        wanted_t = lax.dynamic_slice_in_dim(perm_grid, me * q_local, q_local, axis=1).T.reshape(-1)
        picker_t = (wanted_t[:, None] == jnp.arange(mid, dtype=jnp.int32)[None, :]).astype(w1_table.dtype)
        first_t = jnp.einsum(
            "nj,spkj->spnk", picker_t, w1_table, preferred_element_type=jnp.float32
        ).astype(w1_table.dtype)
        return stacked_part(stem_rows, first_t, w2_table, first_ids, second_ids, sizes)
    else:
        def one_block(index, running):
            stem_one = lax.dynamic_slice_in_dim(stem_rows, index, 1, axis=0)
            first_one = lax.dynamic_slice_in_dim(first_ids, index, 1, axis=0)
            second_one = lax.dynamic_slice_in_dim(second_ids, index, 1, axis=0)
            return running + blocks_part(
                stem_one, first_all, w2_table, first_one, second_one.reshape(-1), sizes
            )

        begin = jnp.zeros((t_local * q_local * 2, out_width), jnp.float32)
        amplitude = lax.fori_loop(0, block_count, one_block, begin)
    return amplitude.reshape(t_local, q_local, 2, out_width)


def solution(mesh):
    placed = (P("cuts", "mode", None, None), P(), P(), P("cuts", None, None), P())
    return jax.shard_map(
        on_device,
        mesh=mesh,
        in_specs=placed,
        out_specs=P("mode", "cuts", None, None),
        check_vma=False,
    )
```

```python
import jax
import jax.numpy as jnp
from jax import lax
from jax.experimental import pallas as pl
from jax.experimental.pallas import tpu as pltpu
from jax.sharding import PartitionSpec as P


def gather_over_cuts(own, n_cuts):
    pieces = [own]
    current = own
    ring = [(j, (j + 1) % n_cuts) for j in range(n_cuts)]
    for _ in range(1, n_cuts):
        current = lax.ppermute(current, "cuts", ring)
        pieces.append(current)
    stacked = jnp.stack(pieces)
    me = lax.axis_index("cuts")
    order = (me - jnp.arange(n_cuts, dtype=jnp.int32)) % n_cuts
    return jnp.take(stacked, order, axis=0)


def blocks_part(stem_rows, first_all, w2_table, first_ids, second_ids, sizes):
    n_mode, t_local, n_cuts, a_count, q_local = sizes
    chunk = stem_rows.shape[0]
    wide_in = stem_rows.shape[2]
    col_width = first_all.shape[2]
    slice_count, _, inner, out_width = w2_table.shape
    first_w = jnp.take(first_all, first_ids, axis=0)
    first_w = jnp.transpose(first_w, (0, 2, 1, 3)).reshape(
        chunk, wide_in, n_cuts * col_width
    )
    product = jnp.einsum(
        "bri,bio->bro", stem_rows, first_w, preferred_element_type=jnp.float32
    ).astype(jnp.bfloat16)
    split = product.reshape(chunk, n_mode, t_local, n_cuts, 2, a_count, q_local)
    real_p, imag_p = split[:, :, :, :, 0], split[:, :, :, :, 1]
    lhs = jnp.stack(
        [
            jnp.stack([real_p, -imag_p]),
            jnp.stack([imag_p, real_p]),
        ]
    )
    lhs = jnp.transpose(lhs, (4, 7, 0, 2, 5, 1, 3, 6)).reshape(
        t_local * q_local * 2, chunk * n_cuts * 2 * inner
    )
    second_w = jnp.take(
        w2_table.reshape(slice_count, 2 * inner, out_width), second_ids, axis=0
    ).reshape(chunk * n_cuts * 2 * inner, out_width)
    return jnp.dot(lhs, second_w, preferred_element_type=jnp.float32)


def regroup_kernel(stem_ref, weight_ref, second_ref, out_ref, lhs_ref):
    block_count, rows, _ = stem_ref.shape
    q_local = weight_ref.shape[2] // 64
    t_local = 16
    n_mode = rows // t_local
    lane = lax.broadcasted_iota(jnp.int32, (t_local, 128), 1)
    low = lane < 64
    imag_lane = (lane // 16) % 2 == 1

    half = q_local * t_local

    def store(row, col, tile):
        lhs_ref[row:row + t_local, col:col + 128] = jnp.where(imag_lane, -tile, tile)
        lhs_ref[half + row:half + row + t_local, col:col + 128] = jnp.where(
            imag_lane, pltpu.roll(tile, 16, 1), pltpu.roll(tile, 112, 1)
        )

    for b in range(block_count):
        product = jnp.dot(
            stem_ref[b], weight_ref[b], preferred_element_type=jnp.float32
        ).astype(jnp.bfloat16)
        for pair in range(n_mode // 2):
            upper = product[(2 * pair) * t_local:(2 * pair + 1) * t_local]
            lower = product[(2 * pair + 1) * t_local:(2 * pair + 2) * t_local]
            col = (b * n_mode // 2 + pair) * 128
            for qp in range(q_local // 2):
                first = upper[:, qp * 128:(qp + 1) * 128]
                second = lower[:, qp * 128:(qp + 1) * 128]
                store((2 * qp) * t_local, col, jnp.where(low, first, pltpu.roll(second, 64, 1)))
                store((2 * qp + 1) * t_local, col, jnp.where(low, pltpu.roll(first, 64, 1), second))
    result = jnp.dot(lhs_ref[...], second_ref[...], preferred_element_type=jnp.float32)
    for part in range(2):
        for q in range(q_local):
            row = part * half + q * t_local
            out_ref[:, q, part, :] = result[row:row + t_local]


def regroup(stem_rows, first_w, second_w, q_local, t_local):
    block_count, rows, _ = stem_rows.shape
    n_mode = rows // t_local
    lhs_shape = (q_local * t_local, block_count * n_mode * 64)
    out_shape = jax.ShapeDtypeStruct(
        (t_local, q_local, 2, second_w.shape[1]), jnp.float32
    )
    flops = 2 * block_count * rows * first_w.shape[1] * first_w.shape[2]
    flops += 2 * 2 * lhs_shape[0] * lhs_shape[1] * second_w.shape[1]
    return pl.pallas_call(
        regroup_kernel,
        out_shape=out_shape,
        in_specs=[pl.BlockSpec(memory_space=pltpu.VMEM)] * 3,
        out_specs=pl.BlockSpec(memory_space=pltpu.VMEM),
        scratch_shapes=[pltpu.VMEM((2 * lhs_shape[0], lhs_shape[1]), jnp.bfloat16)],
        cost_estimate=pl.CostEstimate(
            flops=flops,
            transcendentals=0,
            bytes_accessed=2 * (stem_rows.size + first_w.size + second_w.size)
            + 4 * lhs_shape[0] * 2 * second_w.shape[1],
        ),
    )(stem_rows, first_w, second_w)

def stacked_part(stem_rows, first_t, w2_table, first_ids, second_ids, sizes):
    n_mode, t_local, n_cuts, a_count, q_local = sizes
    block_count = stem_rows.shape[0]
    width = first_t.shape[3]
    _, _, inner, out_width = w2_table.shape
    group = n_cuts * 2 * a_count
    picked = jnp.take(first_t, first_ids.reshape(-1), axis=0)
    picked = picked.reshape(block_count, n_cuts, 2, q_local, a_count, width)
    real_part, imag_part = picked[:, :, 0], picked[:, :, 1]
    first_w = jnp.stack(
        [jnp.stack([real_part, imag_part]), jnp.stack([-imag_part, real_part])]
    )
    first_w = jnp.transpose(first_w, (2, 4, 3, 1, 5, 0, 6)).reshape(
        block_count, q_local * group, 2 * width
    )
    if group == 64 and t_local == 16 and n_mode % 2 == 0 and q_local % 2 == 0:
        second = jnp.take(w2_table, second_ids.reshape(-1), axis=0)
        second = second.reshape(block_count, n_cuts, 2, n_mode, a_count, out_width)
        second_w = jnp.transpose(second, (0, 3, 1, 2, 4, 5)).reshape(
            block_count * n_mode * group, out_width
        )
        return regroup(stem_rows, jnp.swapaxes(first_w, 1, 2), second_w, q_local, t_local)
    else:
        second = jnp.take(w2_table, second_ids.reshape(-1), axis=0)
        second = jnp.swapaxes(second, 2, 3)
        second = second.reshape(block_count, n_cuts, 2, out_width, n_mode, a_count)
        real_two, imag_two = second[:, :, 0], second[:, :, 1]
        second_w = jnp.stack(
            [jnp.stack([real_two, -imag_two]), jnp.stack([imag_two, real_two])]
        )
        second_w = jnp.transpose(second_w, (0, 4, 2, 5, 3, 1, 6)).reshape(
            2 * out_width, block_count * n_mode * group
        )
        product = jnp.einsum(
            "brk,bnk->brn", stem_rows, first_w, preferred_element_type=jnp.float32
        ).astype(jnp.bfloat16)
        lhs = product.reshape(block_count, n_mode, t_local, q_local, group)
        lhs = jnp.transpose(lhs, (3, 2, 0, 1, 4)).reshape(
            q_local * t_local, block_count * n_mode * group
        )
        amplitude = jnp.einsum(
            "mk,nk->mn", lhs, second_w, preferred_element_type=jnp.float32
        )
    amplitude = amplitude.reshape(q_local, t_local, 2, out_width)
    return jnp.transpose(amplitude, (1, 0, 2, 3))


def on_device(stem_blocks, w1_table, w2_table, slice_ids, mode_perm):
    n_mode = lax.axis_size("mode")
    n_cuts = lax.axis_size("cuts")
    rows = stem_blocks.shape[1]
    width = stem_blocks.shape[3]
    mid = w1_table.shape[3]
    inner = w2_table.shape[2]
    out_width = w2_table.shape[3]
    block_count = slice_ids.shape[1]
    t_local = rows // n_mode
    a_count = inner // n_mode
    q_count = mid // a_count
    q_local = q_count // n_cuts
    me = lax.axis_index("cuts")
    sizes = (n_mode, t_local, n_cuts, a_count, q_local)

    pieces = stem_blocks[0].reshape(1, n_mode, t_local, 2 * width)
    payload = jnp.broadcast_to(pieces, (n_cuts, n_mode, t_local, 2 * width))
    payload = payload.reshape(n_cuts * n_mode, t_local, 2 * width)
    stem_rows = lax.all_to_all(payload, ("cuts", "mode"), 0, 0, tiled=True)
    stem_rows = stem_rows.reshape(block_count, n_mode * t_local, 2 * width)

    all_ids = gather_over_cuts(slice_ids[0], n_cuts)
    first_ids = all_ids[:, :, 0].T
    second_ids = all_ids[:, :, 1].T

    perm_grid = mode_perm.reshape(a_count, q_count)
    wanted = lax.dynamic_slice_in_dim(perm_grid, me * q_local, q_local, axis=1).reshape(-1)
    picker = (jnp.arange(mid, dtype=jnp.int32)[:, None] == wanted[None, :]).astype(w1_table.dtype)
    first_cols = jnp.einsum(
        "spkj,jn->spkn", w1_table, picker, preferred_element_type=jnp.float32
    ).astype(w1_table.dtype)
    real_part, imag_part = first_cols[:, 0], first_cols[:, 1]
    upper = jnp.concatenate([real_part, imag_part], axis=2)
    lower = jnp.concatenate([-imag_part, real_part], axis=2)
    first_all = jnp.concatenate([upper, lower], axis=1)

    if block_count * n_cuts <= 8:
        wanted_t = lax.dynamic_slice_in_dim(perm_grid, me * q_local, q_local, axis=1).T.reshape(-1)
        picker_t = (wanted_t[:, None] == jnp.arange(mid, dtype=jnp.int32)[None, :]).astype(w1_table.dtype)
        first_t = jnp.einsum(
            "nj,spkj->spnk", picker_t, w1_table, preferred_element_type=jnp.float32
        ).astype(w1_table.dtype)
        return stacked_part(stem_rows, first_t, w2_table, first_ids, second_ids, sizes)
    else:
        def one_block(index, running):
            stem_one = lax.dynamic_slice_in_dim(stem_rows, index, 1, axis=0)
            first_one = lax.dynamic_slice_in_dim(first_ids, index, 1, axis=0)
            second_one = lax.dynamic_slice_in_dim(second_ids, index, 1, axis=0)
            return running + blocks_part(
                stem_one, first_all, w2_table, first_one, second_one.reshape(-1), sizes
            )

        begin = jnp.zeros((t_local * q_local * 2, out_width), jnp.float32)
        amplitude = lax.fori_loop(0, block_count, one_block, begin)
    return amplitude.reshape(t_local, q_local, 2, out_width)


def solution(mesh):
    placed = (P("cuts", "mode", None, None), P(), P(), P("cuts", None, None), P())
    return jax.shard_map(
        on_device,
        mesh=mesh,
        in_specs=placed,
        out_specs=P("mode", "cuts", None, None),
        check_vma=False,
    )
```

```python
import jax
import jax.numpy as jnp
from jax import lax
from jax.experimental import pallas as pl
from jax.experimental.pallas import tpu as pltpu
from jax.sharding import PartitionSpec as P


def gather_over_cuts(own, n_cuts):
    pieces = [own]
    current = own
    ring = [(j, (j + 1) % n_cuts) for j in range(n_cuts)]
    for _ in range(1, n_cuts):
        current = lax.ppermute(current, "cuts", ring)
        pieces.append(current)
    stacked = jnp.stack(pieces)
    me = lax.axis_index("cuts")
    order = (me - jnp.arange(n_cuts, dtype=jnp.int32)) % n_cuts
    return jnp.take(stacked, order, axis=0)


def blocks_part(stem_rows, first_all, w2_table, first_ids, second_ids, sizes):
    n_mode, t_local, n_cuts, a_count, q_local = sizes
    chunk = stem_rows.shape[0]
    wide_in = stem_rows.shape[2]
    col_width = first_all.shape[2]
    slice_count, _, inner, out_width = w2_table.shape
    first_w = jnp.take(first_all, first_ids, axis=0)
    first_w = jnp.transpose(first_w, (0, 2, 1, 3)).reshape(
        chunk, wide_in, n_cuts * col_width
    )
    product = jnp.einsum(
        "bri,bio->bro", stem_rows, first_w, preferred_element_type=jnp.float32
    ).astype(jnp.bfloat16)
    split = product.reshape(chunk, n_mode, t_local, n_cuts, 2, a_count, q_local)
    real_p, imag_p = split[:, :, :, :, 0], split[:, :, :, :, 1]
    lhs = jnp.stack(
        [
            jnp.stack([real_p, -imag_p]),
            jnp.stack([imag_p, real_p]),
        ]
    )
    lhs = jnp.transpose(lhs, (4, 7, 0, 2, 5, 1, 3, 6)).reshape(
        t_local * q_local * 2, chunk * n_cuts * 2 * inner
    )
    second_w = jnp.take(
        w2_table.reshape(slice_count, 2 * inner, out_width), second_ids, axis=0
    ).reshape(chunk * n_cuts * 2 * inner, out_width)
    return jnp.dot(lhs, second_w, preferred_element_type=jnp.float32)


def payload_kernel(stem_ref, out_ref):
    width = stem_ref.shape[3]
    for part in range(2):
        plane = stem_ref[0, :, part, :]
        for cut in range(out_ref.shape[0]):
            out_ref[cut, :, part * width:(part + 1) * width] = plane


def build_payload(stem_blocks, n_cuts):
    rows, width = stem_blocks.shape[1], stem_blocks.shape[3]
    return pl.pallas_call(
        payload_kernel,
        out_shape=jax.ShapeDtypeStruct((n_cuts, rows, 2 * width), stem_blocks.dtype),
        in_specs=[pl.BlockSpec(memory_space=pltpu.VMEM)],
        out_specs=pl.BlockSpec(memory_space=pltpu.VMEM),
    )(stem_blocks)


def regroup_kernel(stem_ref, weight_ref, second_ref, out_ref, real_ref, imag_ref):
    block_count, rows, _ = stem_ref.shape
    q_local = weight_ref.shape[2] // 64
    t_local = 16
    n_mode = rows // t_local
    lane = lax.broadcasted_iota(jnp.int32, (t_local, 128), 1)
    low = lane < 64
    imag_lane = (lane // 16) % 2 == 1

    def store(row, col, tile):
        real_ref[row:row + t_local, col:col + 128] = jnp.where(imag_lane, -tile, tile)
        imag_ref[row:row + t_local, col:col + 128] = jnp.where(
            imag_lane, pltpu.roll(tile, 16, 1), pltpu.roll(tile, 112, 1)
        )

    for b in range(block_count):
        product = jnp.dot(
            stem_ref[b], weight_ref[b], preferred_element_type=jnp.float32
        ).astype(jnp.bfloat16)
        for pair in range(n_mode // 2):
            upper = product[(2 * pair) * t_local:(2 * pair + 1) * t_local]
            lower = product[(2 * pair + 1) * t_local:(2 * pair + 2) * t_local]
            col = (b * n_mode // 2 + pair) * 128
            for qp in range(q_local // 2):
                first = upper[:, qp * 128:(qp + 1) * 128]
                second = lower[:, qp * 128:(qp + 1) * 128]
                store((2 * qp) * t_local, col, jnp.where(low, first, pltpu.roll(second, 64, 1)))
                store((2 * qp + 1) * t_local, col, jnp.where(low, pltpu.roll(first, 64, 1), second))
    weights = second_ref[...]
    for part, lhs_ref in enumerate((real_ref, imag_ref)):
        result = jnp.dot(lhs_ref[...], weights, preferred_element_type=jnp.float32)
        for q in range(q_local):
            out_ref[:, q, part, :] = result[q * t_local:(q + 1) * t_local]


def regroup(stem_rows, first_w, second_w, q_local, t_local):
    block_count, rows, _ = stem_rows.shape
    n_mode = rows // t_local
    lhs_shape = (q_local * t_local, block_count * n_mode * 64)
    out_shape = jax.ShapeDtypeStruct(
        (t_local, q_local, 2, second_w.shape[1]), jnp.float32
    )
    flops = 2 * block_count * rows * first_w.shape[1] * first_w.shape[2]
    flops += 2 * 2 * lhs_shape[0] * lhs_shape[1] * second_w.shape[1]
    return pl.pallas_call(
        regroup_kernel,
        out_shape=out_shape,
        in_specs=[pl.BlockSpec(memory_space=pltpu.VMEM)] * 3,
        out_specs=pl.BlockSpec(memory_space=pltpu.VMEM),
        scratch_shapes=[pltpu.VMEM(lhs_shape, jnp.bfloat16)] * 2,
        cost_estimate=pl.CostEstimate(
            flops=flops,
            transcendentals=0,
            bytes_accessed=2 * (stem_rows.size + first_w.size + second_w.size)
            + 4 * lhs_shape[0] * 2 * second_w.shape[1],
        ),
    )(stem_rows, first_w, second_w)

def stacked_part(stem_rows, first_t, w2_table, first_ids, second_ids, sizes):
    n_mode, t_local, n_cuts, a_count, q_local = sizes
    block_count = stem_rows.shape[0]
    width = first_t.shape[3]
    _, _, inner, out_width = w2_table.shape
    group = n_cuts * 2 * a_count
    picked = jnp.take(first_t, first_ids.reshape(-1), axis=0)
    picked = picked.reshape(block_count, n_cuts, 2, q_local, a_count, width)
    real_part, imag_part = picked[:, :, 0], picked[:, :, 1]
    first_w = jnp.stack(
        [jnp.stack([real_part, imag_part]), jnp.stack([-imag_part, real_part])]
    )
    first_w = jnp.transpose(first_w, (2, 4, 3, 1, 5, 0, 6)).reshape(
        block_count, q_local * group, 2 * width
    )
    if group == 64 and t_local == 16 and n_mode % 2 == 0 and q_local % 2 == 0:
        second = jnp.take(w2_table, second_ids.reshape(-1), axis=0)
        second = second.reshape(block_count, n_cuts, 2, n_mode, a_count, out_width)
        second_w = jnp.transpose(second, (0, 3, 1, 2, 4, 5)).reshape(
            block_count * n_mode * group, out_width
        )
        return regroup(stem_rows, jnp.swapaxes(first_w, 1, 2), second_w, q_local, t_local)
    else:
        second = jnp.take(w2_table, second_ids.reshape(-1), axis=0)
        second = jnp.swapaxes(second, 2, 3)
        second = second.reshape(block_count, n_cuts, 2, out_width, n_mode, a_count)
        real_two, imag_two = second[:, :, 0], second[:, :, 1]
        second_w = jnp.stack(
            [jnp.stack([real_two, -imag_two]), jnp.stack([imag_two, real_two])]
        )
        second_w = jnp.transpose(second_w, (0, 4, 2, 5, 3, 1, 6)).reshape(
            2 * out_width, block_count * n_mode * group
        )
        product = jnp.einsum(
            "brk,bnk->brn", stem_rows, first_w, preferred_element_type=jnp.float32
        ).astype(jnp.bfloat16)
        lhs = product.reshape(block_count, n_mode, t_local, q_local, group)
        lhs = jnp.transpose(lhs, (3, 2, 0, 1, 4)).reshape(
            q_local * t_local, block_count * n_mode * group
        )
        amplitude = jnp.einsum(
            "mk,nk->mn", lhs, second_w, preferred_element_type=jnp.float32
        )
    amplitude = amplitude.reshape(q_local, t_local, 2, out_width)
    return jnp.transpose(amplitude, (1, 0, 2, 3))


def on_device(stem_blocks, w1_table, w2_table, slice_ids, mode_perm):
    n_mode = lax.axis_size("mode")
    n_cuts = lax.axis_size("cuts")
    rows = stem_blocks.shape[1]
    width = stem_blocks.shape[3]
    mid = w1_table.shape[3]
    inner = w2_table.shape[2]
    out_width = w2_table.shape[3]
    block_count = slice_ids.shape[1]
    t_local = rows // n_mode
    a_count = inner // n_mode
    q_count = mid // a_count
    q_local = q_count // n_cuts
    me = lax.axis_index("cuts")
    sizes = (n_mode, t_local, n_cuts, a_count, q_local)

    payload = build_payload(stem_blocks, n_cuts).reshape(n_cuts * n_mode, t_local, 2 * width)
    stem_rows = lax.all_to_all(payload, ("cuts", "mode"), 0, 0, tiled=True)
    stem_rows = stem_rows.reshape(block_count, n_mode * t_local, 2 * width)

    all_ids = gather_over_cuts(slice_ids[0], n_cuts)
    first_ids = all_ids[:, :, 0].T
    second_ids = all_ids[:, :, 1].T

    perm_grid = mode_perm.reshape(a_count, q_count)
    wanted = lax.dynamic_slice_in_dim(perm_grid, me * q_local, q_local, axis=1).reshape(-1)
    picker = (jnp.arange(mid, dtype=jnp.int32)[:, None] == wanted[None, :]).astype(w1_table.dtype)
    first_cols = jnp.einsum(
        "spkj,jn->spkn", w1_table, picker, preferred_element_type=jnp.float32
    ).astype(w1_table.dtype)
    real_part, imag_part = first_cols[:, 0], first_cols[:, 1]
    upper = jnp.concatenate([real_part, imag_part], axis=2)
    lower = jnp.concatenate([-imag_part, real_part], axis=2)
    first_all = jnp.concatenate([upper, lower], axis=1)

    if block_count * n_cuts <= 8:
        wanted_t = lax.dynamic_slice_in_dim(perm_grid, me * q_local, q_local, axis=1).T.reshape(-1)
        picker_t = (wanted_t[:, None] == jnp.arange(mid, dtype=jnp.int32)[None, :]).astype(w1_table.dtype)
        first_t = jnp.einsum(
            "nj,spkj->spnk", picker_t, w1_table, preferred_element_type=jnp.float32
        ).astype(w1_table.dtype)
        return stacked_part(stem_rows, first_t, w2_table, first_ids, second_ids, sizes)
    else:
        def one_block(index, running):
            stem_one = lax.dynamic_slice_in_dim(stem_rows, index, 1, axis=0)
            first_one = lax.dynamic_slice_in_dim(first_ids, index, 1, axis=0)
            second_one = lax.dynamic_slice_in_dim(second_ids, index, 1, axis=0)
            return running + blocks_part(
                stem_one, first_all, w2_table, first_one, second_one.reshape(-1), sizes
            )

        begin = jnp.zeros((t_local * q_local * 2, out_width), jnp.float32)
        amplitude = lax.fori_loop(0, block_count, one_block, begin)
    return amplitude.reshape(t_local, q_local, 2, out_width)


def solution(mesh):
    placed = (P("cuts", "mode", None, None), P(), P(), P("cuts", None, None), P())
    return jax.shard_map(
        on_device,
        mesh=mesh,
        in_specs=placed,
        out_specs=P("mode", "cuts", None, None),
        check_vma=False,
    )
```

```python
import jax
import jax.numpy as jnp
from jax import lax
from jax.experimental import pallas as pl
from jax.experimental.pallas import tpu as pltpu
from jax.sharding import PartitionSpec as P


def gather_over_cuts(own, n_cuts):
    pieces = [own]
    current = own
    ring = [(j, (j + 1) % n_cuts) for j in range(n_cuts)]
    for _ in range(1, n_cuts):
        current = lax.ppermute(current, "cuts", ring)
        pieces.append(current)
    stacked = jnp.stack(pieces)
    me = lax.axis_index("cuts")
    order = (me - jnp.arange(n_cuts, dtype=jnp.int32)) % n_cuts
    return jnp.take(stacked, order, axis=0)


def blocks_part(stem_rows, first_all, w2_table, first_ids, second_ids, sizes):
    n_mode, t_local, n_cuts, a_count, q_local = sizes
    chunk = stem_rows.shape[0]
    wide_in = stem_rows.shape[2]
    col_width = first_all.shape[2]
    slice_count, _, inner, out_width = w2_table.shape
    first_w = jnp.take(first_all, first_ids, axis=0)
    first_w = jnp.transpose(first_w, (0, 2, 1, 3)).reshape(
        chunk, wide_in, n_cuts * col_width
    )
    product = jnp.einsum(
        "bri,bio->bro", stem_rows, first_w, preferred_element_type=jnp.float32
    ).astype(jnp.bfloat16)
    split = product.reshape(chunk, n_mode, t_local, n_cuts, 2, a_count, q_local)
    real_p, imag_p = split[:, :, :, :, 0], split[:, :, :, :, 1]
    lhs = jnp.stack(
        [
            jnp.stack([real_p, -imag_p]),
            jnp.stack([imag_p, real_p]),
        ]
    )
    lhs = jnp.transpose(lhs, (4, 7, 0, 2, 5, 1, 3, 6)).reshape(
        t_local * q_local * 2, chunk * n_cuts * 2 * inner
    )
    second_w = jnp.take(
        w2_table.reshape(slice_count, 2 * inner, out_width), second_ids, axis=0
    ).reshape(chunk * n_cuts * 2 * inner, out_width)
    return jnp.dot(lhs, second_w, preferred_element_type=jnp.float32)


def regroup_kernel(stem_ref, weight_ref, second_ref, out_ref, real_ref, imag_ref):
    _, rows, _ = stem_ref.shape
    q_local = weight_ref.shape[2] // 64
    t_local = 16
    n_mode = rows // t_local
    b = pl.program_id(0)
    lane = lax.broadcasted_iota(jnp.int32, (t_local, 128), 1)
    low = lane < 64
    imag_lane = (lane // 16) % 2 == 1

    def store(row, col, tile):
        col = pl.ds(pl.multiple_of(col, 128), 128)
        real_ref[row:row + t_local, col] = jnp.where(imag_lane, -tile, tile)
        imag_ref[row:row + t_local, col] = jnp.where(
            imag_lane, pltpu.roll(tile, 16, 1), pltpu.roll(tile, 112, 1)
        )

    product = jnp.dot(
        stem_ref[0], weight_ref[0], preferred_element_type=jnp.float32
    ).astype(jnp.bfloat16)
    for pair in range(n_mode // 2):
        upper = product[(2 * pair) * t_local:(2 * pair + 1) * t_local]
        lower = product[(2 * pair + 1) * t_local:(2 * pair + 2) * t_local]
        col = (b * (n_mode // 2) + pair) * 128
        for qp in range(q_local // 2):
            first = upper[:, qp * 128:(qp + 1) * 128]
            second = lower[:, qp * 128:(qp + 1) * 128]
            store((2 * qp) * t_local, col, jnp.where(low, first, pltpu.roll(second, 64, 1)))
            store((2 * qp + 1) * t_local, col, jnp.where(low, pltpu.roll(first, 64, 1), second))

    @pl.when(b == pl.num_programs(0) - 1)
    def _():
        weights = second_ref[...]
        for part, lhs_ref in enumerate((real_ref, imag_ref)):
            result = jnp.dot(lhs_ref[...], weights, preferred_element_type=jnp.float32)
            for q in range(q_local):
                out_ref[:, q, part, :] = result[q * t_local:(q + 1) * t_local]


def regroup(stem_rows, first_w, second_w, q_local, t_local):
    block_count, rows, _ = stem_rows.shape
    n_mode = rows // t_local
    lhs_shape = (q_local * t_local, block_count * n_mode * 64)
    out_shape = jax.ShapeDtypeStruct(
        (t_local, q_local, 2, second_w.shape[1]), jnp.float32
    )
    flops = 2 * block_count * rows * first_w.shape[1] * first_w.shape[2]
    flops += 2 * 2 * lhs_shape[0] * lhs_shape[1] * second_w.shape[1]
    return pl.pallas_call(
        regroup_kernel,
        out_shape=out_shape,
        grid=(block_count,),
        in_specs=[
            pl.BlockSpec((1,) + stem_rows.shape[1:], lambda b: (b, 0, 0)),
            pl.BlockSpec((1,) + first_w.shape[1:], lambda b: (b, 0, 0)),
            pl.BlockSpec(second_w.shape, lambda b: (0, 0)),
        ],
        out_specs=pl.BlockSpec(out_shape.shape, lambda b: (0, 0, 0, 0)),
        scratch_shapes=[pltpu.VMEM(lhs_shape, jnp.bfloat16)] * 2,
        cost_estimate=pl.CostEstimate(
            flops=flops,
            transcendentals=0,
            bytes_accessed=2 * (stem_rows.size + first_w.size + second_w.size)
            + 4 * lhs_shape[0] * 2 * second_w.shape[1],
        ),
    )(stem_rows, first_w, second_w)

def stacked_part(stem_rows, first_t, w2_table, first_ids, second_ids, sizes):
    n_mode, t_local, n_cuts, a_count, q_local = sizes
    block_count = stem_rows.shape[0]
    width = first_t.shape[3]
    _, _, inner, out_width = w2_table.shape
    group = n_cuts * 2 * a_count
    picked = jnp.take(first_t, first_ids.reshape(-1), axis=0)
    picked = picked.reshape(block_count, n_cuts, 2, q_local, a_count, width)
    real_part, imag_part = picked[:, :, 0], picked[:, :, 1]
    first_w = jnp.stack(
        [jnp.stack([real_part, imag_part]), jnp.stack([-imag_part, real_part])]
    )
    first_w = jnp.transpose(first_w, (2, 4, 3, 1, 5, 0, 6)).reshape(
        block_count, q_local * group, 2 * width
    )
    if group == 64 and t_local == 16 and n_mode % 2 == 0 and q_local % 2 == 0:
        second = jnp.take(w2_table, second_ids.reshape(-1), axis=0)
        second = second.reshape(block_count, n_cuts, 2, n_mode, a_count, out_width)
        second_w = jnp.transpose(second, (0, 3, 1, 2, 4, 5)).reshape(
            block_count * n_mode * group, out_width
        )
        return regroup(stem_rows, jnp.swapaxes(first_w, 1, 2), second_w, q_local, t_local)
    else:
        second = jnp.take(w2_table, second_ids.reshape(-1), axis=0)
        second = jnp.swapaxes(second, 2, 3)
        second = second.reshape(block_count, n_cuts, 2, out_width, n_mode, a_count)
        real_two, imag_two = second[:, :, 0], second[:, :, 1]
        second_w = jnp.stack(
            [jnp.stack([real_two, -imag_two]), jnp.stack([imag_two, real_two])]
        )
        second_w = jnp.transpose(second_w, (0, 4, 2, 5, 3, 1, 6)).reshape(
            2 * out_width, block_count * n_mode * group
        )
        product = jnp.einsum(
            "brk,bnk->brn", stem_rows, first_w, preferred_element_type=jnp.float32
        ).astype(jnp.bfloat16)
        lhs = product.reshape(block_count, n_mode, t_local, q_local, group)
        lhs = jnp.transpose(lhs, (3, 2, 0, 1, 4)).reshape(
            q_local * t_local, block_count * n_mode * group
        )
        amplitude = jnp.einsum(
            "mk,nk->mn", lhs, second_w, preferred_element_type=jnp.float32
        )
    amplitude = amplitude.reshape(q_local, t_local, 2, out_width)
    return jnp.transpose(amplitude, (1, 0, 2, 3))


def on_device(stem_blocks, w1_table, w2_table, slice_ids, mode_perm):
    n_mode = lax.axis_size("mode")
    n_cuts = lax.axis_size("cuts")
    rows = stem_blocks.shape[1]
    width = stem_blocks.shape[3]
    mid = w1_table.shape[3]
    inner = w2_table.shape[2]
    out_width = w2_table.shape[3]
    block_count = slice_ids.shape[1]
    t_local = rows // n_mode
    a_count = inner // n_mode
    q_count = mid // a_count
    q_local = q_count // n_cuts
    me = lax.axis_index("cuts")
    sizes = (n_mode, t_local, n_cuts, a_count, q_local)

    pieces = stem_blocks[0].reshape(1, n_mode, t_local, 2 * width)
    payload = jnp.broadcast_to(pieces, (n_cuts, n_mode, t_local, 2 * width))
    payload = payload.reshape(n_cuts * n_mode, t_local, 2 * width)
    stem_rows = lax.all_to_all(payload, ("cuts", "mode"), 0, 0, tiled=True)
    stem_rows = stem_rows.reshape(block_count, n_mode * t_local, 2 * width)

    all_ids = gather_over_cuts(slice_ids[0], n_cuts)
    first_ids = all_ids[:, :, 0].T
    second_ids = all_ids[:, :, 1].T

    perm_grid = mode_perm.reshape(a_count, q_count)
    wanted = lax.dynamic_slice_in_dim(perm_grid, me * q_local, q_local, axis=1).reshape(-1)
    picker = (jnp.arange(mid, dtype=jnp.int32)[:, None] == wanted[None, :]).astype(w1_table.dtype)
    first_cols = jnp.einsum(
        "spkj,jn->spkn", w1_table, picker, preferred_element_type=jnp.float32
    ).astype(w1_table.dtype)
    real_part, imag_part = first_cols[:, 0], first_cols[:, 1]
    upper = jnp.concatenate([real_part, imag_part], axis=2)
    lower = jnp.concatenate([-imag_part, real_part], axis=2)
    first_all = jnp.concatenate([upper, lower], axis=1)

    if block_count * n_cuts <= 8:
        wanted_t = lax.dynamic_slice_in_dim(perm_grid, me * q_local, q_local, axis=1).T.reshape(-1)
        picker_t = (wanted_t[:, None] == jnp.arange(mid, dtype=jnp.int32)[None, :]).astype(w1_table.dtype)
        first_t = jnp.einsum(
            "nj,spkj->spnk", picker_t, w1_table, preferred_element_type=jnp.float32
        ).astype(w1_table.dtype)
        return stacked_part(stem_rows, first_t, w2_table, first_ids, second_ids, sizes)
    else:
        def one_block(index, running):
            stem_one = lax.dynamic_slice_in_dim(stem_rows, index, 1, axis=0)
            first_one = lax.dynamic_slice_in_dim(first_ids, index, 1, axis=0)
            second_one = lax.dynamic_slice_in_dim(second_ids, index, 1, axis=0)
            return running + blocks_part(
                stem_one, first_all, w2_table, first_one, second_one.reshape(-1), sizes
            )

        begin = jnp.zeros((t_local * q_local * 2, out_width), jnp.float32)
        amplitude = lax.fori_loop(0, block_count, one_block, begin)
    return amplitude.reshape(t_local, q_local, 2, out_width)


def solution(mesh):
    placed = (P("cuts", "mode", None, None), P(), P(), P("cuts", None, None), P())
    return jax.shard_map(
        on_device,
        mesh=mesh,
        in_specs=placed,
        out_specs=P("mode", "cuts", None, None),
        check_vma=False,
    )
```

```python
import jax
import jax.numpy as jnp
from jax import lax
from jax.experimental import pallas as pl
from jax.experimental.pallas import tpu as pltpu
from jax.sharding import PartitionSpec as P


def gather_over_cuts(own, n_cuts):
    pieces = [own]
    current = own
    ring = [(j, (j + 1) % n_cuts) for j in range(n_cuts)]
    for _ in range(1, n_cuts):
        current = lax.ppermute(current, "cuts", ring)
        pieces.append(current)
    stacked = jnp.stack(pieces)
    me = lax.axis_index("cuts")
    order = (me - jnp.arange(n_cuts, dtype=jnp.int32)) % n_cuts
    return jnp.take(stacked, order, axis=0)


def blocks_part(stem_rows, first_all, w2_table, first_ids, second_ids, sizes):
    n_mode, t_local, n_cuts, a_count, q_local = sizes
    chunk = stem_rows.shape[0]
    wide_in = stem_rows.shape[2]
    col_width = first_all.shape[2]
    slice_count, _, inner, out_width = w2_table.shape
    first_w = jnp.take(first_all, first_ids, axis=0)
    first_w = jnp.transpose(first_w, (0, 2, 1, 3)).reshape(
        chunk, wide_in, n_cuts * col_width
    )
    product = jnp.einsum(
        "bri,bio->bro", stem_rows, first_w, preferred_element_type=jnp.float32
    ).astype(jnp.bfloat16)
    split = product.reshape(chunk, n_mode, t_local, n_cuts, 2, a_count, q_local)
    real_p, imag_p = split[:, :, :, :, 0], split[:, :, :, :, 1]
    lhs = jnp.stack(
        [
            jnp.stack([real_p, -imag_p]),
            jnp.stack([imag_p, real_p]),
        ]
    )
    lhs = jnp.transpose(lhs, (4, 7, 0, 2, 5, 1, 3, 6)).reshape(
        t_local * q_local * 2, chunk * n_cuts * 2 * inner
    )
    second_w = jnp.take(
        w2_table.reshape(slice_count, 2 * inner, out_width), second_ids, axis=0
    ).reshape(chunk * n_cuts * 2 * inner, out_width)
    return jnp.dot(lhs, second_w, preferred_element_type=jnp.float32)


def regroup_kernel(stem_ref, weight_ref, second_ref, out_ref, real_ref, imag_ref):
    block_count, rows, _ = stem_ref.shape
    q_local = weight_ref.shape[2] // 64
    t_local = 16
    n_mode = rows // t_local
    lane = lax.broadcasted_iota(jnp.int32, (t_local, 128), 1)
    low = lane < 64
    imag_lane = (lane // 16) % 2 == 1

    def store(row, col, tile):
        real_ref[row:row + t_local, col:col + 128] = jnp.where(imag_lane, -tile, tile)
        imag_ref[row:row + t_local, col:col + 128] = jnp.where(
            imag_lane, pltpu.roll(tile, 16, 1), pltpu.roll(tile, 112, 1)
        )

    for b in range(block_count):
        product = jnp.dot(
            stem_ref[b], weight_ref[b], preferred_element_type=jnp.float32
        ).astype(jnp.bfloat16)
        for pair in range(n_mode // 2):
            upper = product[(2 * pair) * t_local:(2 * pair + 1) * t_local]
            lower = product[(2 * pair + 1) * t_local:(2 * pair + 2) * t_local]
            col = (b * n_mode // 2 + pair) * 128
            for qp in range(q_local // 2):
                first = upper[:, qp * 128:(qp + 1) * 128]
                second = lower[:, qp * 128:(qp + 1) * 128]
                store((2 * qp) * t_local, col, jnp.where(low, first, pltpu.roll(second, 64, 1)))
                store((2 * qp + 1) * t_local, col, jnp.where(low, pltpu.roll(first, 64, 1), second))
    weights = second_ref[...]
    real_out = jnp.dot(real_ref[...], weights, preferred_element_type=jnp.float32)
    imag_out = jnp.dot(imag_ref[...], weights, preferred_element_type=jnp.float32)
    for q in range(q_local):
        rows = slice(q * t_local, (q + 1) * t_local)
        out_ref[:, q] = jnp.stack([real_out[rows], imag_out[rows]], axis=1)


def regroup(stem_rows, first_w, second_w, q_local, t_local):
    block_count, rows, _ = stem_rows.shape
    n_mode = rows // t_local
    lhs_shape = (q_local * t_local, block_count * n_mode * 64)
    out_shape = jax.ShapeDtypeStruct(
        (t_local, q_local, 2, second_w.shape[1]), jnp.float32
    )
    flops = 2 * block_count * rows * first_w.shape[1] * first_w.shape[2]
    flops += 2 * 2 * lhs_shape[0] * lhs_shape[1] * second_w.shape[1]
    return pl.pallas_call(
        regroup_kernel,
        out_shape=out_shape,
        in_specs=[pl.BlockSpec(memory_space=pltpu.VMEM)] * 3,
        out_specs=pl.BlockSpec(memory_space=pltpu.VMEM),
        scratch_shapes=[pltpu.VMEM(lhs_shape, jnp.bfloat16)] * 2,
        cost_estimate=pl.CostEstimate(
            flops=flops,
            transcendentals=0,
            bytes_accessed=2 * (stem_rows.size + first_w.size + second_w.size)
            + 4 * lhs_shape[0] * 2 * second_w.shape[1],
        ),
    )(stem_rows, first_w, second_w)

def stacked_part(stem_rows, first_t, w2_table, first_ids, second_ids, sizes):
    n_mode, t_local, n_cuts, a_count, q_local = sizes
    block_count = stem_rows.shape[0]
    width = first_t.shape[3]
    _, _, inner, out_width = w2_table.shape
    group = n_cuts * 2 * a_count
    picked = jnp.take(first_t, first_ids.reshape(-1), axis=0)
    picked = picked.reshape(block_count, n_cuts, 2, q_local, a_count, width)
    real_part, imag_part = picked[:, :, 0], picked[:, :, 1]
    first_w = jnp.stack(
        [jnp.stack([real_part, imag_part]), jnp.stack([-imag_part, real_part])]
    )
    first_w = jnp.transpose(first_w, (2, 4, 3, 1, 5, 0, 6)).reshape(
        block_count, q_local * group, 2 * width
    )
    if group == 64 and t_local == 16 and n_mode % 2 == 0 and q_local % 2 == 0:
        second = jnp.take(w2_table, second_ids.reshape(-1), axis=0)
        second = second.reshape(block_count, n_cuts, 2, n_mode, a_count, out_width)
        second_w = jnp.transpose(second, (0, 3, 1, 2, 4, 5)).reshape(
            block_count * n_mode * group, out_width
        )
        return regroup(stem_rows, jnp.swapaxes(first_w, 1, 2), second_w, q_local, t_local)
    else:
        second = jnp.take(w2_table, second_ids.reshape(-1), axis=0)
        second = jnp.swapaxes(second, 2, 3)
        second = second.reshape(block_count, n_cuts, 2, out_width, n_mode, a_count)
        real_two, imag_two = second[:, :, 0], second[:, :, 1]
        second_w = jnp.stack(
            [jnp.stack([real_two, -imag_two]), jnp.stack([imag_two, real_two])]
        )
        second_w = jnp.transpose(second_w, (0, 4, 2, 5, 3, 1, 6)).reshape(
            2 * out_width, block_count * n_mode * group
        )
        product = jnp.einsum(
            "brk,bnk->brn", stem_rows, first_w, preferred_element_type=jnp.float32
        ).astype(jnp.bfloat16)
        lhs = product.reshape(block_count, n_mode, t_local, q_local, group)
        lhs = jnp.transpose(lhs, (3, 2, 0, 1, 4)).reshape(
            q_local * t_local, block_count * n_mode * group
        )
        amplitude = jnp.einsum(
            "mk,nk->mn", lhs, second_w, preferred_element_type=jnp.float32
        )
    amplitude = amplitude.reshape(q_local, t_local, 2, out_width)
    return jnp.transpose(amplitude, (1, 0, 2, 3))


def on_device(stem_blocks, w1_table, w2_table, slice_ids, mode_perm):
    n_mode = lax.axis_size("mode")
    n_cuts = lax.axis_size("cuts")
    rows = stem_blocks.shape[1]
    width = stem_blocks.shape[3]
    mid = w1_table.shape[3]
    inner = w2_table.shape[2]
    out_width = w2_table.shape[3]
    block_count = slice_ids.shape[1]
    t_local = rows // n_mode
    a_count = inner // n_mode
    q_count = mid // a_count
    q_local = q_count // n_cuts
    me = lax.axis_index("cuts")
    sizes = (n_mode, t_local, n_cuts, a_count, q_local)

    pieces = stem_blocks[0].reshape(1, n_mode, t_local, 2 * width)
    payload = jnp.broadcast_to(pieces, (n_cuts, n_mode, t_local, 2 * width))
    payload = payload.reshape(n_cuts * n_mode, t_local, 2 * width)
    stem_rows = lax.all_to_all(payload, ("cuts", "mode"), 0, 0, tiled=True)
    stem_rows = stem_rows.reshape(block_count, n_mode * t_local, 2 * width)

    all_ids = gather_over_cuts(slice_ids[0], n_cuts)
    first_ids = all_ids[:, :, 0].T
    second_ids = all_ids[:, :, 1].T

    perm_grid = mode_perm.reshape(a_count, q_count)
    wanted = lax.dynamic_slice_in_dim(perm_grid, me * q_local, q_local, axis=1).reshape(-1)
    picker = (jnp.arange(mid, dtype=jnp.int32)[:, None] == wanted[None, :]).astype(w1_table.dtype)
    first_cols = jnp.einsum(
        "spkj,jn->spkn", w1_table, picker, preferred_element_type=jnp.float32
    ).astype(w1_table.dtype)
    real_part, imag_part = first_cols[:, 0], first_cols[:, 1]
    upper = jnp.concatenate([real_part, imag_part], axis=2)
    lower = jnp.concatenate([-imag_part, real_part], axis=2)
    first_all = jnp.concatenate([upper, lower], axis=1)

    if block_count * n_cuts <= 8:
        wanted_t = lax.dynamic_slice_in_dim(perm_grid, me * q_local, q_local, axis=1).T.reshape(-1)
        picker_t = (wanted_t[:, None] == jnp.arange(mid, dtype=jnp.int32)[None, :]).astype(w1_table.dtype)
        first_t = jnp.einsum(
            "nj,spkj->spnk", picker_t, w1_table, preferred_element_type=jnp.float32
        ).astype(w1_table.dtype)
        return stacked_part(stem_rows, first_t, w2_table, first_ids, second_ids, sizes)
    else:
        def one_block(index, running):
            stem_one = lax.dynamic_slice_in_dim(stem_rows, index, 1, axis=0)
            first_one = lax.dynamic_slice_in_dim(first_ids, index, 1, axis=0)
            second_one = lax.dynamic_slice_in_dim(second_ids, index, 1, axis=0)
            return running + blocks_part(
                stem_one, first_all, w2_table, first_one, second_one.reshape(-1), sizes
            )

        begin = jnp.zeros((t_local * q_local * 2, out_width), jnp.float32)
        amplitude = lax.fori_loop(0, block_count, one_block, begin)
    return amplitude.reshape(t_local, q_local, 2, out_width)


def solution(mesh):
    placed = (P("cuts", "mode", None, None), P(), P(), P("cuts", None, None), P())
    return jax.shard_map(
        on_device,
        mesh=mesh,
        in_specs=placed,
        out_specs=P("mode", "cuts", None, None),
        check_vma=False,
    )
```

```python
import jax
import jax.numpy as jnp
from jax import lax
from jax.experimental import pallas as pl
from jax.experimental.pallas import tpu as pltpu
from jax.sharding import PartitionSpec as P


def gather_over_cuts(own, n_cuts):
    pieces = [own]
    current = own
    ring = [(j, (j + 1) % n_cuts) for j in range(n_cuts)]
    for _ in range(1, n_cuts):
        current = lax.ppermute(current, "cuts", ring)
        pieces.append(current)
    stacked = jnp.stack(pieces)
    me = lax.axis_index("cuts")
    order = (me - jnp.arange(n_cuts, dtype=jnp.int32)) % n_cuts
    return jnp.take(stacked, order, axis=0)


def blocks_part(stem_rows, first_all, w2_table, first_ids, second_ids, sizes):
    n_mode, t_local, n_cuts, a_count, q_local = sizes
    chunk = stem_rows.shape[0]
    wide_in = stem_rows.shape[2]
    col_width = first_all.shape[2]
    slice_count, _, inner, out_width = w2_table.shape
    first_w = jnp.take(first_all, first_ids, axis=0)
    first_w = jnp.transpose(first_w, (0, 2, 1, 3)).reshape(
        chunk, wide_in, n_cuts * col_width
    )
    product = jnp.einsum(
        "bri,bio->bro", stem_rows, first_w, preferred_element_type=jnp.float32
    ).astype(jnp.bfloat16)
    split = product.reshape(chunk, n_mode, t_local, n_cuts, 2, a_count, q_local)
    real_p, imag_p = split[:, :, :, :, 0], split[:, :, :, :, 1]
    lhs = jnp.stack(
        [
            jnp.stack([real_p, -imag_p]),
            jnp.stack([imag_p, real_p]),
        ]
    )
    lhs = jnp.transpose(lhs, (4, 7, 0, 2, 5, 1, 3, 6)).reshape(
        t_local * q_local * 2, chunk * n_cuts * 2 * inner
    )
    second_w = jnp.take(
        w2_table.reshape(slice_count, 2 * inner, out_width), second_ids, axis=0
    ).reshape(chunk * n_cuts * 2 * inner, out_width)
    return jnp.dot(lhs, second_w, preferred_element_type=jnp.float32)


def regroup_kernel(stem_ref, weight_ref, second_ref, out_ref, real_ref, imag_ref):
    block_count, rows, _ = stem_ref.shape
    q_local = weight_ref.shape[2] // 64
    t_local = 16
    n_mode = rows // t_local
    lane = lax.broadcasted_iota(jnp.int32, (t_local, 128), 1)
    low = lane < 64
    imag_lane = (lane // 16) % 2 == 1

    def store(row, col, tile):
        real_ref[row:row + t_local, col:col + 128] = jnp.where(imag_lane, -tile, tile)
        imag_ref[row:row + t_local, col:col + 128] = jnp.where(
            imag_lane, pltpu.roll(tile, 16, 1), pltpu.roll(tile, 112, 1)
        )

    for b in range(block_count):
        width = weight_ref.shape[1]
        from_real = jnp.dot(
            stem_ref[b, :, :width], weight_ref[b], preferred_element_type=jnp.float32
        )
        from_imag = jnp.dot(
            stem_ref[b, :, width:], weight_ref[b], preferred_element_type=jnp.float32
        )
        wide_lane = lax.broadcasted_iota(jnp.int32, from_imag.shape, 1)
        second_group = (wide_lane // 16) % 2 == 1
        product = from_real + jnp.where(
            second_group, pltpu.roll(from_imag, 16, 1), -pltpu.roll(from_imag, 496, 1)
        )
        product = product.astype(jnp.bfloat16)
        for pair in range(n_mode // 2):
            upper = product[(2 * pair) * t_local:(2 * pair + 1) * t_local]
            lower = product[(2 * pair + 1) * t_local:(2 * pair + 2) * t_local]
            col = (b * n_mode // 2 + pair) * 128
            for qp in range(q_local // 2):
                first = upper[:, qp * 128:(qp + 1) * 128]
                second = lower[:, qp * 128:(qp + 1) * 128]
                store((2 * qp) * t_local, col, jnp.where(low, first, pltpu.roll(second, 64, 1)))
                store((2 * qp + 1) * t_local, col, jnp.where(low, pltpu.roll(first, 64, 1), second))
    weights = second_ref[...]
    for part, lhs_ref in enumerate((real_ref, imag_ref)):
        result = jnp.dot(lhs_ref[...], weights, preferred_element_type=jnp.float32)
        for q in range(q_local):
            out_ref[:, q, part, :] = result[q * t_local:(q + 1) * t_local]


def regroup(stem_rows, first_w, second_w, q_local, t_local):
    block_count, rows, _ = stem_rows.shape
    n_mode = rows // t_local
    lhs_shape = (q_local * t_local, block_count * n_mode * 64)
    out_shape = jax.ShapeDtypeStruct(
        (t_local, q_local, 2, second_w.shape[1]), jnp.float32
    )
    flops = 2 * block_count * rows * first_w.shape[1] * first_w.shape[2]
    flops += 2 * 2 * lhs_shape[0] * lhs_shape[1] * second_w.shape[1]
    return pl.pallas_call(
        regroup_kernel,
        out_shape=out_shape,
        in_specs=[pl.BlockSpec(memory_space=pltpu.VMEM)] * 3,
        out_specs=pl.BlockSpec(memory_space=pltpu.VMEM),
        scratch_shapes=[pltpu.VMEM(lhs_shape, jnp.bfloat16)] * 2,
        compiler_params=pltpu.CompilerParams(vmem_limit_bytes=16 * 1024 * 1024),
        cost_estimate=pl.CostEstimate(
            flops=flops,
            transcendentals=0,
            bytes_accessed=2 * (stem_rows.size + first_w.size + second_w.size)
            + 4 * lhs_shape[0] * 2 * second_w.shape[1],
        ),
    )(stem_rows, first_w, second_w)

def stacked_part(stem_rows, first_t, w2_table, first_ids, second_ids, sizes):
    n_mode, t_local, n_cuts, a_count, q_local = sizes
    block_count = stem_rows.shape[0]
    width = first_t.shape[3]
    _, _, inner, out_width = w2_table.shape
    group = n_cuts * 2 * a_count
    picked = jnp.take(first_t, first_ids.reshape(-1), axis=0)
    picked = picked.reshape(block_count, n_cuts, 2, q_local, a_count, width)
    real_part, imag_part = picked[:, :, 0], picked[:, :, 1]
    first_w = jnp.stack(
        [jnp.stack([real_part, imag_part]), jnp.stack([-imag_part, real_part])]
    )
    first_w = jnp.transpose(first_w, (2, 4, 3, 1, 5, 0, 6)).reshape(
        block_count, q_local * group, 2 * width
    )
    if group == 64 and t_local == 16 and n_mode % 2 == 0 and q_local % 2 == 0:
        second = jnp.take(w2_table, second_ids.reshape(-1), axis=0)
        second = second.reshape(block_count, n_cuts, 2, n_mode, a_count, out_width)
        second_w = jnp.transpose(second, (0, 3, 1, 2, 4, 5)).reshape(
            block_count * n_mode * group, out_width
        )
        first_half = jnp.transpose(picked, (0, 5, 3, 1, 2, 4)).reshape(
            block_count, width, q_local * group
        )
        return regroup(stem_rows, first_half, second_w, q_local, t_local)
    else:
        second = jnp.take(w2_table, second_ids.reshape(-1), axis=0)
        second = jnp.swapaxes(second, 2, 3)
        second = second.reshape(block_count, n_cuts, 2, out_width, n_mode, a_count)
        real_two, imag_two = second[:, :, 0], second[:, :, 1]
        second_w = jnp.stack(
            [jnp.stack([real_two, -imag_two]), jnp.stack([imag_two, real_two])]
        )
        second_w = jnp.transpose(second_w, (0, 4, 2, 5, 3, 1, 6)).reshape(
            2 * out_width, block_count * n_mode * group
        )
        product = jnp.einsum(
            "brk,bnk->brn", stem_rows, first_w, preferred_element_type=jnp.float32
        ).astype(jnp.bfloat16)
        lhs = product.reshape(block_count, n_mode, t_local, q_local, group)
        lhs = jnp.transpose(lhs, (3, 2, 0, 1, 4)).reshape(
            q_local * t_local, block_count * n_mode * group
        )
        amplitude = jnp.einsum(
            "mk,nk->mn", lhs, second_w, preferred_element_type=jnp.float32
        )
    amplitude = amplitude.reshape(q_local, t_local, 2, out_width)
    return jnp.transpose(amplitude, (1, 0, 2, 3))


def on_device(stem_blocks, w1_table, w2_table, slice_ids, mode_perm):
    n_mode = lax.axis_size("mode")
    n_cuts = lax.axis_size("cuts")
    rows = stem_blocks.shape[1]
    width = stem_blocks.shape[3]
    mid = w1_table.shape[3]
    inner = w2_table.shape[2]
    out_width = w2_table.shape[3]
    block_count = slice_ids.shape[1]
    t_local = rows // n_mode
    a_count = inner // n_mode
    q_count = mid // a_count
    q_local = q_count // n_cuts
    me = lax.axis_index("cuts")
    sizes = (n_mode, t_local, n_cuts, a_count, q_local)

    pieces = stem_blocks[0].reshape(1, n_mode, t_local, 2 * width)
    payload = jnp.broadcast_to(pieces, (n_cuts, n_mode, t_local, 2 * width))
    payload = payload.reshape(n_cuts * n_mode, t_local, 2 * width)
    stem_rows = lax.all_to_all(payload, ("cuts", "mode"), 0, 0, tiled=True)
    stem_rows = stem_rows.reshape(block_count, n_mode * t_local, 2 * width)

    all_ids = gather_over_cuts(slice_ids[0], n_cuts)
    first_ids = all_ids[:, :, 0].T
    second_ids = all_ids[:, :, 1].T

    perm_grid = mode_perm.reshape(a_count, q_count)
    wanted = lax.dynamic_slice_in_dim(perm_grid, me * q_local, q_local, axis=1).reshape(-1)
    picker = (jnp.arange(mid, dtype=jnp.int32)[:, None] == wanted[None, :]).astype(w1_table.dtype)
    first_cols = jnp.einsum(
        "spkj,jn->spkn", w1_table, picker, preferred_element_type=jnp.float32
    ).astype(w1_table.dtype)
    real_part, imag_part = first_cols[:, 0], first_cols[:, 1]
    upper = jnp.concatenate([real_part, imag_part], axis=2)
    lower = jnp.concatenate([-imag_part, real_part], axis=2)
    first_all = jnp.concatenate([upper, lower], axis=1)

    if block_count * n_cuts <= 8:
        wanted_t = lax.dynamic_slice_in_dim(perm_grid, me * q_local, q_local, axis=1).T.reshape(-1)
        picker_t = (wanted_t[:, None] == jnp.arange(mid, dtype=jnp.int32)[None, :]).astype(w1_table.dtype)
        first_t = jnp.einsum(
            "nj,spkj->spnk", picker_t, w1_table, preferred_element_type=jnp.float32
        ).astype(w1_table.dtype)
        return stacked_part(stem_rows, first_t, w2_table, first_ids, second_ids, sizes)
    else:
        def one_block(index, running):
            stem_one = lax.dynamic_slice_in_dim(stem_rows, index, 1, axis=0)
            first_one = lax.dynamic_slice_in_dim(first_ids, index, 1, axis=0)
            second_one = lax.dynamic_slice_in_dim(second_ids, index, 1, axis=0)
            return running + blocks_part(
                stem_one, first_all, w2_table, first_one, second_one.reshape(-1), sizes
            )

        begin = jnp.zeros((t_local * q_local * 2, out_width), jnp.float32)
        amplitude = lax.fori_loop(0, block_count, one_block, begin)
    return amplitude.reshape(t_local, q_local, 2, out_width)


def solution(mesh):
    placed = (P("cuts", "mode", None, None), P(), P(), P("cuts", None, None), P())
    return jax.shard_map(
        on_device,
        mesh=mesh,
        in_specs=placed,
        out_specs=P("mode", "cuts", None, None),
        check_vma=False,
    )
```

```python
import jax
import jax.numpy as jnp
from jax import lax
from jax.experimental import pallas as pl
from jax.experimental.pallas import tpu as pltpu
from jax.sharding import PartitionSpec as P


def gather_over_cuts(own, n_cuts):
    pieces = [own]
    current = own
    ring = [(j, (j + 1) % n_cuts) for j in range(n_cuts)]
    for _ in range(1, n_cuts):
        current = lax.ppermute(current, "cuts", ring)
        pieces.append(current)
    stacked = jnp.stack(pieces)
    me = lax.axis_index("cuts")
    order = (me - jnp.arange(n_cuts, dtype=jnp.int32)) % n_cuts
    return jnp.take(stacked, order, axis=0)


def blocks_part(stem_rows, first_all, w2_table, first_ids, second_ids, sizes):
    n_mode, t_local, n_cuts, a_count, q_local = sizes
    chunk = stem_rows.shape[0]
    wide_in = stem_rows.shape[2]
    col_width = first_all.shape[2]
    slice_count, _, inner, out_width = w2_table.shape
    first_w = jnp.take(first_all, first_ids, axis=0)
    first_w = jnp.transpose(first_w, (0, 2, 1, 3)).reshape(
        chunk, wide_in, n_cuts * col_width
    )
    product = jnp.einsum(
        "bri,bio->bro", stem_rows, first_w, preferred_element_type=jnp.float32
    ).astype(jnp.bfloat16)
    split = product.reshape(chunk, n_mode, t_local, n_cuts, 2, a_count, q_local)
    real_p, imag_p = split[:, :, :, :, 0], split[:, :, :, :, 1]
    lhs = jnp.stack(
        [
            jnp.stack([real_p, -imag_p]),
            jnp.stack([imag_p, real_p]),
        ]
    )
    lhs = jnp.transpose(lhs, (4, 7, 0, 2, 5, 1, 3, 6)).reshape(
        t_local * q_local * 2, chunk * n_cuts * 2 * inner
    )
    second_w = jnp.take(
        w2_table.reshape(slice_count, 2 * inner, out_width), second_ids, axis=0
    ).reshape(chunk * n_cuts * 2 * inner, out_width)
    return jnp.dot(lhs, second_w, preferred_element_type=jnp.float32)


def regroup_kernel(stem_ref, weight_ref, second_ref, out_ref, real_ref, imag_ref):
    block_count, rows, _ = stem_ref.shape
    q_local = weight_ref.shape[2] // 64
    t_local = 16
    n_mode = rows // t_local
    lane = lax.broadcasted_iota(jnp.int32, (t_local, 128), 1)
    low = lane < 64
    imag_lane = (lane // 16) % 2 == 1

    def store(row, col, tile):
        real_ref[row:row + t_local, col:col + 128] = jnp.where(imag_lane, -tile, tile)
        imag_ref[row:row + t_local, col:col + 128] = jnp.where(
            imag_lane, pltpu.roll(tile, 16, 1), pltpu.roll(tile, 112, 1)
        )

    for b in range(block_count):
        product = jnp.dot(
            stem_ref[b], weight_ref[b], preferred_element_type=jnp.float32
        ).astype(jnp.bfloat16)
        for pair in range(n_mode // 2):
            upper = product[(2 * pair) * t_local:(2 * pair + 1) * t_local]
            lower = product[(2 * pair + 1) * t_local:(2 * pair + 2) * t_local]
            col = (b * n_mode // 2 + pair) * 128
            for qp in range(q_local // 2):
                first = upper[:, qp * 128:(qp + 1) * 128]
                second = lower[:, qp * 128:(qp + 1) * 128]
                store((2 * qp) * t_local, col, jnp.where(low, first, pltpu.roll(second, 64, 1)))
                store((2 * qp + 1) * t_local, col, jnp.where(low, pltpu.roll(first, 64, 1), second))
    weights = second_ref[...]
    for part, lhs_ref in enumerate((real_ref, imag_ref)):
        result = jnp.dot(lhs_ref[...], weights, preferred_element_type=jnp.float32)
        for q in range(q_local):
            out_ref[:, q, part, :] = result[q * t_local:(q + 1) * t_local]


def regroup(stem_rows, first_w, second_w, q_local, t_local):
    block_count, rows, _ = stem_rows.shape
    n_mode = rows // t_local
    lhs_shape = (q_local * t_local, block_count * n_mode * 64)
    out_shape = jax.ShapeDtypeStruct(
        (t_local, q_local, 2, second_w.shape[1]), jnp.float32
    )
    flops = 2 * block_count * rows * first_w.shape[1] * first_w.shape[2]
    flops += 2 * 2 * lhs_shape[0] * lhs_shape[1] * second_w.shape[1]
    return pl.pallas_call(
        regroup_kernel,
        out_shape=out_shape,
        in_specs=[pl.BlockSpec(memory_space=pltpu.VMEM)] * 3,
        out_specs=pl.BlockSpec(memory_space=pltpu.VMEM),
        scratch_shapes=[pltpu.VMEM(lhs_shape, jnp.bfloat16)] * 2,
        cost_estimate=pl.CostEstimate(
            flops=flops,
            transcendentals=0,
            bytes_accessed=2 * (stem_rows.size + first_w.size + second_w.size)
            + 4 * lhs_shape[0] * 2 * second_w.shape[1],
        ),
    )(stem_rows, first_w, second_w)

def stacked_part(stem_rows, first_t, w2_table, first_ids, second_ids, sizes):
    n_mode, t_local, n_cuts, a_count, q_local = sizes
    block_count = stem_rows.shape[0]
    width = first_t.shape[3]
    _, _, inner, out_width = w2_table.shape
    group = n_cuts * 2 * a_count
    picked = jnp.take(first_t, first_ids.reshape(-1), axis=0)
    picked = picked.reshape(block_count, n_cuts, 2, q_local, a_count, width)
    real_part, imag_part = picked[:, :, 0], picked[:, :, 1]
    first_w = jnp.stack(
        [jnp.stack([real_part, imag_part]), jnp.stack([-imag_part, real_part])]
    )
    first_w = jnp.transpose(first_w, (2, 4, 3, 1, 5, 0, 6)).reshape(
        block_count, q_local * group, 2 * width
    )
    if group == 64 and t_local == 16 and n_mode % 2 == 0 and q_local % 2 == 0:
        second = jnp.take(w2_table, second_ids.reshape(-1), axis=0)
        second = second.reshape(block_count, n_cuts, 2, n_mode, a_count, out_width)
        second_w = jnp.transpose(second, (0, 3, 1, 2, 4, 5)).reshape(
            block_count * n_mode * group, out_width
        )
        return regroup(stem_rows, jnp.swapaxes(first_w, 1, 2), second_w, q_local, t_local)
    else:
        second = jnp.take(w2_table, second_ids.reshape(-1), axis=0)
        second = jnp.swapaxes(second, 2, 3)
        second = second.reshape(block_count, n_cuts, 2, out_width, n_mode, a_count)
        real_two, imag_two = second[:, :, 0], second[:, :, 1]
        second_w = jnp.stack(
            [jnp.stack([real_two, -imag_two]), jnp.stack([imag_two, real_two])]
        )
        second_w = jnp.transpose(second_w, (0, 4, 2, 5, 3, 1, 6)).reshape(
            2 * out_width, block_count * n_mode * group
        )
        product = jnp.einsum(
            "brk,bnk->brn", stem_rows, first_w, preferred_element_type=jnp.float32
        ).astype(jnp.bfloat16)
        lhs = product.reshape(block_count, n_mode, t_local, q_local, group)
        lhs = jnp.transpose(lhs, (3, 2, 0, 1, 4)).reshape(
            q_local * t_local, block_count * n_mode * group
        )
        amplitude = jnp.einsum(
            "mk,nk->mn", lhs, second_w, preferred_element_type=jnp.float32
        )
    amplitude = amplitude.reshape(q_local, t_local, 2, out_width)
    return jnp.transpose(amplitude, (1, 0, 2, 3))


def on_device(stem_blocks, w1_table, w2_table, slice_ids, mode_perm):
    n_mode = lax.axis_size("mode")
    n_cuts = lax.axis_size("cuts")
    rows = stem_blocks.shape[1]
    width = stem_blocks.shape[3]
    mid = w1_table.shape[3]
    inner = w2_table.shape[2]
    out_width = w2_table.shape[3]
    block_count = slice_ids.shape[1]
    t_local = rows // n_mode
    a_count = inner // n_mode
    q_count = mid // a_count
    q_local = q_count // n_cuts
    me = lax.axis_index("cuts")
    sizes = (n_mode, t_local, n_cuts, a_count, q_local)

    pieces = stem_blocks[0].reshape(1, n_mode, t_local, 2 * width)
    payload = jnp.broadcast_to(pieces, (n_cuts, n_mode, t_local, 2 * width))
    payload = payload.reshape(n_cuts * n_mode, t_local, 2 * width)
    stem_rows = lax.all_to_all(payload, ("cuts", "mode"), 0, 0, tiled=True)
    stem_rows = stem_rows.reshape(block_count, n_mode * t_local, 2 * width)

    tie = (payload[0, 0, 0] * 0).astype(slice_ids.dtype)
    all_ids = gather_over_cuts(slice_ids[0] + tie, n_cuts)
    first_ids = all_ids[:, :, 0].T
    second_ids = all_ids[:, :, 1].T

    perm_grid = mode_perm.reshape(a_count, q_count)
    wanted = lax.dynamic_slice_in_dim(perm_grid, me * q_local, q_local, axis=1).reshape(-1)
    picker = (jnp.arange(mid, dtype=jnp.int32)[:, None] == wanted[None, :]).astype(w1_table.dtype)
    first_cols = jnp.einsum(
        "spkj,jn->spkn", w1_table, picker, preferred_element_type=jnp.float32
    ).astype(w1_table.dtype)
    real_part, imag_part = first_cols[:, 0], first_cols[:, 1]
    upper = jnp.concatenate([real_part, imag_part], axis=2)
    lower = jnp.concatenate([-imag_part, real_part], axis=2)
    first_all = jnp.concatenate([upper, lower], axis=1)

    if block_count * n_cuts <= 8:
        wanted_t = lax.dynamic_slice_in_dim(perm_grid, me * q_local, q_local, axis=1).T.reshape(-1)
        picker_t = (wanted_t[:, None] == jnp.arange(mid, dtype=jnp.int32)[None, :]).astype(w1_table.dtype)
        first_t = jnp.einsum(
            "nj,spkj->spnk", picker_t, w1_table, preferred_element_type=jnp.float32
        ).astype(w1_table.dtype)
        return stacked_part(stem_rows, first_t, w2_table, first_ids, second_ids, sizes)
    else:
        def one_block(index, running):
            stem_one = lax.dynamic_slice_in_dim(stem_rows, index, 1, axis=0)
            first_one = lax.dynamic_slice_in_dim(first_ids, index, 1, axis=0)
            second_one = lax.dynamic_slice_in_dim(second_ids, index, 1, axis=0)
            return running + blocks_part(
                stem_one, first_all, w2_table, first_one, second_one.reshape(-1), sizes
            )

        begin = jnp.zeros((t_local * q_local * 2, out_width), jnp.float32)
        amplitude = lax.fori_loop(0, block_count, one_block, begin)
    return amplitude.reshape(t_local, q_local, 2, out_width)


def solution(mesh):
    placed = (P("cuts", "mode", None, None), P(), P(), P("cuts", None, None), P())
    return jax.shard_map(
        on_device,
        mesh=mesh,
        in_specs=placed,
        out_specs=P("mode", "cuts", None, None),
        check_vma=False,
    )
```

```python
import jax
import jax.numpy as jnp
from jax import lax
from jax.experimental import pallas as pl
from jax.experimental.pallas import tpu as pltpu
from jax.sharding import PartitionSpec as P


def gather_over_cuts(own, n_cuts):
    pieces = [own]
    current = own
    ring = [(j, (j + 1) % n_cuts) for j in range(n_cuts)]
    for _ in range(1, n_cuts):
        current = lax.ppermute(current, "cuts", ring)
        pieces.append(current)
    stacked = jnp.stack(pieces)
    me = lax.axis_index("cuts")
    order = (me - jnp.arange(n_cuts, dtype=jnp.int32)) % n_cuts
    return jnp.take(stacked, order, axis=0)


def blocks_part(stem_rows, first_all, w2_table, first_ids, second_ids, sizes):
    n_mode, t_local, n_cuts, a_count, q_local = sizes
    chunk = stem_rows.shape[0]
    wide_in = stem_rows.shape[2]
    col_width = first_all.shape[2]
    slice_count, _, inner, out_width = w2_table.shape
    first_w = jnp.take(first_all, first_ids, axis=0)
    first_w = jnp.transpose(first_w, (0, 2, 1, 3)).reshape(
        chunk, wide_in, n_cuts * col_width
    )
    product = jnp.einsum(
        "bri,bio->bro", stem_rows, first_w, preferred_element_type=jnp.float32
    ).astype(jnp.bfloat16)
    split = product.reshape(chunk, n_mode, t_local, n_cuts, 2, a_count, q_local)
    real_p, imag_p = split[:, :, :, :, 0], split[:, :, :, :, 1]
    lhs = jnp.stack(
        [
            jnp.stack([real_p, -imag_p]),
            jnp.stack([imag_p, real_p]),
        ]
    )
    lhs = jnp.transpose(lhs, (4, 7, 0, 2, 5, 1, 3, 6)).reshape(
        t_local * q_local * 2, chunk * n_cuts * 2 * inner
    )
    second_w = jnp.take(
        w2_table.reshape(slice_count, 2 * inner, out_width), second_ids, axis=0
    ).reshape(chunk * n_cuts * 2 * inner, out_width)
    return jnp.dot(lhs, second_w, preferred_element_type=jnp.float32)


def regroup_kernel(stem_ref, weight_ref, second_ref, out_ref, real_ref, imag_ref):
    block_count, rows, _ = stem_ref.shape
    q_local = weight_ref.shape[1] // 64
    t_local = 16
    n_mode = rows // t_local
    lane = lax.broadcasted_iota(jnp.int32, (t_local, 128), 1)
    low = lane < 64
    imag_lane = (lane // 16) % 2 == 1

    def store(row, col, tile):
        real_ref[row:row + t_local, col:col + 128] = jnp.where(imag_lane, -tile, tile)
        imag_ref[row:row + t_local, col:col + 128] = jnp.where(
            imag_lane, pltpu.roll(tile, 16, 1), pltpu.roll(tile, 112, 1)
        )

    for b in range(block_count):
        product = lax.dot_general(
            stem_ref[b], weight_ref[b], (((1,), (1,)), ((), ())),
            preferred_element_type=jnp.float32,
        ).astype(jnp.bfloat16)
        for pair in range(n_mode // 2):
            upper = product[(2 * pair) * t_local:(2 * pair + 1) * t_local]
            lower = product[(2 * pair + 1) * t_local:(2 * pair + 2) * t_local]
            col = (b * n_mode // 2 + pair) * 128
            for qp in range(q_local // 2):
                first = upper[:, qp * 128:(qp + 1) * 128]
                second = lower[:, qp * 128:(qp + 1) * 128]
                store((2 * qp) * t_local, col, jnp.where(low, first, pltpu.roll(second, 64, 1)))
                store((2 * qp + 1) * t_local, col, jnp.where(low, pltpu.roll(first, 64, 1), second))
    weights = second_ref[...]
    for part, lhs_ref in enumerate((real_ref, imag_ref)):
        result = jnp.dot(lhs_ref[...], weights, preferred_element_type=jnp.float32)
        for q in range(q_local):
            out_ref[:, q, part, :] = result[q * t_local:(q + 1) * t_local]


def regroup(stem_rows, first_w, second_w, q_local, t_local):
    block_count, rows, _ = stem_rows.shape
    n_mode = rows // t_local
    lhs_shape = (q_local * t_local, block_count * n_mode * 64)
    out_shape = jax.ShapeDtypeStruct(
        (t_local, q_local, 2, second_w.shape[1]), jnp.float32
    )
    flops = 2 * block_count * rows * first_w.shape[1] * first_w.shape[2]
    flops += 2 * 2 * lhs_shape[0] * lhs_shape[1] * second_w.shape[1]
    return pl.pallas_call(
        regroup_kernel,
        out_shape=out_shape,
        in_specs=[pl.BlockSpec(memory_space=pltpu.VMEM)] * 3,
        out_specs=pl.BlockSpec(memory_space=pltpu.VMEM),
        scratch_shapes=[pltpu.VMEM(lhs_shape, jnp.bfloat16)] * 2,
        cost_estimate=pl.CostEstimate(
            flops=flops,
            transcendentals=0,
            bytes_accessed=2 * (stem_rows.size + first_w.size + second_w.size)
            + 4 * lhs_shape[0] * 2 * second_w.shape[1],
        ),
    )(stem_rows, first_w, second_w)

def stacked_part(stem_rows, first_t, w2_table, first_ids, second_ids, sizes):
    n_mode, t_local, n_cuts, a_count, q_local = sizes
    block_count = stem_rows.shape[0]
    width = first_t.shape[3]
    _, _, inner, out_width = w2_table.shape
    group = n_cuts * 2 * a_count
    picked = jnp.take(first_t, first_ids.reshape(-1), axis=0)
    picked = picked.reshape(block_count, n_cuts, 2, q_local, a_count, width)
    real_part, imag_part = picked[:, :, 0], picked[:, :, 1]
    first_w = jnp.stack(
        [jnp.stack([real_part, imag_part]), jnp.stack([-imag_part, real_part])]
    )
    first_w = jnp.transpose(first_w, (2, 4, 3, 1, 5, 0, 6)).reshape(
        block_count, q_local * group, 2 * width
    )
    if group == 64 and t_local == 16 and n_mode % 2 == 0 and q_local % 2 == 0:
        second = jnp.take(w2_table, second_ids.reshape(-1), axis=0)
        second = second.reshape(block_count, n_cuts, 2, n_mode, a_count, out_width)
        second_w = jnp.transpose(second, (0, 3, 1, 2, 4, 5)).reshape(
            block_count * n_mode * group, out_width
        )
        return regroup(stem_rows, first_w, second_w, q_local, t_local)
    else:
        second = jnp.take(w2_table, second_ids.reshape(-1), axis=0)
        second = jnp.swapaxes(second, 2, 3)
        second = second.reshape(block_count, n_cuts, 2, out_width, n_mode, a_count)
        real_two, imag_two = second[:, :, 0], second[:, :, 1]
        second_w = jnp.stack(
            [jnp.stack([real_two, -imag_two]), jnp.stack([imag_two, real_two])]
        )
        second_w = jnp.transpose(second_w, (0, 4, 2, 5, 3, 1, 6)).reshape(
            2 * out_width, block_count * n_mode * group
        )
        product = jnp.einsum(
            "brk,bnk->brn", stem_rows, first_w, preferred_element_type=jnp.float32
        ).astype(jnp.bfloat16)
        lhs = product.reshape(block_count, n_mode, t_local, q_local, group)
        lhs = jnp.transpose(lhs, (3, 2, 0, 1, 4)).reshape(
            q_local * t_local, block_count * n_mode * group
        )
        amplitude = jnp.einsum(
            "mk,nk->mn", lhs, second_w, preferred_element_type=jnp.float32
        )
    amplitude = amplitude.reshape(q_local, t_local, 2, out_width)
    return jnp.transpose(amplitude, (1, 0, 2, 3))


def on_device(stem_blocks, w1_table, w2_table, slice_ids, mode_perm):
    n_mode = lax.axis_size("mode")
    n_cuts = lax.axis_size("cuts")
    rows = stem_blocks.shape[1]
    width = stem_blocks.shape[3]
    mid = w1_table.shape[3]
    inner = w2_table.shape[2]
    out_width = w2_table.shape[3]
    block_count = slice_ids.shape[1]
    t_local = rows // n_mode
    a_count = inner // n_mode
    q_count = mid // a_count
    q_local = q_count // n_cuts
    me = lax.axis_index("cuts")
    sizes = (n_mode, t_local, n_cuts, a_count, q_local)

    pieces = stem_blocks[0].reshape(1, n_mode, t_local, 2 * width)
    payload = jnp.broadcast_to(pieces, (n_cuts, n_mode, t_local, 2 * width))
    payload = payload.reshape(n_cuts * n_mode, t_local, 2 * width)
    stem_rows = lax.all_to_all(payload, ("cuts", "mode"), 0, 0, tiled=True)
    stem_rows = stem_rows.reshape(block_count, n_mode * t_local, 2 * width)

    all_ids = gather_over_cuts(slice_ids[0], n_cuts)
    first_ids = all_ids[:, :, 0].T
    second_ids = all_ids[:, :, 1].T

    perm_grid = mode_perm.reshape(a_count, q_count)
    wanted = lax.dynamic_slice_in_dim(perm_grid, me * q_local, q_local, axis=1).reshape(-1)
    picker = (jnp.arange(mid, dtype=jnp.int32)[:, None] == wanted[None, :]).astype(w1_table.dtype)
    first_cols = jnp.einsum(
        "spkj,jn->spkn", w1_table, picker, preferred_element_type=jnp.float32
    ).astype(w1_table.dtype)
    real_part, imag_part = first_cols[:, 0], first_cols[:, 1]
    upper = jnp.concatenate([real_part, imag_part], axis=2)
    lower = jnp.concatenate([-imag_part, real_part], axis=2)
    first_all = jnp.concatenate([upper, lower], axis=1)

    if block_count * n_cuts <= 8:
        wanted_t = lax.dynamic_slice_in_dim(perm_grid, me * q_local, q_local, axis=1).T.reshape(-1)
        picker_t = (wanted_t[:, None] == jnp.arange(mid, dtype=jnp.int32)[None, :]).astype(w1_table.dtype)
        first_t = jnp.einsum(
            "nj,spkj->spnk", picker_t, w1_table, preferred_element_type=jnp.float32
        ).astype(w1_table.dtype)
        return stacked_part(stem_rows, first_t, w2_table, first_ids, second_ids, sizes)
    else:
        def one_block(index, running):
            stem_one = lax.dynamic_slice_in_dim(stem_rows, index, 1, axis=0)
            first_one = lax.dynamic_slice_in_dim(first_ids, index, 1, axis=0)
            second_one = lax.dynamic_slice_in_dim(second_ids, index, 1, axis=0)
            return running + blocks_part(
                stem_one, first_all, w2_table, first_one, second_one.reshape(-1), sizes
            )

        begin = jnp.zeros((t_local * q_local * 2, out_width), jnp.float32)
        amplitude = lax.fori_loop(0, block_count, one_block, begin)
    return amplitude.reshape(t_local, q_local, 2, out_width)


def solution(mesh):
    placed = (P("cuts", "mode", None, None), P(), P(), P("cuts", None, None), P())
    return jax.shard_map(
        on_device,
        mesh=mesh,
        in_specs=placed,
        out_specs=P("mode", "cuts", None, None),
        check_vma=False,
    )
```

```python
import jax
import jax.numpy as jnp
from jax import lax
from jax.experimental import pallas as pl
from jax.experimental.pallas import tpu as pltpu
from jax.sharding import PartitionSpec as P


def gather_over_cuts(own, n_cuts):
    pieces = [own]
    current = own
    ring = [(j, (j + 1) % n_cuts) for j in range(n_cuts)]
    for _ in range(1, n_cuts):
        current = lax.ppermute(current, "cuts", ring)
        pieces.append(current)
    stacked = jnp.stack(pieces)
    me = lax.axis_index("cuts")
    order = (me - jnp.arange(n_cuts, dtype=jnp.int32)) % n_cuts
    return jnp.take(stacked, order, axis=0)


def blocks_part(stem_rows, first_all, w2_table, first_ids, second_ids, sizes):
    n_mode, t_local, n_cuts, a_count, q_local = sizes
    chunk = stem_rows.shape[0]
    wide_in = stem_rows.shape[2]
    col_width = first_all.shape[2]
    slice_count, _, inner, out_width = w2_table.shape
    first_w = jnp.take(first_all, first_ids, axis=0)
    first_w = jnp.transpose(first_w, (0, 2, 1, 3)).reshape(
        chunk, wide_in, n_cuts * col_width
    )
    product = jnp.einsum(
        "bri,bio->bro", stem_rows, first_w, preferred_element_type=jnp.float32
    ).astype(jnp.bfloat16)
    split = product.reshape(chunk, n_mode, t_local, n_cuts, 2, a_count, q_local)
    real_p, imag_p = split[:, :, :, :, 0], split[:, :, :, :, 1]
    lhs = jnp.stack(
        [
            jnp.stack([real_p, -imag_p]),
            jnp.stack([imag_p, real_p]),
        ]
    )
    lhs = jnp.transpose(lhs, (4, 7, 0, 2, 5, 1, 3, 6)).reshape(
        t_local * q_local * 2, chunk * n_cuts * 2 * inner
    )
    second_w = jnp.take(
        w2_table.reshape(slice_count, 2 * inner, out_width), second_ids, axis=0
    ).reshape(chunk * n_cuts * 2 * inner, out_width)
    return jnp.dot(lhs, second_w, preferred_element_type=jnp.float32)


def regroup_kernel(stem_ref, weight_ref, second_ref, out_ref, real_ref, imag_ref):
    block_count, rows, _ = stem_ref.shape
    q_local = weight_ref.shape[1] // 64
    t_local = 16
    n_mode = rows // t_local
    lane = lax.broadcasted_iota(jnp.int32, (t_local, 128), 1)
    low = lane < 64
    imag_lane = (lane // 16) % 2 == 1

    def store(row, col, tile):
        real_ref[row:row + t_local, col:col + 128] = jnp.where(imag_lane, -tile, tile)
        imag_ref[row:row + t_local, col:col + 128] = jnp.where(
            imag_lane, pltpu.roll(tile, 16, 1), pltpu.roll(tile, 112, 1)
        )

    for b in range(block_count):
        product = lax.dot_general(
            stem_ref[b], weight_ref[b], (((1,), (1,)), ((), ())),
            preferred_element_type=jnp.float32,
        ).astype(jnp.bfloat16)
        for pair in range(n_mode // 2):
            upper = product[(2 * pair) * t_local:(2 * pair + 1) * t_local]
            lower = product[(2 * pair + 1) * t_local:(2 * pair + 2) * t_local]
            col = (b * n_mode // 2 + pair) * 128
            for qp in range(q_local // 2):
                first = upper[:, qp * 128:(qp + 1) * 128]
                second = lower[:, qp * 128:(qp + 1) * 128]
                store((2 * qp) * t_local, col, jnp.where(low, first, pltpu.roll(second, 64, 1)))
                store((2 * qp + 1) * t_local, col, jnp.where(low, pltpu.roll(first, 64, 1), second))
    weights = second_ref[...]
    for part, lhs_ref in enumerate((real_ref, imag_ref)):
        result = jnp.dot(lhs_ref[...], weights, preferred_element_type=jnp.float32)
        for q in range(q_local):
            out_ref[:, q, part, :] = result[q * t_local:(q + 1) * t_local]


def regroup(stem_rows, first_w, second_w, q_local, t_local):
    block_count, rows, _ = stem_rows.shape
    n_mode = rows // t_local
    lhs_shape = (q_local * t_local, block_count * n_mode * 64)
    out_shape = jax.ShapeDtypeStruct(
        (t_local, q_local, 2, second_w.shape[1]), jnp.float32
    )
    flops = 2 * block_count * rows * first_w.shape[1] * first_w.shape[2]
    flops += 2 * 2 * lhs_shape[0] * lhs_shape[1] * second_w.shape[1]
    return pl.pallas_call(
        regroup_kernel,
        out_shape=out_shape,
        in_specs=[pl.BlockSpec(memory_space=pltpu.VMEM)] * 3,
        out_specs=pl.BlockSpec(memory_space=pltpu.VMEM),
        scratch_shapes=[pltpu.VMEM(lhs_shape, jnp.bfloat16)] * 2,
        cost_estimate=pl.CostEstimate(
            flops=flops,
            transcendentals=0,
            bytes_accessed=2 * (stem_rows.size + first_w.size + second_w.size)
            + 4 * lhs_shape[0] * 2 * second_w.shape[1],
        ),
    )(stem_rows, first_w, second_w)

def stacked_part(stem_rows, first_t, w2_table, first_ids, second_ids, sizes):
    n_mode, t_local, n_cuts, a_count, q_local = sizes
    block_count = stem_rows.shape[0]
    width = first_t.shape[3]
    _, _, inner, out_width = w2_table.shape
    group = n_cuts * 2 * a_count
    picked = jnp.take(first_t, first_ids.reshape(-1), axis=0)
    picked = picked.reshape(block_count, n_cuts, 2, q_local, a_count, width)
    real_part, imag_part = picked[:, :, 0], picked[:, :, 1]
    first_w = jnp.stack(
        [jnp.stack([real_part, imag_part]), jnp.stack([-imag_part, real_part])]
    )
    first_w = jnp.transpose(first_w, (2, 4, 3, 1, 5, 0, 6)).reshape(
        block_count, q_local * group, 2 * width
    )
    if group == 64 and t_local == 16 and n_mode % 2 == 0 and q_local % 2 == 0:
        flat_ids = second_ids.reshape(-1)
        second = jnp.stack(
            [lax.dynamic_index_in_dim(w2_table, flat_ids[i], 0, keepdims=False)
             for i in range(flat_ids.shape[0])]
        )
        second = second.reshape(block_count, n_cuts, 2, n_mode, a_count, out_width)
        second_w = jnp.transpose(second, (0, 3, 1, 2, 4, 5)).reshape(
            block_count * n_mode * group, out_width
        )
        return regroup(stem_rows, first_w, second_w, q_local, t_local)
    else:
        second = jnp.take(w2_table, second_ids.reshape(-1), axis=0)
        second = jnp.swapaxes(second, 2, 3)
        second = second.reshape(block_count, n_cuts, 2, out_width, n_mode, a_count)
        real_two, imag_two = second[:, :, 0], second[:, :, 1]
        second_w = jnp.stack(
            [jnp.stack([real_two, -imag_two]), jnp.stack([imag_two, real_two])]
        )
        second_w = jnp.transpose(second_w, (0, 4, 2, 5, 3, 1, 6)).reshape(
            2 * out_width, block_count * n_mode * group
        )
        product = jnp.einsum(
            "brk,bnk->brn", stem_rows, first_w, preferred_element_type=jnp.float32
        ).astype(jnp.bfloat16)
        lhs = product.reshape(block_count, n_mode, t_local, q_local, group)
        lhs = jnp.transpose(lhs, (3, 2, 0, 1, 4)).reshape(
            q_local * t_local, block_count * n_mode * group
        )
        amplitude = jnp.einsum(
            "mk,nk->mn", lhs, second_w, preferred_element_type=jnp.float32
        )
    amplitude = amplitude.reshape(q_local, t_local, 2, out_width)
    return jnp.transpose(amplitude, (1, 0, 2, 3))


def on_device(stem_blocks, w1_table, w2_table, slice_ids, mode_perm):
    n_mode = lax.axis_size("mode")
    n_cuts = lax.axis_size("cuts")
    rows = stem_blocks.shape[1]
    width = stem_blocks.shape[3]
    mid = w1_table.shape[3]
    inner = w2_table.shape[2]
    out_width = w2_table.shape[3]
    block_count = slice_ids.shape[1]
    t_local = rows // n_mode
    a_count = inner // n_mode
    q_count = mid // a_count
    q_local = q_count // n_cuts
    me = lax.axis_index("cuts")
    sizes = (n_mode, t_local, n_cuts, a_count, q_local)

    pieces = stem_blocks[0].reshape(1, n_mode, t_local, 2 * width)
    payload = jnp.broadcast_to(pieces, (n_cuts, n_mode, t_local, 2 * width))
    payload = payload.reshape(n_cuts * n_mode, t_local, 2 * width)
    stem_rows = lax.all_to_all(payload, ("cuts", "mode"), 0, 0, tiled=True)
    stem_rows = stem_rows.reshape(block_count, n_mode * t_local, 2 * width)

    all_ids = gather_over_cuts(slice_ids[0], n_cuts)
    first_ids = all_ids[:, :, 0].T
    second_ids = all_ids[:, :, 1].T

    perm_grid = mode_perm.reshape(a_count, q_count)
    wanted = lax.dynamic_slice_in_dim(perm_grid, me * q_local, q_local, axis=1).reshape(-1)
    picker = (jnp.arange(mid, dtype=jnp.int32)[:, None] == wanted[None, :]).astype(w1_table.dtype)
    first_cols = jnp.einsum(
        "spkj,jn->spkn", w1_table, picker, preferred_element_type=jnp.float32
    ).astype(w1_table.dtype)
    real_part, imag_part = first_cols[:, 0], first_cols[:, 1]
    upper = jnp.concatenate([real_part, imag_part], axis=2)
    lower = jnp.concatenate([-imag_part, real_part], axis=2)
    first_all = jnp.concatenate([upper, lower], axis=1)

    if block_count * n_cuts <= 8:
        wanted_t = lax.dynamic_slice_in_dim(perm_grid, me * q_local, q_local, axis=1).T.reshape(-1)
        picker_t = (wanted_t[:, None] == jnp.arange(mid, dtype=jnp.int32)[None, :]).astype(w1_table.dtype)
        first_t = jnp.einsum(
            "nj,spkj->spnk", picker_t, w1_table, preferred_element_type=jnp.float32
        ).astype(w1_table.dtype)
        return stacked_part(stem_rows, first_t, w2_table, first_ids, second_ids, sizes)
    else:
        def one_block(index, running):
            stem_one = lax.dynamic_slice_in_dim(stem_rows, index, 1, axis=0)
            first_one = lax.dynamic_slice_in_dim(first_ids, index, 1, axis=0)
            second_one = lax.dynamic_slice_in_dim(second_ids, index, 1, axis=0)
            return running + blocks_part(
                stem_one, first_all, w2_table, first_one, second_one.reshape(-1), sizes
            )

        begin = jnp.zeros((t_local * q_local * 2, out_width), jnp.float32)
        amplitude = lax.fori_loop(0, block_count, one_block, begin)
    return amplitude.reshape(t_local, q_local, 2, out_width)


def solution(mesh):
    placed = (P("cuts", "mode", None, None), P(), P(), P("cuts", None, None), P())
    return jax.shard_map(
        on_device,
        mesh=mesh,
        in_specs=placed,
        out_specs=P("mode", "cuts", None, None),
        check_vma=False,
    )
```

```python
import jax
import jax.numpy as jnp
from jax import lax
from jax.experimental import pallas as pl
from jax.experimental.pallas import tpu as pltpu
from jax.sharding import PartitionSpec as P


def gather_over_cuts(own, n_cuts):
    pieces = [own]
    current = own
    ring = [(j, (j + 1) % n_cuts) for j in range(n_cuts)]
    for _ in range(1, n_cuts):
        current = lax.ppermute(current, "cuts", ring)
        pieces.append(current)
    stacked = jnp.stack(pieces)
    me = lax.axis_index("cuts")
    order = (me - jnp.arange(n_cuts, dtype=jnp.int32)) % n_cuts
    return jnp.take(stacked, order, axis=0)


def blocks_part(stem_rows, first_all, w2_table, first_ids, second_ids, sizes):
    n_mode, t_local, n_cuts, a_count, q_local = sizes
    chunk = stem_rows.shape[0]
    wide_in = stem_rows.shape[2]
    col_width = first_all.shape[2]
    slice_count, _, inner, out_width = w2_table.shape
    first_w = jnp.take(first_all, first_ids, axis=0)
    first_w = jnp.transpose(first_w, (0, 2, 1, 3)).reshape(
        chunk, wide_in, n_cuts * col_width
    )
    product = jnp.einsum(
        "bri,bio->bro", stem_rows, first_w, preferred_element_type=jnp.float32
    ).astype(jnp.bfloat16)
    split = product.reshape(chunk, n_mode, t_local, n_cuts, 2, a_count, q_local)
    real_p, imag_p = split[:, :, :, :, 0], split[:, :, :, :, 1]
    lhs = jnp.stack(
        [
            jnp.stack([real_p, -imag_p]),
            jnp.stack([imag_p, real_p]),
        ]
    )
    lhs = jnp.transpose(lhs, (4, 7, 0, 2, 5, 1, 3, 6)).reshape(
        t_local * q_local * 2, chunk * n_cuts * 2 * inner
    )
    second_w = jnp.take(
        w2_table.reshape(slice_count, 2 * inner, out_width), second_ids, axis=0
    ).reshape(chunk * n_cuts * 2 * inner, out_width)
    return jnp.dot(lhs, second_w, preferred_element_type=jnp.float32)


def regroup_kernel(stem_ref, weight_ref, second_ref, out_ref, real_ref, imag_ref):
    block_count, rows, _ = stem_ref.shape
    q_local = weight_ref.shape[1] // 64
    t_local = 16
    n_mode = rows // t_local
    lane = lax.broadcasted_iota(jnp.int32, (t_local, 128), 1)
    low = lane < 64
    imag_lane = (lane // 16) % 2 == 1

    def store(row, col, tile):
        real_ref[row:row + t_local, col:col + 128] = jnp.where(imag_lane, -tile, tile)
        imag_ref[row:row + t_local, col:col + 128] = jnp.where(
            imag_lane, pltpu.roll(tile, 16, 1), pltpu.roll(tile, 112, 1)
        )

    for b in range(block_count):
        product = lax.dot_general(
            stem_ref[b], weight_ref[b], (((1,), (1,)), ((), ())),
            preferred_element_type=jnp.float32,
        ).astype(jnp.bfloat16)
        for pair in range(n_mode // 2):
            upper = product[(2 * pair) * t_local:(2 * pair + 1) * t_local]
            lower = product[(2 * pair + 1) * t_local:(2 * pair + 2) * t_local]
            col = (b * n_mode // 2 + pair) * 128
            for qp in range(q_local // 2):
                first = upper[:, qp * 128:(qp + 1) * 128]
                second = lower[:, qp * 128:(qp + 1) * 128]
                store((2 * qp) * t_local, col, jnp.where(low, first, pltpu.roll(second, 64, 1)))
                store((2 * qp + 1) * t_local, col, jnp.where(low, pltpu.roll(first, 64, 1), second))
    weights = second_ref[...]
    for part, lhs_ref in enumerate((real_ref, imag_ref)):
        result = jnp.dot(lhs_ref[...], weights, preferred_element_type=jnp.float32)
        for q in range(q_local):
            out_ref[:, q, part, :] = result[q * t_local:(q + 1) * t_local]


def regroup(stem_rows, first_w, second_w, q_local, t_local):
    block_count, rows, _ = stem_rows.shape
    n_mode = rows // t_local
    lhs_shape = (q_local * t_local, block_count * n_mode * 64)
    out_shape = jax.ShapeDtypeStruct(
        (t_local, q_local, 2, second_w.shape[1]), jnp.float32
    )
    flops = 2 * block_count * rows * first_w.shape[1] * first_w.shape[2]
    flops += 2 * 2 * lhs_shape[0] * lhs_shape[1] * second_w.shape[1]
    return pl.pallas_call(
        regroup_kernel,
        out_shape=out_shape,
        in_specs=[pl.BlockSpec(memory_space=pltpu.VMEM)] * 3,
        out_specs=pl.BlockSpec(memory_space=pltpu.VMEM),
        scratch_shapes=[pltpu.VMEM(lhs_shape, jnp.bfloat16)] * 2,
        cost_estimate=pl.CostEstimate(
            flops=flops,
            transcendentals=0,
            bytes_accessed=2 * (stem_rows.size + first_w.size + second_w.size)
            + 4 * lhs_shape[0] * 2 * second_w.shape[1],
        ),
    )(stem_rows, first_w, second_w)

def stacked_part(stem_rows, first_t, w2_table, first_ids, second_ids, sizes):
    n_mode, t_local, n_cuts, a_count, q_local = sizes
    block_count = stem_rows.shape[0]
    width = first_t.shape[3]
    _, _, inner, out_width = w2_table.shape
    group = n_cuts * 2 * a_count
    picked = first_t if first_ids is None else jnp.take(first_t, first_ids.reshape(-1), axis=0)
    picked = picked.reshape(block_count, n_cuts, 2, q_local, a_count, width)
    real_part, imag_part = picked[:, :, 0], picked[:, :, 1]
    first_w = jnp.stack(
        [jnp.stack([real_part, imag_part]), jnp.stack([-imag_part, real_part])]
    )
    first_w = jnp.transpose(first_w, (2, 4, 3, 1, 5, 0, 6)).reshape(
        block_count, q_local * group, 2 * width
    )
    if group == 64 and t_local == 16 and n_mode % 2 == 0 and q_local % 2 == 0:
        second = jnp.take(w2_table, second_ids.reshape(-1), axis=0)
        second = second.reshape(block_count, n_cuts, 2, n_mode, a_count, out_width)
        second_w = jnp.transpose(second, (0, 3, 1, 2, 4, 5)).reshape(
            block_count * n_mode * group, out_width
        )
        return regroup(stem_rows, first_w, second_w, q_local, t_local)
    else:
        second = jnp.take(w2_table, second_ids.reshape(-1), axis=0)
        second = jnp.swapaxes(second, 2, 3)
        second = second.reshape(block_count, n_cuts, 2, out_width, n_mode, a_count)
        real_two, imag_two = second[:, :, 0], second[:, :, 1]
        second_w = jnp.stack(
            [jnp.stack([real_two, -imag_two]), jnp.stack([imag_two, real_two])]
        )
        second_w = jnp.transpose(second_w, (0, 4, 2, 5, 3, 1, 6)).reshape(
            2 * out_width, block_count * n_mode * group
        )
        product = jnp.einsum(
            "brk,bnk->brn", stem_rows, first_w, preferred_element_type=jnp.float32
        ).astype(jnp.bfloat16)
        lhs = product.reshape(block_count, n_mode, t_local, q_local, group)
        lhs = jnp.transpose(lhs, (3, 2, 0, 1, 4)).reshape(
            q_local * t_local, block_count * n_mode * group
        )
        amplitude = jnp.einsum(
            "mk,nk->mn", lhs, second_w, preferred_element_type=jnp.float32
        )
    amplitude = amplitude.reshape(q_local, t_local, 2, out_width)
    return jnp.transpose(amplitude, (1, 0, 2, 3))


def on_device(stem_blocks, w1_table, w2_table, slice_ids, mode_perm):
    n_mode = lax.axis_size("mode")
    n_cuts = lax.axis_size("cuts")
    rows = stem_blocks.shape[1]
    width = stem_blocks.shape[3]
    mid = w1_table.shape[3]
    inner = w2_table.shape[2]
    out_width = w2_table.shape[3]
    block_count = slice_ids.shape[1]
    t_local = rows // n_mode
    a_count = inner // n_mode
    q_count = mid // a_count
    q_local = q_count // n_cuts
    me = lax.axis_index("cuts")
    sizes = (n_mode, t_local, n_cuts, a_count, q_local)

    pieces = stem_blocks[0].reshape(1, n_mode, t_local, 2 * width)
    payload = jnp.broadcast_to(pieces, (n_cuts, n_mode, t_local, 2 * width))
    payload = payload.reshape(n_cuts * n_mode, t_local, 2 * width)
    stem_rows = lax.all_to_all(payload, ("cuts", "mode"), 0, 0, tiled=True)
    stem_rows = stem_rows.reshape(block_count, n_mode * t_local, 2 * width)

    all_ids = gather_over_cuts(slice_ids[0], n_cuts)
    first_ids = all_ids[:, :, 0].T
    second_ids = all_ids[:, :, 1].T

    perm_grid = mode_perm.reshape(a_count, q_count)
    wanted = lax.dynamic_slice_in_dim(perm_grid, me * q_local, q_local, axis=1).reshape(-1)
    picker = (jnp.arange(mid, dtype=jnp.int32)[:, None] == wanted[None, :]).astype(w1_table.dtype)
    first_cols = jnp.einsum(
        "spkj,jn->spkn", w1_table, picker, preferred_element_type=jnp.float32
    ).astype(w1_table.dtype)
    real_part, imag_part = first_cols[:, 0], first_cols[:, 1]
    upper = jnp.concatenate([real_part, imag_part], axis=2)
    lower = jnp.concatenate([-imag_part, real_part], axis=2)
    first_all = jnp.concatenate([upper, lower], axis=1)

    if block_count * n_cuts <= 8:
        wanted_t = lax.dynamic_slice_in_dim(perm_grid, me * q_local, q_local, axis=1).T.reshape(-1)
        picker_t = (wanted_t[:, None] == jnp.arange(mid, dtype=jnp.int32)[None, :]).astype(w1_table.dtype)
        used = jnp.take(w1_table, first_ids.reshape(-1), axis=0)
        first_t = jnp.einsum(
            "nj,spkj->spnk", picker_t, used, preferred_element_type=jnp.float32
        ).astype(w1_table.dtype)
        return stacked_part(stem_rows, first_t, w2_table, None, second_ids, sizes)
    else:
        def one_block(index, running):
            stem_one = lax.dynamic_slice_in_dim(stem_rows, index, 1, axis=0)
            first_one = lax.dynamic_slice_in_dim(first_ids, index, 1, axis=0)
            second_one = lax.dynamic_slice_in_dim(second_ids, index, 1, axis=0)
            return running + blocks_part(
                stem_one, first_all, w2_table, first_one, second_one.reshape(-1), sizes
            )

        begin = jnp.zeros((t_local * q_local * 2, out_width), jnp.float32)
        amplitude = lax.fori_loop(0, block_count, one_block, begin)
    return amplitude.reshape(t_local, q_local, 2, out_width)


def solution(mesh):
    placed = (P("cuts", "mode", None, None), P(), P(), P("cuts", None, None), P())
    return jax.shard_map(
        on_device,
        mesh=mesh,
        in_specs=placed,
        out_specs=P("mode", "cuts", None, None),
        check_vma=False,
    )
```
